256 devices in a mesh: gx: 128 (over z, y, x_hi, core), gy: 2 (over x_lo).
Axes of the slice: x: 4 (x_hi: 2, x_lo: 2; x = x_hi * 2 + x_lo), y: 4, z: 8, core: 2. Of those that a mesh axis runs over, the one named last changes fastest.
Arguments:
- displacement: float32 [2, 4096, 16384], P(None, 'gx', 'gy'), may hold values from -4 to 4
- velocity: float32 [2, 4096, 16384], P(None, 'gx', 'gy'), may hold values from -6 to 6
- damage: float32 [4096, 16384], P('gx', 'gy'), may hold values from 0 to 0.9
- history: float32 [4096, 16384], P('gx', 'gy'), may hold values from 0.02 to 1
- toughness: float32 [4096, 16384], P('gx', 'gy'), may hold values from 0.3 to 3
Outputs:
- displacement_new: float32 [2, 4096, 16384], P(None, 'gx', 'gy')
- velocity_new: float32 [2, 4096, 16384], P(None, 'gx', 'gy')
- history_new: float32 [4096, 16384], P('gx', 'gy')
- damage_new: float32 [4096, 16384], P('gx', 'gy')
The draws below stay inside these ranges and needn't reach their ends.
All inputs are finite; a program needn't handle non-finite values.
Results may differ from the reference program's by a relative error of at most 0.00002.
Values sent between devices are 32-bit elements; how exact they have to be, the bound alone decides.
No kernel may reach another device: no remote copies, remote signals or barrier semaphores. Data moves between devices by JAX's collectives and lax.ppermute only.
A program may use at most 128 MiB of HBM per device.

```python
import math
import jax
import jax.numpy as jnp

NX = 4096
NY = 16384


def shard_levels(stream_key, extent, split, least, largest):
    factor_of, own = 1.0, jax.random.fold_in(stream_key, 6)
    for position, blocks in split:
        steps = jnp.exp(jax.random.uniform(jax.random.fold_in(own, position), (blocks,), jnp.float32, least / len(split), largest / len(split)))
        factor_of = factor_of * jnp.repeat(steps, extent[position] // blocks).reshape([-1 if axis == position else 1 for axis in range(len(extent))])
    return factor_of


def noise(stream_key, shape, deviation, bound, split=(), held_as=jnp.bfloat16):
    drawn = deviation * jax.random.normal(stream_key, shape, jnp.float32)
    if split:
        drawn = drawn * shard_levels(stream_key, shape, split, -0.22, 0.18)
    return jnp.clip(drawn, -bound, bound).astype(held_as)


def setup_inputs(seed: int = 0) -> dict:
    arg_keys = jax.random.split(jax.random.key(seed), 6)
    return {
        "displacement": noise(arg_keys[0], (2, NX, NY), 0.3, 4.0, ((1, 128), (2, 2)), jnp.float32),
        "velocity": noise(arg_keys[1], (2, NX, NY), 0.5, 6.0, ((1, 128), (2, 2)), jnp.float32),
        "damage": jnp.clip(0.9 * jax.random.uniform(arg_keys[2], (NX, NY), jnp.float32) ** shard_levels(arg_keys[2], (NX, NY), ((0, 128), (1, 2)), -0.2, 0.2), 0.0, 0.9),
        "history": jnp.clip(jnp.exp(math.log(1.0) - 3.912023 * jax.random.uniform(arg_keys[3], (NX, NY), jnp.float32) ** shard_levels(arg_keys[3], (NX, NY), ((0, 128), (1, 2)), -0.2, 0.2)), 0.02, 1.0),
        "toughness": jnp.clip(jnp.exp(math.log(3.0) - 2.3025851 * jax.random.uniform(arg_keys[4], (NX, NY), jnp.float32) ** shard_levels(arg_keys[4], (NX, NY), ((0, 128), (1, 2)), -0.2, 0.2)), 0.3, 3.0),
    }


CHEB = 0.94
WEIGHT_TWO = 1.0 / (1.0 - CHEB * CHEB / 2.0)
WEIGHT_THREE = 1.0 / (1.0 - CHEB * CHEB * WEIGHT_TWO / 4.0)


def strain(first, second):
    exx = (first[2:, 1:-1] - first[:-2, 1:-1]) * 0.5
    eyy = (second[1:-1, 2:] - second[1:-1, :-2]) * 0.5
    exy = ((first[1:-1, 2:] - first[1:-1, :-2]) + (second[2:, 1:-1] - second[:-2, 1:-1])) * 0.25
    return exx, eyy, exy


def stress_of(eu, ev, dmg):
    exx = eu[0] + 0.5 * ev[0]
    eyy = eu[1] + 0.5 * ev[1]
    exy = eu[2] + 0.5 * ev[2]
    degrade = (1.0 - dmg) ** 2 + 0.001
    trace = exx + eyy
    return jnp.stack([degrade * (trace + 2.0 * exx), degrade * (trace + 2.0 * eyy), degrade * 2.0 * exy])


def accel(sxx, syy, sxy):
    first = ((sxx[2:, 1:-1] - sxx[:-2, 1:-1]) + (sxy[1:-1, 2:] - sxy[1:-1, :-2])) * 0.5
    second = ((sxy[2:, 1:-1] - sxy[:-2, 1:-1]) + (syy[1:-1, 2:] - syy[1:-1, :-2])) * 0.5
    return jnp.stack([first, second])


def energy(eu):
    trace = jnp.maximum(eu[0] + eu[1], 0.0)
    return 0.5 * trace * trace + eu[0] ** 2 + eu[1] ** 2 + 2.0 * eu[2] ** 2


def jacobi(field_pad, hist, tough_pad, valid):
    tough = tough_pad[1:-1, 1:-1]
    k_down = (tough + tough_pad[2:, 1:-1])
    k_up = (tough + tough_pad[:-2, 1:-1])
    k_right = (tough + tough_pad[1:-1, 2:])
    k_left = (tough + tough_pad[1:-1, :-2])
    numer = 2.0 * hist + k_down * field_pad[2:, 1:-1] + k_up * field_pad[:-2, 1:-1]
    numer = numer + k_right * field_pad[1:-1, 2:] + k_left * field_pad[1:-1, :-2]
    denom = tough * 0.5 + 2.0 * hist + k_down + k_up + k_right + k_left
    return jnp.where(valid, numer / jnp.where(valid, denom, 1.0), 0.0)


def reference(displacement, velocity, damage, history, toughness):
    def accel_of(disp, vel):
        dp = jnp.pad(disp, ((0, 0), (1, 1), (1, 1)))
        vp = jnp.pad(vel, ((0, 0), (1, 1), (1, 1)))
        eu = strain(dp[0], dp[1])
        ev = strain(vp[0], vp[1])
        sig = jnp.pad(stress_of(eu, ev, damage), ((0, 0), (1, 1), (1, 1)))
        return accel(sig[0], sig[1], sig[2]), eu

    first_acc, unused = accel_of(displacement, velocity)
    half = velocity + 0.1 * first_acc
    disp_new = displacement + 0.2 * half
    second_acc, eu = accel_of(disp_new, half)
    vel_new = half + 0.1 * second_acc
    hist_new = jnp.maximum(history, energy(eu))
    tough_pad = jnp.pad(toughness, 1)
    dmg_one = jacobi(jnp.pad(damage, 1), hist_new, tough_pad, True)
    dmg_two = damage + WEIGHT_TWO * (jacobi(jnp.pad(dmg_one, 1), hist_new, tough_pad, True) - damage)
    dmg_three = dmg_one + WEIGHT_THREE * (jacobi(jnp.pad(dmg_two, 1), hist_new, tough_pad, True) - dmg_one)
    return disp_new, vel_new, hist_new, dmg_three
```

```python
import jax
import jax.numpy as jnp
from jax import lax
from jax.experimental import pallas as pl
from jax.experimental.pallas import tpu as pltpu
from jax.sharding import PartitionSpec as P

CHEB = 0.94
WEIGHT_TWO = 1.0 / (1.0 - CHEB * CHEB / 2.0)
WEIGHT_THREE = 1.0 / (1.0 - CHEB * CHEB * WEIGHT_TWO / 4.0)

RAD = 5
HR = 8
HC = 128
BW = 1024
INTERPRET = False


def roll_shift(x, d, axis):
    return pltpu.roll(x, (-d) % x.shape[axis], axis)


def jnp_shift(x, d, axis):
    return jnp.roll(x, -d, axis)


def step_fields(u0, u1, v0, v1, dmg, hist, tough, valid, sh):
    zero = jnp.zeros_like(dmg)

    def strain(first, second):
        exx = (sh(first, 1, 0) - sh(first, -1, 0)) * 0.5
        eyy = (sh(second, 1, 1) - sh(second, -1, 1)) * 0.5
        exy = ((sh(first, 1, 1) - sh(first, -1, 1)) + (sh(second, 1, 0) - sh(second, -1, 0))) * 0.25
        return exx, eyy, exy

    degrade = (1.0 - dmg) ** 2 + 0.001

    def accel(w0, w1, z0, z1):
        eu = strain(w0, w1)
        ev = strain(z0, z1)
        exx = eu[0] + 0.5 * ev[0]
        eyy = eu[1] + 0.5 * ev[1]
        exy = eu[2] + 0.5 * ev[2]
        trace = exx + eyy
        sxx = jnp.where(valid, degrade * (trace + 2.0 * exx), zero)
        syy = jnp.where(valid, degrade * (trace + 2.0 * eyy), zero)
        sxy = jnp.where(valid, degrade * 2.0 * exy, zero)
        a0 = ((sh(sxx, 1, 0) - sh(sxx, -1, 0)) + (sh(sxy, 1, 1) - sh(sxy, -1, 1))) * 0.5
        a1 = ((sh(sxy, 1, 0) - sh(sxy, -1, 0)) + (sh(syy, 1, 1) - sh(syy, -1, 1))) * 0.5
        return a0, a1

    a0, a1 = accel(u0, u1, v0, v1)
    h0 = jnp.where(valid, v0 + 0.1 * a0, zero)
    h1 = jnp.where(valid, v1 + 0.1 * a1, zero)
    n0 = jnp.where(valid, u0 + 0.2 * h0, zero)
    n1 = jnp.where(valid, u1 + 0.2 * h1, zero)
    b0, b1 = accel(n0, n1, h0, h1)
    vel0 = h0 + 0.1 * b0
    vel1 = h1 + 0.1 * b1
    e = strain(n0, n1)
    tr = jnp.maximum(e[0] + e[1], 0.0)
    hist_new = jnp.maximum(hist, 0.5 * tr * tr + e[0] * e[0] + e[1] * e[1] + 2.0 * e[2] * e[2])

    k_down = tough + sh(tough, 1, 0)
    k_up = tough + sh(tough, -1, 0)
    k_right = tough + sh(tough, 1, 1)
    k_left = tough + sh(tough, -1, 1)
    two_h = 2.0 * hist_new
    denom = tough * 0.5 + two_h + k_down + k_up + k_right + k_left

    def jacobi(f):
        numer = two_h + k_down * sh(f, 1, 0) + k_up * sh(f, -1, 0)
        numer = numer + k_right * sh(f, 1, 1) + k_left * sh(f, -1, 1)
        return numer / denom

    d1 = jnp.where(valid, jacobi(dmg), zero)
    d2 = jnp.where(valid, dmg + WEIGHT_TWO * (jacobi(d1) - dmg), zero)
    d3 = d1 + WEIGHT_THREE * (jacobi(d2) - d1)
    return n0, n1, vel0, vel1, hist_new, d3


def exchange(fields):
    rows, cols = fields[0].shape
    nf = len(fields)
    iy = lax.axis_index("gy")
    ny = lax.axis_size("gy")
    nx = lax.axis_size("gx")
    left = jnp.stack([f[:, :RAD] for f in fields])
    right = jnp.stack([f[:, cols - RAD:] for f in fields])
    if ny == 2:
        got = lax.ppermute(jnp.where(iy == 0, right, left), "gy", [(0, 1), (1, 0)])
        from_left = jnp.where(iy == 1, got, 0.0)
        from_right = jnp.where(iy == 0, got, 0.0)
    else:
        from_left = lax.ppermute(right, "gy", [(i, i + 1) for i in range(ny - 1)])
        from_right = lax.ppermute(left, "gy", [(i + 1, i) for i in range(ny - 1)])
    left_block = jnp.pad(from_left, ((0, 0), (0, 0), (HC - RAD, 0)))
    right_block = jnp.pad(from_right, ((0, 0), (0, 0), (0, HC - RAD)))

    def ext_rows(lo, hi):
        mid = jnp.stack([f[lo:hi] for f in fields])
        return jnp.concatenate([left_block[:, lo:hi], mid, right_block[:, lo:hi]], axis=2)

    top = ext_rows(0, RAD)
    bottom = ext_rows(rows - RAD, rows)
    from_above = lax.ppermute(bottom, "gx", [(i, i + 1) for i in range(nx - 1)])
    from_below = lax.ppermute(top, "gx", [(i + 1, i) for i in range(nx - 1)])
    gap = jnp.zeros((HR - RAD, cols + 2 * HC), fields[0].dtype)
    out = []
    for k in range(nf):
        core = jnp.concatenate([left_block[k], fields[k], right_block[k]], axis=1)
        out.append(jnp.concatenate([gap, from_above[k], core, from_below[k], gap], axis=0))
    return out


def on_device(displacement, velocity, damage, history, toughness):
    rows, cols = damage.shape
    nx = lax.axis_size("gx")
    ny = lax.axis_size("gy")
    ix = lax.axis_index("gx")
    iy = lax.axis_index("gy")
    total_rows, total_cols = rows * nx, cols * ny
    fields = [displacement[0], displacement[1], velocity[0], velocity[1], damage, history, toughness]
    ext = exchange(fields)
    eu = jnp.stack(ext[0:2])
    ev = jnp.stack(ext[2:4])
    ed, eh, et = ext[4], ext[5], ext[6]
    ext_rows = rows + 2 * HR
    pos = jnp.stack([ix, iy]).astype(jnp.int32)
    nblocks = cols // BW
    extra = 2 * HC

    def kernel(pos_ref, um, ue, vm, ve, dm, de, hm, he, tm, te, uo, vo, ho, do):
        j = pl.program_id(0)

        def cat(a, b):
            return jnp.concatenate([a, b], axis=-1)

        u0 = cat(um[0], ue[0])
        u1 = cat(um[1], ue[1])
        v0 = cat(vm[0], ve[0])
        v1 = cat(vm[1], ve[1])
        d = cat(dm[...], de[...])
        h = cat(hm[...], he[...])
        t = cat(tm[...], te[...])
        shape = d.shape
        grow = lax.broadcasted_iota(jnp.int32, shape, 0) + (pos_ref[0] * rows - HR)
        gcol = lax.broadcasted_iota(jnp.int32, shape, 1) + (pos_ref[1] * cols + j * BW - HC)
        valid = (grow >= 0) & (grow < total_rows) & (gcol >= 0) & (gcol < total_cols)
        sh = jnp_shift if INTERPRET else roll_shift
        n0, n1, w0, w1, hn, d3 = step_fields(u0, u1, v0, v1, d, h, t, valid, sh)

        def core(x):
            return x[HR:HR + rows, HC:HC + BW]

        uo[0] = core(n0)
        uo[1] = core(n1)
        vo[0] = core(w0)
        vo[1] = core(w1)
        ho[...] = core(hn)
        do[...] = core(d3)

    main2 = pl.BlockSpec((2, ext_rows, BW), lambda j: (0, 0, j))
    extra2 = pl.BlockSpec((2, ext_rows, extra), lambda j: (0, 0, (j + 1) * (BW // extra)))
    main1 = pl.BlockSpec((ext_rows, BW), lambda j: (0, j))
    extra1 = pl.BlockSpec((ext_rows, extra), lambda j: (0, (j + 1) * (BW // extra)))
    out2 = pl.BlockSpec((2, rows, BW), lambda j: (0, 0, j))
    out1 = pl.BlockSpec((rows, BW), lambda j: (0, j))
    f32 = damage.dtype
    outs = pl.pallas_call(
        kernel,
        grid=(nblocks,),
        in_specs=[pl.BlockSpec(memory_space=pltpu.SMEM), main2, extra2, main2, extra2,
                  main1, extra1, main1, extra1, main1, extra1],
        out_specs=[out2, out2, out1, out1],
        out_shape=[jax.ShapeDtypeStruct((2, rows, cols), f32), jax.ShapeDtypeStruct((2, rows, cols), f32),
                   jax.ShapeDtypeStruct((rows, cols), f32), jax.ShapeDtypeStruct((rows, cols), f32)],
        interpret=INTERPRET,
    )(pos, eu, eu, ev, ev, ed, ed, eh, eh, et, et)
    return tuple(outs)


def solution(mesh):
    placed = (P(None, "gx", "gy"), P(None, "gx", "gy"), P("gx", "gy"), P("gx", "gy"), P("gx", "gy"))
    return jax.shard_map(
        on_device,
        mesh=mesh,
        in_specs=placed,
        out_specs=(P(None, "gx", "gy"), P(None, "gx", "gy"), P("gx", "gy"), P("gx", "gy")),
        check_vma=False,
    )
```

```python
import jax
import jax.numpy as jnp
from jax import lax
from jax.experimental import pallas as pl
from jax.experimental.pallas import tpu as pltpu
from jax.sharding import PartitionSpec as P

CHEB = 0.94
WEIGHT_TWO = 1.0 / (1.0 - CHEB * CHEB / 2.0)
WEIGHT_THREE = 1.0 / (1.0 - CHEB * CHEB * WEIGHT_TWO / 4.0)

RAD = 5
HR = 8
HC = 128
BW = 1024
INTERPRET = False


def roll_shift(x, d, axis):
    return pltpu.roll(x, (-d) % x.shape[axis], axis)


def jnp_shift(x, d, axis):
    return jnp.roll(x, -d, axis)


def step_fields(u0, u1, v0, v1, dmg, hist, tough, valid, sh):
    zero = jnp.zeros_like(dmg)

    def strain(first, second):
        exx = (sh(first, 1, 0) - sh(first, -1, 0)) * 0.5
        eyy = (sh(second, 1, 1) - sh(second, -1, 1)) * 0.5
        exy = ((sh(first, 1, 1) - sh(first, -1, 1)) + (sh(second, 1, 0) - sh(second, -1, 0))) * 0.25
        return exx, eyy, exy

    degrade = (1.0 - dmg) ** 2 + 0.001

    def accel(w0, w1, z0, z1):
        eu = strain(w0, w1)
        ev = strain(z0, z1)
        exx = eu[0] + 0.5 * ev[0]
        eyy = eu[1] + 0.5 * ev[1]
        exy = eu[2] + 0.5 * ev[2]
        trace = exx + eyy
        sxx = jnp.where(valid, degrade * (trace + 2.0 * exx), zero)
        syy = jnp.where(valid, degrade * (trace + 2.0 * eyy), zero)
        sxy = jnp.where(valid, degrade * 2.0 * exy, zero)
        a0 = ((sh(sxx, 1, 0) - sh(sxx, -1, 0)) + (sh(sxy, 1, 1) - sh(sxy, -1, 1))) * 0.5
        a1 = ((sh(sxy, 1, 0) - sh(sxy, -1, 0)) + (sh(syy, 1, 1) - sh(syy, -1, 1))) * 0.5
        return a0, a1

    a0, a1 = accel(u0, u1, v0, v1)
    h0 = jnp.where(valid, v0 + 0.1 * a0, zero)
    h1 = jnp.where(valid, v1 + 0.1 * a1, zero)
    n0 = jnp.where(valid, u0 + 0.2 * h0, zero)
    n1 = jnp.where(valid, u1 + 0.2 * h1, zero)
    b0, b1 = accel(n0, n1, h0, h1)
    vel0 = h0 + 0.1 * b0
    vel1 = h1 + 0.1 * b1
    e = strain(n0, n1)
    tr = jnp.maximum(e[0] + e[1], 0.0)
    hist_new = jnp.maximum(hist, 0.5 * tr * tr + e[0] * e[0] + e[1] * e[1] + 2.0 * e[2] * e[2])

    k_down = tough + sh(tough, 1, 0)
    k_up = tough + sh(tough, -1, 0)
    k_right = tough + sh(tough, 1, 1)
    k_left = tough + sh(tough, -1, 1)
    two_h = 2.0 * hist_new
    denom = tough * 0.5 + two_h + k_down + k_up + k_right + k_left

    def jacobi(f):
        numer = two_h + k_down * sh(f, 1, 0) + k_up * sh(f, -1, 0)
        numer = numer + k_right * sh(f, 1, 1) + k_left * sh(f, -1, 1)
        return numer / denom

    d1 = jnp.where(valid, jacobi(dmg), zero)
    d2 = jnp.where(valid, dmg + WEIGHT_TWO * (jacobi(d1) - dmg), zero)
    d3 = d1 + WEIGHT_THREE * (jacobi(d2) - d1)
    return n0, n1, vel0, vel1, hist_new, d3


def exchange(fields):
    rows, cols = fields[0].shape
    iy = lax.axis_index("gy")
    ny = lax.axis_size("gy")
    nx = lax.axis_size("gx")
    left = jnp.stack([f[:, :RAD] for f in fields])
    right = jnp.stack([f[:, cols - RAD:] for f in fields])
    if ny == 2:
        got = lax.ppermute(jnp.where(iy == 0, right, left), "gy", [(0, 1), (1, 0)])
        from_left = jnp.where(iy == 1, got, 0.0)
        from_right = jnp.where(iy == 0, got, 0.0)
    else:
        from_left = lax.ppermute(right, "gy", [(i, i + 1) for i in range(ny - 1)])
        from_right = lax.ppermute(left, "gy", [(i + 1, i) for i in range(ny - 1)])
    left_block = jnp.pad(from_left, ((0, 0), (0, 0), (HC - RAD, 0)))
    right_block = jnp.pad(from_right, ((0, 0), (0, 0), (0, HC - RAD)))

    def ext_rows(lo, hi):
        mid = jnp.stack([f[lo:hi] for f in fields])
        return jnp.concatenate([left_block[:, lo:hi], mid, right_block[:, lo:hi]], axis=2)

    top = ext_rows(0, RAD)
    bottom = ext_rows(rows - RAD, rows)
    from_above = lax.ppermute(bottom, "gx", [(i, i + 1) for i in range(nx - 1)])
    from_below = lax.ppermute(top, "gx", [(i + 1, i) for i in range(nx - 1)])
    above = jnp.pad(from_above, ((0, 0), (HR - RAD, 0), (0, 0)))
    below = jnp.pad(from_below, ((0, 0), (0, HR - RAD), (0, 0)))
    return left_block, right_block, above, below


def on_device(displacement, velocity, damage, history, toughness):
    rows, cols = damage.shape
    nx = lax.axis_size("gx")
    ny = lax.axis_size("gy")
    ix = lax.axis_index("gx")
    iy = lax.axis_index("gy")
    total_rows, total_cols = rows * nx, cols * ny
    fields = [displacement[0], displacement[1], velocity[0], velocity[1], damage, history, toughness]
    nf = len(fields)
    col_left, col_right, above, below = exchange(fields)
    pos = jnp.stack([ix, iy]).astype(jnp.int32)
    nblocks = cols // BW
    per = BW // HC
    last_col_block = cols // HC - 1
    extra = 2 * HC

    def kernel(pos_ref, um, ul, ur, vm, vl, vr, dm, dl, dr, hm, hl, hr, tm, tl, tr,
               cl, cr, am, ae, bm, be, uo, vo, ho, do):
        j = pl.program_id(0)
        first = j == 0
        last = j == nblocks - 1

        def window(k, main, lft, rgt):
            lft = jnp.where(first, cl[k], lft)
            rgt = jnp.where(last, cr[k], rgt)
            core = jnp.concatenate([lft, main, rgt], axis=-1)
            top = jnp.concatenate([am[k], ae[k]], axis=-1)
            bot = jnp.concatenate([bm[k], be[k]], axis=-1)
            return jnp.concatenate([top, core, bot], axis=0)

        u0 = window(0, um[0], ul[0], ur[0])
        u1 = window(1, um[1], ul[1], ur[1])
        v0 = window(2, vm[0], vl[0], vr[0])
        v1 = window(3, vm[1], vl[1], vr[1])
        d = window(4, dm[...], dl[...], dr[...])
        h = window(5, hm[...], hl[...], hr[...])
        t = window(6, tm[...], tl[...], tr[...])
        shape = d.shape
        grow = lax.broadcasted_iota(jnp.int32, shape, 0) + (pos_ref[0] * rows - HR)
        gcol = lax.broadcasted_iota(jnp.int32, shape, 1) + (pos_ref[1] * cols + j * BW - HC)
        valid = (grow >= 0) & (grow < total_rows) & (gcol >= 0) & (gcol < total_cols)
        sh = jnp_shift if INTERPRET else roll_shift
        n0, n1, w0, w1, hn, d3 = step_fields(u0, u1, v0, v1, d, h, t, valid, sh)

        def core(x):
            return x[HR:HR + rows, HC:HC + BW]

        uo[0] = core(n0)
        uo[1] = core(n1)
        vo[0] = core(w0)
        vo[1] = core(w1)
        ho[...] = core(hn)
        do[...] = core(d3)

    def lcol(j):
        return jnp.maximum(j * per - 1, 0)

    def rcol(j):
        return jnp.minimum((j + 1) * per, last_col_block)

    main2 = pl.BlockSpec((2, rows, BW), lambda j: (0, 0, j))
    left2 = pl.BlockSpec((2, rows, HC), lambda j: (0, 0, lcol(j)))
    right2 = pl.BlockSpec((2, rows, HC), lambda j: (0, 0, rcol(j)))
    main1 = pl.BlockSpec((rows, BW), lambda j: (0, j))
    left1 = pl.BlockSpec((rows, HC), lambda j: (0, lcol(j)))
    right1 = pl.BlockSpec((rows, HC), lambda j: (0, rcol(j)))
    colh = pl.BlockSpec((nf, rows, HC), lambda j: (0, 0, 0))
    rowm = pl.BlockSpec((nf, HR, BW), lambda j: (0, 0, j))
    rowe = pl.BlockSpec((nf, HR, extra), lambda j: (0, 0, (j + 1) * (BW // extra)))
    out2 = pl.BlockSpec((2, rows, BW), lambda j: (0, 0, j))
    out1 = pl.BlockSpec((rows, BW), lambda j: (0, j))
    f32 = damage.dtype
    outs = pl.pallas_call(
        kernel,
        grid=(nblocks,),
        in_specs=[pl.BlockSpec(memory_space=pltpu.SMEM), main2, left2, right2, main2, left2, right2,
                  main1, left1, right1, main1, left1, right1, main1, left1, right1,
                  colh, colh, rowm, rowe, rowm, rowe],
        out_specs=[out2, out2, out1, out1],
        out_shape=[jax.ShapeDtypeStruct((2, rows, cols), f32), jax.ShapeDtypeStruct((2, rows, cols), f32),
                   jax.ShapeDtypeStruct((rows, cols), f32), jax.ShapeDtypeStruct((rows, cols), f32)],
        interpret=INTERPRET,
    )(pos, displacement, displacement, displacement, velocity, velocity, velocity,
      damage, damage, damage, history, history, history, toughness, toughness, toughness,
      col_left, col_right, above, above, below, below)
    return tuple(outs)


def solution(mesh):
    placed = (P(None, "gx", "gy"), P(None, "gx", "gy"), P("gx", "gy"), P("gx", "gy"), P("gx", "gy"))
    return jax.shard_map(
        on_device,
        mesh=mesh,
        in_specs=placed,
        out_specs=(P(None, "gx", "gy"), P(None, "gx", "gy"), P("gx", "gy"), P("gx", "gy")),
        check_vma=False,
    )
```

```python
import jax
import jax.numpy as jnp
from jax import lax
from jax.experimental import pallas as pl
from jax.experimental.pallas import tpu as pltpu
from jax.sharding import PartitionSpec as P

CHEB = 0.94
WEIGHT_TWO = 1.0 / (1.0 - CHEB * CHEB / 2.0)
WEIGHT_THREE = 1.0 / (1.0 - CHEB * CHEB * WEIGHT_TWO / 4.0)

HR = 8
HC = 128
BW = 1024
INTERPRET = False


def roll_shift(x, d, axis):
    return pltpu.roll(x, (-d) % x.shape[axis], axis)


def jnp_shift(x, d, axis):
    return jnp.roll(x, -d, axis)


def step_fields(u0, u1, v0, v1, dmg, hist, tough, valid, sh):
    zero = jnp.zeros_like(dmg)

    def strain(first, second):
        exx = (sh(first, 1, 0) - sh(first, -1, 0)) * 0.5
        eyy = (sh(second, 1, 1) - sh(second, -1, 1)) * 0.5
        exy = ((sh(first, 1, 1) - sh(first, -1, 1)) + (sh(second, 1, 0) - sh(second, -1, 0))) * 0.25
        return exx, eyy, exy

    degrade = (1.0 - dmg) ** 2 + 0.001

    def accel(w0, w1, z0, z1):
        eu = strain(w0, w1)
        ev = strain(z0, z1)
        exx = eu[0] + 0.5 * ev[0]
        eyy = eu[1] + 0.5 * ev[1]
        exy = eu[2] + 0.5 * ev[2]
        trace = exx + eyy
        sxx = jnp.where(valid, degrade * (trace + 2.0 * exx), zero)
        syy = jnp.where(valid, degrade * (trace + 2.0 * eyy), zero)
        sxy = jnp.where(valid, degrade * 2.0 * exy, zero)
        a0 = ((sh(sxx, 1, 0) - sh(sxx, -1, 0)) + (sh(sxy, 1, 1) - sh(sxy, -1, 1))) * 0.5
        a1 = ((sh(sxy, 1, 0) - sh(sxy, -1, 0)) + (sh(syy, 1, 1) - sh(syy, -1, 1))) * 0.5
        return a0, a1

    a0, a1 = accel(u0, u1, v0, v1)
    h0 = jnp.where(valid, v0 + 0.1 * a0, zero)
    h1 = jnp.where(valid, v1 + 0.1 * a1, zero)
    n0 = jnp.where(valid, u0 + 0.2 * h0, zero)
    n1 = jnp.where(valid, u1 + 0.2 * h1, zero)
    b0, b1 = accel(n0, n1, h0, h1)
    vel0 = h0 + 0.1 * b0
    vel1 = h1 + 0.1 * b1
    e = strain(n0, n1)
    tr = jnp.maximum(e[0] + e[1], 0.0)
    hist_new = jnp.maximum(hist, 0.5 * tr * tr + e[0] * e[0] + e[1] * e[1] + 2.0 * e[2] * e[2])

    k_down = tough + sh(tough, 1, 0)
    k_up = tough + sh(tough, -1, 0)
    k_right = tough + sh(tough, 1, 1)
    k_left = tough + sh(tough, -1, 1)
    two_h = 2.0 * hist_new
    denom = tough * 0.5 + two_h + k_down + k_up + k_right + k_left

    def jacobi(f):
        numer = two_h + k_down * sh(f, 1, 0) + k_up * sh(f, -1, 0)
        numer = numer + k_right * sh(f, 1, 1) + k_left * sh(f, -1, 1)
        return numer / denom

    d1 = jnp.where(valid, jacobi(dmg), zero)
    d2 = jnp.where(valid, dmg + WEIGHT_TWO * (jacobi(d1) - dmg), zero)
    d3 = d1 + WEIGHT_THREE * (jacobi(d2) - d1)
    return n0, n1, vel0, vel1, hist_new, d3


RADII = (5, 5, 5, 5, 4, 2, 3)
OFFSETS = tuple(sum(RADII[:k]) for k in range(len(RADII)))
STRIP = 32
LANE_W = 5


def on_device(displacement, velocity, damage, history, toughness):
    rows, cols = damage.shape
    nx = lax.axis_size("gx")
    ny = lax.axis_size("gy")
    ix = lax.axis_index("gx")
    iy = lax.axis_index("gy")
    assert ny == 2 and rows % 8 == 0 and cols % BW == 0
    total_rows, total_cols = rows * nx, cols * ny
    nf = len(RADII)
    pos = jnp.stack([ix, iy]).astype(jnp.int32)
    nblocks = cols // BW
    per = BW // HC
    last_col_block = cols // HC - 1
    last_row_block = rows // 8 - 1
    f32 = damage.dtype
    rl = jnp_shift if INTERPRET else roll_shift

    def roll(x, s, axis):
        return rl(x, -s, axis)

    def split(refs):
        du, dv, dd, dh, dt = refs
        return [du[0], du[1], dv[0], dv[1], dd[...], dh[...], dt[...]]

    def pack_kernel(pos_ref, tu, tv, td, th, tt, bu, bv, bd, bh, bt,
                    lu, lv, ld, lh, lt, ru, rv, rd, rh, rt, top_o, bot_o, col_o):
        j = pl.program_id(0)
        tops = split((tu, tv, td, th, tt))
        bots = split((bu, bv, bd, bh, bt))
        ridx = lax.broadcasted_iota(jnp.int32, (STRIP, BW), 0)
        top = jnp.zeros((STRIP, BW), f32)
        bot = jnp.zeros((STRIP, BW), f32)
        pad = jnp.zeros((STRIP - 8, BW), f32)
        for k in range(nf):
            r, o = RADII[k], OFFSETS[k]
            inside = (ridx >= o) & (ridx < o + r)
            x = roll(jnp.concatenate([tops[k], pad], axis=0), o, 0)
            top = jnp.where(inside, x, top)
            y = roll(jnp.concatenate([bots[k], pad], axis=0), o - (8 - r), 0)
            bot = jnp.where(inside, y, bot)
        top_o[...] = top
        bot_o[...] = bot

        @pl.when(j == 0)
        def _():
            lefts = split((lu, lv, ld, lh, lt))
            rights = split((ru, rv, rd, rh, rt))
            lidx = lax.broadcasted_iota(jnp.int32, (rows, HC), 1)
            col = jnp.zeros((rows, HC), f32)
            to_right = pos_ref[1] == 0
            for k in range(nf):
                inside = (lidx >= LANE_W * k) & (lidx < LANE_W * (k + 1))
                a = roll(rights[k], LANE_W * k - (HC - LANE_W), 1)
                b = roll(lefts[k], LANE_W * k, 1)
                col = jnp.where(inside, jnp.where(to_right, a, b), col)
            col_o[...] = col

    t2 = pl.BlockSpec((2, 8, BW), lambda j: (0, 0, j))
    t1 = pl.BlockSpec((8, BW), lambda j: (0, j))
    b2 = pl.BlockSpec((2, 8, BW), lambda j: (0, last_row_block, j))
    b1 = pl.BlockSpec((8, BW), lambda j: (last_row_block, j))
    l2 = pl.BlockSpec((2, rows, HC), lambda j: (0, 0, 0))
    l1 = pl.BlockSpec((rows, HC), lambda j: (0, 0))
    r2 = pl.BlockSpec((2, rows, HC), lambda j: (0, 0, last_col_block))
    r1 = pl.BlockSpec((rows, HC), lambda j: (0, last_col_block))
    smem = pl.BlockSpec(memory_space=pltpu.SMEM)
    ins = (displacement, velocity, damage, history, toughness)
    top_s, bot_s, col_s = pl.pallas_call(
        pack_kernel,
        grid=(nblocks,),
        in_specs=[smem, t2, t2, t1, t1, t1, b2, b2, b1, b1, b1, l2, l2, l1, l1, l1, r2, r2, r1, r1, r1],
        out_specs=[pl.BlockSpec((STRIP, BW), lambda j: (0, j)), pl.BlockSpec((STRIP, BW), lambda j: (0, j)),
                   pl.BlockSpec((rows, HC), lambda j: (0, 0))],
        out_shape=[jax.ShapeDtypeStruct((STRIP, cols), f32), jax.ShapeDtypeStruct((STRIP, cols), f32),
                   jax.ShapeDtypeStruct((rows, HC), f32)],
        interpret=INTERPRET,
    )(pos, *ins, *ins, *ins, *ins)

    above = lax.ppermute(bot_s, "gx", [(i, i + 1) for i in range(nx - 1)])
    below = lax.ppermute(top_s, "gx", [(i + 1, i) for i in range(nx - 1)])
    side = lax.ppermute(col_s, "gy", [(0, 1), (1, 0)])
    both = ("gx", "gy")
    corner_above = lax.ppermute(col_s[rows - 8:], both,
                                [(i * 2 + g, (i + 1) * 2 + 1 - g) for i in range(nx - 1) for g in range(2)])
    corner_below = lax.ppermute(col_s[:8], both,
                                [((i + 1) * 2 + g, i * 2 + 1 - g) for i in range(nx - 1) for g in range(2)])

    def kernel(pos_ref, um, ul, ur, vm, vl, vr, dm, dl, dr, hm, hl, hr, tm, tl, tr,
               am, al, ar, bm, bl, br, side_ref, ca_ref, cb_ref, uo, vo, ho, do):
        j = pl.program_id(0)
        first = j == 0
        last = j == nblocks - 1
        has_left = pos_ref[1] == 1
        has_right = pos_ref[1] == 0
        mains = split((um, vm, dm, hm, tm))
        lefts = split((ul, vl, dl, hl, tl))
        rights = split((ur, vr, dr, hr, tr))
        side_v = side_ref[...]
        ca = ca_ref[...]
        cb = cb_ref[...]

        def lane_left(x, k):
            lidx = lax.broadcasted_iota(jnp.int32, x.shape, 1)
            y = roll(x, HC - LANE_W - LANE_W * k, 1)
            return jnp.where((lidx >= HC - LANE_W) & has_left, y, 0.0)

        def lane_right(x, k):
            lidx = lax.broadcasted_iota(jnp.int32, x.shape, 1)
            y = roll(x, -LANE_W * k, 1)
            return jnp.where((lidx < LANE_W) & has_right, y, 0.0)

        def above_tile(x, k):
            r, o = RADII[k], OFFSETS[k]
            y = roll(x, 8 - r - o, 0)[:8]
            ridx = lax.broadcasted_iota(jnp.int32, y.shape, 0)
            return jnp.where(ridx >= 8 - r, y, 0.0)

        def below_tile(x, k):
            r, o = RADII[k], OFFSETS[k]
            y = roll(x, -o, 0)[:8]
            ridx = lax.broadcasted_iota(jnp.int32, y.shape, 0)
            return jnp.where(ridx < r, y, 0.0)

        a_m, a_l, a_r = am[...], al[...], ar[...]
        b_m, b_l, b_r = bm[...], bl[...], br[...]

        def window(k):
            lft = jnp.where(first, lane_left(side_v, k), lefts[k])
            rgt = jnp.where(last, lane_right(side_v, k), rights[k])
            core = jnp.concatenate([lft, mains[k], rgt], axis=-1)
            top = jnp.concatenate([jnp.where(first, lane_left(ca, k), above_tile(a_l, k)),
                                   above_tile(a_m, k),
                                   jnp.where(last, lane_right(ca, k), above_tile(a_r, k))], axis=-1)
            bot = jnp.concatenate([jnp.where(first, lane_left(cb, k), below_tile(b_l, k)),
                                   below_tile(b_m, k),
                                   jnp.where(last, lane_right(cb, k), below_tile(b_r, k))], axis=-1)
            return jnp.concatenate([top, core, bot], axis=0)

        u0, u1, v0, v1, d, h, t = [window(k) for k in range(nf)]
        shape = d.shape
        grow = lax.broadcasted_iota(jnp.int32, shape, 0) + (pos_ref[0] * rows - HR)
        gcol = lax.broadcasted_iota(jnp.int32, shape, 1) + (pos_ref[1] * cols + j * BW - HC)
        valid = (grow >= 0) & (grow < total_rows) & (gcol >= 0) & (gcol < total_cols)
        n0, n1, w0, w1, hn, d3 = step_fields(u0, u1, v0, v1, d, h, t, valid, rl)

        def core(x):
            return x[HR:HR + rows, HC:HC + BW]

        uo[0] = core(n0)
        uo[1] = core(n1)
        vo[0] = core(w0)
        vo[1] = core(w1)
        ho[...] = core(hn)
        do[...] = core(d3)

    def lcol(j):
        return jnp.maximum(j * per - 1, 0)

    def rcol(j):
        return jnp.minimum((j + 1) * per, last_col_block)

    main2 = pl.BlockSpec((2, rows, BW), lambda j: (0, 0, j))
    left2 = pl.BlockSpec((2, rows, HC), lambda j: (0, 0, lcol(j)))
    right2 = pl.BlockSpec((2, rows, HC), lambda j: (0, 0, rcol(j)))
    main1 = pl.BlockSpec((rows, BW), lambda j: (0, j))
    left1 = pl.BlockSpec((rows, HC), lambda j: (0, lcol(j)))
    right1 = pl.BlockSpec((rows, HC), lambda j: (0, rcol(j)))
    sm = pl.BlockSpec((STRIP, BW), lambda j: (0, j))
    sl = pl.BlockSpec((STRIP, HC), lambda j: (0, lcol(j)))
    sr = pl.BlockSpec((STRIP, HC), lambda j: (0, rcol(j)))
    sidespec = pl.BlockSpec((rows, HC), lambda j: (0, 0))
    cornerspec = pl.BlockSpec((8, HC), lambda j: (0, 0))
    out2 = pl.BlockSpec((2, rows, BW), lambda j: (0, 0, j))
    out1 = pl.BlockSpec((rows, BW), lambda j: (0, j))
    outs = pl.pallas_call(
        kernel,
        grid=(nblocks,),
        in_specs=[smem, main2, left2, right2, main2, left2, right2,
                  main1, left1, right1, main1, left1, right1, main1, left1, right1,
                  sm, sl, sr, sm, sl, sr, sidespec, cornerspec, cornerspec],
        out_specs=[out2, out2, out1, out1],
        out_shape=[jax.ShapeDtypeStruct((2, rows, cols), f32), jax.ShapeDtypeStruct((2, rows, cols), f32),
                   jax.ShapeDtypeStruct((rows, cols), f32), jax.ShapeDtypeStruct((rows, cols), f32)],
        interpret=INTERPRET,
    )(pos, displacement, displacement, displacement, velocity, velocity, velocity,
      damage, damage, damage, history, history, history, toughness, toughness, toughness,
      above, above, above, below, below, below, side, corner_above, corner_below)
    return tuple(outs)


def solution(mesh):
    placed = (P(None, "gx", "gy"), P(None, "gx", "gy"), P("gx", "gy"), P("gx", "gy"), P("gx", "gy"))
    return jax.shard_map(
        on_device,
        mesh=mesh,
        in_specs=placed,
        out_specs=(P(None, "gx", "gy"), P(None, "gx", "gy"), P("gx", "gy"), P("gx", "gy")),
        check_vma=False,
    )
```

```python
import jax
import jax.numpy as jnp
from jax import lax
from jax.experimental import pallas as pl
from jax.experimental.pallas import tpu as pltpu
from jax.sharding import PartitionSpec as P

CHEB = 0.94
WEIGHT_TWO = 1.0 / (1.0 - CHEB * CHEB / 2.0)
WEIGHT_THREE = 1.0 / (1.0 - CHEB * CHEB * WEIGHT_TWO / 4.0)

HR = 8
HC = 128
BW = 2048
INTERPRET = False


def roll_shift(x, d, axis):
    return pltpu.roll(x, (-d) % x.shape[axis], axis)


def jnp_shift(x, d, axis):
    return jnp.roll(x, -d, axis)


def step_fields(u0, u1, v0, v1, dmg, hist, tough, valid, sh):
    zero = jnp.zeros_like(dmg)

    def strain(first, second):
        exx = (sh(first, 1, 0) - sh(first, -1, 0)) * 0.5
        eyy = (sh(second, 1, 1) - sh(second, -1, 1)) * 0.5
        exy = ((sh(first, 1, 1) - sh(first, -1, 1)) + (sh(second, 1, 0) - sh(second, -1, 0))) * 0.25
        return exx, eyy, exy

    degrade = (1.0 - dmg) ** 2 + 0.001

    def accel(exx, eyy, exy):
        trace = exx + eyy
        sxx = jnp.where(valid, degrade * (trace + 2.0 * exx), zero)
        syy = jnp.where(valid, degrade * (trace + 2.0 * eyy), zero)
        sxy = jnp.where(valid, degrade * 2.0 * exy, zero)
        a0 = ((sh(sxx, 1, 0) - sh(sxx, -1, 0)) + (sh(sxy, 1, 1) - sh(sxy, -1, 1))) * 0.5
        a1 = ((sh(sxy, 1, 0) - sh(sxy, -1, 0)) + (sh(syy, 1, 1) - sh(syy, -1, 1))) * 0.5
        return a0, a1

    a0, a1 = accel(*strain(u0 + 0.5 * v0, u1 + 0.5 * v1))
    h0 = jnp.where(valid, v0 + 0.1 * a0, zero)
    h1 = jnp.where(valid, v1 + 0.1 * a1, zero)
    n0 = jnp.where(valid, u0 + 0.2 * h0, zero)
    n1 = jnp.where(valid, u1 + 0.2 * h1, zero)
    e = strain(n0, n1)
    eh = strain(h0, h1)
    b0, b1 = accel(e[0] + 0.5 * eh[0], e[1] + 0.5 * eh[1], e[2] + 0.5 * eh[2])
    vel0 = h0 + 0.1 * b0
    vel1 = h1 + 0.1 * b1
    tr = jnp.maximum(e[0] + e[1], 0.0)
    hist_new = jnp.maximum(hist, 0.5 * tr * tr + e[0] * e[0] + e[1] * e[1] + 2.0 * e[2] * e[2])

    k_down = tough + sh(tough, 1, 0)
    k_up = tough + sh(tough, -1, 0)
    k_right = tough + sh(tough, 1, 1)
    k_left = tough + sh(tough, -1, 1)
    two_h = 2.0 * hist_new
    inv_denom = 1.0 / (tough * 0.5 + two_h + k_down + k_up + k_right + k_left)

    def jacobi(f):
        numer = two_h + k_down * sh(f, 1, 0) + k_up * sh(f, -1, 0)
        numer = numer + k_right * sh(f, 1, 1) + k_left * sh(f, -1, 1)
        return numer * inv_denom

    d1 = jnp.where(valid, jacobi(dmg), zero)
    d2 = jnp.where(valid, dmg + WEIGHT_TWO * (jacobi(d1) - dmg), zero)
    d3 = d1 + WEIGHT_THREE * (jacobi(d2) - d1)
    return n0, n1, vel0, vel1, hist_new, d3


RADII = (5, 5, 5, 5, 4, 2, 3)
OFFSETS = tuple(sum(RADII[:k]) for k in range(len(RADII)))
STRIP = 32
LANE_W = 5


def on_device(displacement, velocity, damage, history, toughness):
    rows, cols = damage.shape
    nx = lax.axis_size("gx")
    ny = lax.axis_size("gy")
    ix = lax.axis_index("gx")
    iy = lax.axis_index("gy")
    assert ny == 2 and rows % 8 == 0 and cols % BW == 0
    total_rows, total_cols = rows * nx, cols * ny
    nf = len(RADII)
    pos = jnp.stack([ix, iy]).astype(jnp.int32)
    nblocks = cols // BW
    per = BW // HC
    last_col_block = cols // HC - 1
    last_row_block = rows // 8 - 1
    f32 = damage.dtype
    rl = jnp_shift if INTERPRET else roll_shift

    def roll(x, s, axis):
        return rl(x, -s, axis)

    def split(refs):
        du, dv, dd, dh, dt = refs
        return [du[0], du[1], dv[0], dv[1], dd[...], dh[...], dt[...]]

    pw = cols

    def pack_kernel(pos_ref, tu, tv, td, th, tt, bu, bv, bd, bh, bt,
                    lu, lv, ld, lh, lt, ru, rv, rd, rh, rt, top_o, bot_o, col_o):
        j = pl.program_id(0)
        tops = split((tu, tv, td, th, tt))
        bots = split((bu, bv, bd, bh, bt))
        ridx = lax.broadcasted_iota(jnp.int32, (STRIP, pw), 0)
        top = jnp.zeros((STRIP, pw), f32)
        bot = jnp.zeros((STRIP, pw), f32)
        pad = jnp.zeros((STRIP - 8, pw), f32)
        for k in range(nf):
            r, o = RADII[k], OFFSETS[k]
            inside = (ridx >= o) & (ridx < o + r)
            x = roll(jnp.concatenate([tops[k], pad], axis=0), o, 0)
            top = jnp.where(inside, x, top)
            y = roll(jnp.concatenate([bots[k], pad], axis=0), o - (8 - r), 0)
            bot = jnp.where(inside, y, bot)
        top_o[...] = top
        bot_o[...] = bot

        @pl.when(j == 0)
        def _():
            lefts = split((lu, lv, ld, lh, lt))
            rights = split((ru, rv, rd, rh, rt))
            lidx = lax.broadcasted_iota(jnp.int32, (rows, HC), 1)
            col = jnp.zeros((rows, HC), f32)
            to_right = pos_ref[1] == 0
            for k in range(nf):
                inside = (lidx >= LANE_W * k) & (lidx < LANE_W * (k + 1))
                a = roll(rights[k], LANE_W * k - (HC - LANE_W), 1)
                b = roll(lefts[k], LANE_W * k, 1)
                col = jnp.where(inside, jnp.where(to_right, a, b), col)
            col_o[...] = col

    t2 = pl.BlockSpec((2, 8, pw), lambda j: (0, 0, j))
    t1 = pl.BlockSpec((8, pw), lambda j: (0, j))
    b2 = pl.BlockSpec((2, 8, pw), lambda j: (0, last_row_block, j))
    b1 = pl.BlockSpec((8, pw), lambda j: (last_row_block, j))
    l2 = pl.BlockSpec((2, rows, HC), lambda j: (0, 0, 0))
    l1 = pl.BlockSpec((rows, HC), lambda j: (0, 0))
    r2 = pl.BlockSpec((2, rows, HC), lambda j: (0, 0, last_col_block))
    r1 = pl.BlockSpec((rows, HC), lambda j: (0, last_col_block))
    smem = pl.BlockSpec(memory_space=pltpu.SMEM)
    ins = (displacement, velocity, damage, history, toughness)
    top_s, bot_s, col_s = pl.pallas_call(
        pack_kernel,
        grid=(cols // pw,),
        in_specs=[smem, t2, t2, t1, t1, t1, b2, b2, b1, b1, b1, l2, l2, l1, l1, l1, r2, r2, r1, r1, r1],
        out_specs=[pl.BlockSpec((STRIP, pw), lambda j: (0, j)), pl.BlockSpec((STRIP, pw), lambda j: (0, j)),
                   pl.BlockSpec((rows, HC), lambda j: (0, 0))],
        out_shape=[jax.ShapeDtypeStruct((STRIP, cols), f32), jax.ShapeDtypeStruct((STRIP, cols), f32),
                   jax.ShapeDtypeStruct((rows, HC), f32)],
        interpret=INTERPRET,
    )(pos, *ins, *ins, *ins, *ins)

    above = lax.ppermute(bot_s, "gx", [(i, i + 1) for i in range(nx - 1)])
    below = lax.ppermute(top_s, "gx", [(i + 1, i) for i in range(nx - 1)])
    side = lax.ppermute(col_s, "gy", [(0, 1), (1, 0)])
    both = ("gx", "gy")
    corner_above = lax.ppermute(col_s[rows - 8:], both,
                                [(i * 2 + g, (i + 1) * 2 + 1 - g) for i in range(nx - 1) for g in range(2)])
    corner_below = lax.ppermute(col_s[:8], both,
                                [((i + 1) * 2 + g, i * 2 + 1 - g) for i in range(nx - 1) for g in range(2)])

    def kernel(pos_ref, um, ul, ur, vm, vl, vr, dm, dl, dr, hm, hl, hr, tm, tl, tr,
               am, al, ar, bm, bl, br, side_ref, ca_ref, cb_ref, uo, vo, ho, do):
        j = pl.program_id(0)
        first = j == 0
        last = j == nblocks - 1
        has_left = pos_ref[1] == 1
        has_right = pos_ref[1] == 0
        mains = split((um, vm, dm, hm, tm))
        lefts = split((ul, vl, dl, hl, tl))
        rights = split((ur, vr, dr, hr, tr))
        side_v = side_ref[...]
        ca = ca_ref[...]
        cb = cb_ref[...]

        def lane_left(x, k):
            lidx = lax.broadcasted_iota(jnp.int32, x.shape, 1)
            y = roll(x, HC - LANE_W - LANE_W * k, 1)
            return jnp.where((lidx >= HC - LANE_W) & has_left, y, 0.0)

        def lane_right(x, k):
            lidx = lax.broadcasted_iota(jnp.int32, x.shape, 1)
            y = roll(x, -LANE_W * k, 1)
            return jnp.where((lidx < LANE_W) & has_right, y, 0.0)

        def above_tile(x, k):
            r, o = RADII[k], OFFSETS[k]
            y = roll(x, 8 - r - o, 0)[:8]
            ridx = lax.broadcasted_iota(jnp.int32, y.shape, 0)
            return jnp.where(ridx >= 8 - r, y, 0.0)

        def below_tile(x, k):
            r, o = RADII[k], OFFSETS[k]
            y = roll(x, -o, 0)[:8]
            ridx = lax.broadcasted_iota(jnp.int32, y.shape, 0)
            return jnp.where(ridx < r, y, 0.0)

        a_m, a_l, a_r = am[...], al[...], ar[...]
        b_m, b_l, b_r = bm[...], bl[...], br[...]

        def window(k):
            lft = jnp.where(first, lane_left(side_v, k), lefts[k])
            rgt = jnp.where(last, lane_right(side_v, k), rights[k])
            core = jnp.concatenate([lft, mains[k], rgt], axis=-1)
            top = jnp.concatenate([jnp.where(first, lane_left(ca, k), above_tile(a_l, k)),
                                   above_tile(a_m, k),
                                   jnp.where(last, lane_right(ca, k), above_tile(a_r, k))], axis=-1)
            bot = jnp.concatenate([jnp.where(first, lane_left(cb, k), below_tile(b_l, k)),
                                   below_tile(b_m, k),
                                   jnp.where(last, lane_right(cb, k), below_tile(b_r, k))], axis=-1)
            return jnp.concatenate([top, core, bot], axis=0)

        u0, u1, v0, v1, d, h, t = [window(k) for k in range(nf)]
        shape = d.shape
        grow = lax.broadcasted_iota(jnp.int32, shape, 0) + (pos_ref[0] * rows - HR)
        gcol = lax.broadcasted_iota(jnp.int32, shape, 1) + (pos_ref[1] * cols + j * BW - HC)
        valid = (grow >= 0) & (grow < total_rows) & (gcol >= 0) & (gcol < total_cols)
        n0, n1, w0, w1, hn, d3 = step_fields(u0, u1, v0, v1, d, h, t, valid, rl)

        def core(x):
            return x[HR:HR + rows, HC:HC + BW]

        uo[0] = core(n0)
        uo[1] = core(n1)
        vo[0] = core(w0)
        vo[1] = core(w1)
        ho[...] = core(hn)
        do[...] = core(d3)

    def lcol(j):
        return jnp.maximum(j * per - 1, 0)

    def rcol(j):
        return jnp.minimum((j + 1) * per, last_col_block)

    main2 = pl.BlockSpec((2, rows, BW), lambda j: (0, 0, j))
    left2 = pl.BlockSpec((2, rows, HC), lambda j: (0, 0, lcol(j)))
    right2 = pl.BlockSpec((2, rows, HC), lambda j: (0, 0, rcol(j)))
    main1 = pl.BlockSpec((rows, BW), lambda j: (0, j))
    left1 = pl.BlockSpec((rows, HC), lambda j: (0, lcol(j)))
    right1 = pl.BlockSpec((rows, HC), lambda j: (0, rcol(j)))
    sm = pl.BlockSpec((STRIP, BW), lambda j: (0, j))
    sl = pl.BlockSpec((STRIP, HC), lambda j: (0, lcol(j)))
    sr = pl.BlockSpec((STRIP, HC), lambda j: (0, rcol(j)))
    sidespec = pl.BlockSpec((rows, HC), lambda j: (0, 0))
    cornerspec = pl.BlockSpec((8, HC), lambda j: (0, 0))
    out2 = pl.BlockSpec((2, rows, BW), lambda j: (0, 0, j))
    out1 = pl.BlockSpec((rows, BW), lambda j: (0, j))
    outs = pl.pallas_call(
        kernel,
        grid=(nblocks,),
        in_specs=[smem, main2, left2, right2, main2, left2, right2,
                  main1, left1, right1, main1, left1, right1, main1, left1, right1,
                  sm, sl, sr, sm, sl, sr, sidespec, cornerspec, cornerspec],
        out_specs=[out2, out2, out1, out1],
        out_shape=[jax.ShapeDtypeStruct((2, rows, cols), f32), jax.ShapeDtypeStruct((2, rows, cols), f32),
                   jax.ShapeDtypeStruct((rows, cols), f32), jax.ShapeDtypeStruct((rows, cols), f32)],
        interpret=INTERPRET,
    )(pos, displacement, displacement, displacement, velocity, velocity, velocity,
      damage, damage, damage, history, history, history, toughness, toughness, toughness,
      above, above, above, below, below, below, side, corner_above, corner_below)
    return tuple(outs)


def solution(mesh):
    placed = (P(None, "gx", "gy"), P(None, "gx", "gy"), P("gx", "gy"), P("gx", "gy"), P("gx", "gy"))
    return jax.shard_map(
        on_device,
        mesh=mesh,
        in_specs=placed,
        out_specs=(P(None, "gx", "gy"), P(None, "gx", "gy"), P("gx", "gy"), P("gx", "gy")),
        check_vma=False,
    )
```

```python
import jax
import jax.numpy as jnp
from jax import lax
from jax.experimental import pallas as pl
from jax.experimental.pallas import tpu as pltpu
from jax.sharding import PartitionSpec as P

CHEB = 0.94
WEIGHT_TWO = 1.0 / (1.0 - CHEB * CHEB / 2.0)
WEIGHT_THREE = 1.0 / (1.0 - CHEB * CHEB * WEIGHT_TWO / 4.0)

HR = 8
HC = 128
BW = 4096
INTERPRET = False


def roll_shift(x, d, axis):
    return pltpu.roll(x, (-d) % x.shape[axis], axis)


def jnp_shift(x, d, axis):
    return jnp.roll(x, -d, axis)


def step_fields(u0, u1, v0, v1, dmg, hist, tough, valid, sh):
    zero = jnp.zeros_like(dmg)

    def strain(first, second):
        exx = (sh(first, 1, 0) - sh(first, -1, 0)) * 0.5
        eyy = (sh(second, 1, 1) - sh(second, -1, 1)) * 0.5
        exy = ((sh(first, 1, 1) - sh(first, -1, 1)) + (sh(second, 1, 0) - sh(second, -1, 0))) * 0.25
        return exx, eyy, exy

    degrade = (1.0 - dmg) ** 2 + 0.001

    def accel(exx, eyy, exy):
        trace = exx + eyy
        sxx = jnp.where(valid, degrade * (trace + 2.0 * exx), zero)
        syy = jnp.where(valid, degrade * (trace + 2.0 * eyy), zero)
        sxy = jnp.where(valid, degrade * 2.0 * exy, zero)
        a0 = ((sh(sxx, 1, 0) - sh(sxx, -1, 0)) + (sh(sxy, 1, 1) - sh(sxy, -1, 1))) * 0.5
        a1 = ((sh(sxy, 1, 0) - sh(sxy, -1, 0)) + (sh(syy, 1, 1) - sh(syy, -1, 1))) * 0.5
        return a0, a1

    a0, a1 = accel(*strain(u0 + 0.5 * v0, u1 + 0.5 * v1))
    h0 = jnp.where(valid, v0 + 0.1 * a0, zero)
    h1 = jnp.where(valid, v1 + 0.1 * a1, zero)
    n0 = jnp.where(valid, u0 + 0.2 * h0, zero)
    n1 = jnp.where(valid, u1 + 0.2 * h1, zero)
    e = strain(n0, n1)
    eh = strain(h0, h1)
    b0, b1 = accel(e[0] + 0.5 * eh[0], e[1] + 0.5 * eh[1], e[2] + 0.5 * eh[2])
    vel0 = h0 + 0.1 * b0
    vel1 = h1 + 0.1 * b1
    tr = jnp.maximum(e[0] + e[1], 0.0)
    hist_new = jnp.maximum(hist, 0.5 * tr * tr + e[0] * e[0] + e[1] * e[1] + 2.0 * e[2] * e[2])

    k_down = tough + sh(tough, 1, 0)
    k_up = tough + sh(tough, -1, 0)
    k_right = tough + sh(tough, 1, 1)
    k_left = tough + sh(tough, -1, 1)
    two_h = 2.0 * hist_new
    inv_denom = 1.0 / (tough * 0.5 + two_h + k_down + k_up + k_right + k_left)

    def jacobi(f):
        numer = two_h + k_down * sh(f, 1, 0) + k_up * sh(f, -1, 0)
        numer = numer + k_right * sh(f, 1, 1) + k_left * sh(f, -1, 1)
        return numer * inv_denom

    d1 = jnp.where(valid, jacobi(dmg), zero)
    d2 = jnp.where(valid, dmg + WEIGHT_TWO * (jacobi(d1) - dmg), zero)
    d3 = d1 + WEIGHT_THREE * (jacobi(d2) - d1)
    return n0, n1, vel0, vel1, hist_new, d3


RADII = (5, 5, 5, 5, 4, 2, 3)
OFFSETS = tuple(sum(RADII[:k]) for k in range(len(RADII)))
STRIP = 32
LANE_W = 5


def on_device(displacement, velocity, damage, history, toughness):
    rows, cols = damage.shape
    nx = lax.axis_size("gx")
    ny = lax.axis_size("gy")
    ix = lax.axis_index("gx")
    iy = lax.axis_index("gy")
    assert ny == 2 and rows % 8 == 0 and cols % BW == 0
    total_rows, total_cols = rows * nx, cols * ny
    nf = len(RADII)
    pos = jnp.stack([ix, iy]).astype(jnp.int32)
    nblocks = cols // BW
    per = BW // HC
    last_col_block = cols // HC - 1
    last_row_block = rows // 8 - 1
    f32 = damage.dtype
    rl = jnp_shift if INTERPRET else roll_shift

    def roll(x, s, axis):
        return rl(x, -s, axis)

    def split(refs):
        du, dv, dd, dh, dt = refs
        return [du[0], du[1], dv[0], dv[1], dd[...], dh[...], dt[...]]

    pw = cols

    def pack_kernel(pos_ref, tu, tv, td, th, tt, bu, bv, bd, bh, bt,
                    lu, lv, ld, lh, lt, ru, rv, rd, rh, rt, top_o, bot_o, col_o):
        j = pl.program_id(0)
        tops = split((tu, tv, td, th, tt))
        bots = split((bu, bv, bd, bh, bt))
        sidx = lax.broadcasted_iota(jnp.int32, (8, pw), 0)
        top_groups, bot_groups = [], []
        for g in range(STRIP // 8):
            top = jnp.zeros((8, pw), f32)
            bot = jnp.zeros((8, pw), f32)
            for k in range(nf):
                r, o = RADII[k], OFFSETS[k]
                lo, hi = o - 8 * g, o - 8 * g + r
                if hi <= 0 or lo >= 8:
                    continue
                inside = (sidx >= lo) & (sidx < hi)
                top = jnp.where(inside, roll(tops[k], lo, 0), top)
                bot = jnp.where(inside, roll(bots[k], lo - (8 - r), 0), bot)
            top_groups.append(top)
            bot_groups.append(bot)
        top = jnp.concatenate(top_groups, axis=0)
        bot = jnp.concatenate(bot_groups, axis=0)
        top_o[...] = top
        bot_o[...] = bot

        @pl.when(j == 0)
        def _():
            lefts = split((lu, lv, ld, lh, lt))
            rights = split((ru, rv, rd, rh, rt))
            lidx = lax.broadcasted_iota(jnp.int32, (rows, HC), 1)
            col = jnp.zeros((rows, HC), f32)
            to_right = pos_ref[1] == 0
            for k in range(nf):
                inside = (lidx >= LANE_W * k) & (lidx < LANE_W * (k + 1))
                a = roll(rights[k], LANE_W * k - (HC - LANE_W), 1)
                b = roll(lefts[k], LANE_W * k, 1)
                col = jnp.where(inside, jnp.where(to_right, a, b), col)
            col_o[...] = col

    t2 = pl.BlockSpec((2, 8, pw), lambda j: (0, 0, j))
    t1 = pl.BlockSpec((8, pw), lambda j: (0, j))
    b2 = pl.BlockSpec((2, 8, pw), lambda j: (0, last_row_block, j))
    b1 = pl.BlockSpec((8, pw), lambda j: (last_row_block, j))
    l2 = pl.BlockSpec((2, rows, HC), lambda j: (0, 0, 0))
    l1 = pl.BlockSpec((rows, HC), lambda j: (0, 0))
    r2 = pl.BlockSpec((2, rows, HC), lambda j: (0, 0, last_col_block))
    r1 = pl.BlockSpec((rows, HC), lambda j: (0, last_col_block))
    smem = pl.BlockSpec(memory_space=pltpu.SMEM)
    ins = (displacement, velocity, damage, history, toughness)
    top_s, bot_s, col_s = pl.pallas_call(
        pack_kernel,
        grid=(cols // pw,),
        in_specs=[smem, t2, t2, t1, t1, t1, b2, b2, b1, b1, b1, l2, l2, l1, l1, l1, r2, r2, r1, r1, r1],
        out_specs=[pl.BlockSpec((STRIP, pw), lambda j: (0, j)), pl.BlockSpec((STRIP, pw), lambda j: (0, j)),
                   pl.BlockSpec((rows, HC), lambda j: (0, 0))],
        out_shape=[jax.ShapeDtypeStruct((STRIP, cols), f32), jax.ShapeDtypeStruct((STRIP, cols), f32),
                   jax.ShapeDtypeStruct((rows, HC), f32)],
        interpret=INTERPRET,
    )(pos, *ins, *ins, *ins, *ins)

    above = lax.ppermute(bot_s, "gx", [(i, i + 1) for i in range(nx - 1)])
    below = lax.ppermute(top_s, "gx", [(i + 1, i) for i in range(nx - 1)])
    side = lax.ppermute(col_s, "gy", [(0, 1), (1, 0)])
    both = ("gx", "gy")
    corner_above = lax.ppermute(col_s[rows - 8:], both,
                                [(i * 2 + g, (i + 1) * 2 + 1 - g) for i in range(nx - 1) for g in range(2)])
    corner_below = lax.ppermute(col_s[:8], both,
                                [((i + 1) * 2 + g, i * 2 + 1 - g) for i in range(nx - 1) for g in range(2)])

    def kernel(pos_ref, um, ul, ur, vm, vl, vr, dm, dl, dr, hm, hl, hr, tm, tl, tr,
               am, al, ar, bm, bl, br, side_ref, ca_ref, cb_ref, uo, vo, ho, do):
        j = pl.program_id(0)
        first = j == 0
        last = j == nblocks - 1
        has_left = pos_ref[1] == 1
        has_right = pos_ref[1] == 0
        mains = split((um, vm, dm, hm, tm))
        lefts = split((ul, vl, dl, hl, tl))
        rights = split((ur, vr, dr, hr, tr))
        side_v = side_ref[...]
        ca = ca_ref[...]
        cb = cb_ref[...]

        def lane_left(x, k):
            lidx = lax.broadcasted_iota(jnp.int32, x.shape, 1)
            y = roll(x, HC - LANE_W - LANE_W * k, 1)
            return jnp.where((lidx >= HC - LANE_W) & has_left, y, 0.0)

        def lane_right(x, k):
            lidx = lax.broadcasted_iota(jnp.int32, x.shape, 1)
            y = roll(x, -LANE_W * k, 1)
            return jnp.where((lidx < LANE_W) & has_right, y, 0.0)

        def from_groups(x, k, first_row):
            r, o = RADII[k], OFFSETS[k]
            sidx = lax.broadcasted_iota(jnp.int32, (8,) + x.shape[1:], 0)
            out = jnp.zeros((8,) + x.shape[1:], x.dtype)
            for g in range(o // 8, (o + r - 1) // 8 + 1):
                shift = first_row - o + 8 * g
                src_row = sidx - shift
                inside = (sidx >= first_row) & (sidx < first_row + r) & (src_row >= 0) & (src_row < 8)
                out = jnp.where(inside, roll(x[8 * g:8 * g + 8], shift % 8, 0), out)
            return out

        def above_tile(x, k):
            return from_groups(x, k, 8 - RADII[k])

        def below_tile(x, k):
            return from_groups(x, k, 0)

        a_m, a_l, a_r = am[...], al[...], ar[...]
        b_m, b_l, b_r = bm[...], bl[...], br[...]

        def window(k):
            lft = jnp.where(first, lane_left(side_v, k), lefts[k])
            rgt = jnp.where(last, lane_right(side_v, k), rights[k])
            core = jnp.concatenate([lft, mains[k], rgt], axis=-1)
            top = jnp.concatenate([jnp.where(first, lane_left(ca, k), above_tile(a_l, k)),
                                   above_tile(a_m, k),
                                   jnp.where(last, lane_right(ca, k), above_tile(a_r, k))], axis=-1)
            bot = jnp.concatenate([jnp.where(first, lane_left(cb, k), below_tile(b_l, k)),
                                   below_tile(b_m, k),
                                   jnp.where(last, lane_right(cb, k), below_tile(b_r, k))], axis=-1)
            return jnp.concatenate([top, core, bot], axis=0)

        u0, u1, v0, v1, d, h, t = [window(k) for k in range(nf)]
        shape = d.shape
        grow = lax.broadcasted_iota(jnp.int32, shape, 0) + (pos_ref[0] * rows - HR)
        gcol = lax.broadcasted_iota(jnp.int32, shape, 1) + (pos_ref[1] * cols + j * BW - HC)
        valid = (grow >= 0) & (grow < total_rows) & (gcol >= 0) & (gcol < total_cols)
        n0, n1, w0, w1, hn, d3 = step_fields(u0, u1, v0, v1, d, h, t, valid, rl)

        def core(x):
            return x[HR:HR + rows, HC:HC + BW]

        uo[0] = core(n0)
        uo[1] = core(n1)
        vo[0] = core(w0)
        vo[1] = core(w1)
        ho[...] = core(hn)
        do[...] = core(d3)

    def lcol(j):
        return jnp.maximum(j * per - 1, 0)

    def rcol(j):
        return jnp.minimum((j + 1) * per, last_col_block)

    main2 = pl.BlockSpec((2, rows, BW), lambda j: (0, 0, j))
    left2 = pl.BlockSpec((2, rows, HC), lambda j: (0, 0, lcol(j)))
    right2 = pl.BlockSpec((2, rows, HC), lambda j: (0, 0, rcol(j)))
    main1 = pl.BlockSpec((rows, BW), lambda j: (0, j))
    left1 = pl.BlockSpec((rows, HC), lambda j: (0, lcol(j)))
    right1 = pl.BlockSpec((rows, HC), lambda j: (0, rcol(j)))
    sm = pl.BlockSpec((STRIP, BW), lambda j: (0, j))
    sl = pl.BlockSpec((STRIP, HC), lambda j: (0, lcol(j)))
    sr = pl.BlockSpec((STRIP, HC), lambda j: (0, rcol(j)))
    sidespec = pl.BlockSpec((rows, HC), lambda j: (0, 0))
    cornerspec = pl.BlockSpec((8, HC), lambda j: (0, 0))
    out2 = pl.BlockSpec((2, rows, BW), lambda j: (0, 0, j))
    out1 = pl.BlockSpec((rows, BW), lambda j: (0, j))
    outs = pl.pallas_call(
        kernel,
        grid=(nblocks,),
        in_specs=[smem, main2, left2, right2, main2, left2, right2,
                  main1, left1, right1, main1, left1, right1, main1, left1, right1,
                  sm, sl, sr, sm, sl, sr, sidespec, cornerspec, cornerspec],
        out_specs=[out2, out2, out1, out1],
        out_shape=[jax.ShapeDtypeStruct((2, rows, cols), f32), jax.ShapeDtypeStruct((2, rows, cols), f32),
                   jax.ShapeDtypeStruct((rows, cols), f32), jax.ShapeDtypeStruct((rows, cols), f32)],
        interpret=INTERPRET,
    )(pos, displacement, displacement, displacement, velocity, velocity, velocity,
      damage, damage, damage, history, history, history, toughness, toughness, toughness,
      above, above, above, below, below, below, side, corner_above, corner_below)
    return tuple(outs)


def solution(mesh):
    placed = (P(None, "gx", "gy"), P(None, "gx", "gy"), P("gx", "gy"), P("gx", "gy"), P("gx", "gy"))
    return jax.shard_map(
        on_device,
        mesh=mesh,
        in_specs=placed,
        out_specs=(P(None, "gx", "gy"), P(None, "gx", "gy"), P("gx", "gy"), P("gx", "gy")),
        check_vma=False,
    )
```

```python
import functools

import jax
import jax.numpy as jnp
from jax import lax
from jax.experimental import pallas as pl
from jax.experimental.pallas import tpu as pltpu
from jax.sharding import PartitionSpec as P

CHEB = 0.94
WEIGHT_TWO = 1.0 / (1.0 - CHEB * CHEB / 2.0)
WEIGHT_THREE = 1.0 / (1.0 - CHEB * CHEB * WEIGHT_TWO / 4.0)

HR = 8
HC = 128
BW = 2048
INTERPRET = False


def roll_shift(x, d, axis):
    return pltpu.roll(x, (-d) % x.shape[axis], axis)


def jnp_shift(x, d, axis):
    return jnp.roll(x, -d, axis)


def step_fields(u0, u1, v0, v1, dmg, hist, tough, valid, sh):
    zero = jnp.zeros_like(dmg)

    def strain(first, second):
        exx = (sh(first, 1, 0) - sh(first, -1, 0)) * 0.5
        eyy = (sh(second, 1, 1) - sh(second, -1, 1)) * 0.5
        exy = ((sh(first, 1, 1) - sh(first, -1, 1)) + (sh(second, 1, 0) - sh(second, -1, 0))) * 0.25
        return exx, eyy, exy

    degrade = (1.0 - dmg) ** 2 + 0.001

    def accel(exx, eyy, exy):
        trace = exx + eyy
        sxx = jnp.where(valid, degrade * (trace + 2.0 * exx), zero)
        syy = jnp.where(valid, degrade * (trace + 2.0 * eyy), zero)
        sxy = jnp.where(valid, degrade * 2.0 * exy, zero)
        a0 = ((sh(sxx, 1, 0) - sh(sxx, -1, 0)) + (sh(sxy, 1, 1) - sh(sxy, -1, 1))) * 0.5
        a1 = ((sh(sxy, 1, 0) - sh(sxy, -1, 0)) + (sh(syy, 1, 1) - sh(syy, -1, 1))) * 0.5
        return a0, a1

    a0, a1 = accel(*strain(u0 + 0.5 * v0, u1 + 0.5 * v1))
    h0 = jnp.where(valid, v0 + 0.1 * a0, zero)
    h1 = jnp.where(valid, v1 + 0.1 * a1, zero)
    n0 = jnp.where(valid, u0 + 0.2 * h0, zero)
    n1 = jnp.where(valid, u1 + 0.2 * h1, zero)
    e = strain(n0, n1)
    eh = strain(h0, h1)
    b0, b1 = accel(e[0] + 0.5 * eh[0], e[1] + 0.5 * eh[1], e[2] + 0.5 * eh[2])
    vel0 = h0 + 0.1 * b0
    vel1 = h1 + 0.1 * b1
    tr = jnp.maximum(e[0] + e[1], 0.0)
    hist_new = jnp.maximum(hist, 0.5 * tr * tr + e[0] * e[0] + e[1] * e[1] + 2.0 * e[2] * e[2])

    k_down = tough + sh(tough, 1, 0)
    k_up = tough + sh(tough, -1, 0)
    k_right = tough + sh(tough, 1, 1)
    k_left = tough + sh(tough, -1, 1)
    two_h = 2.0 * hist_new
    inv_denom = 1.0 / (tough * 0.5 + two_h + k_down + k_up + k_right + k_left)

    def jacobi(f):
        numer = two_h + k_down * sh(f, 1, 0) + k_up * sh(f, -1, 0)
        numer = numer + k_right * sh(f, 1, 1) + k_left * sh(f, -1, 1)
        return numer * inv_denom

    d1 = jnp.where(valid, jacobi(dmg), zero)
    d2 = jnp.where(valid, dmg + WEIGHT_TWO * (jacobi(d1) - dmg), zero)
    d3 = d1 + WEIGHT_THREE * (jacobi(d2) - d1)
    return n0, n1, vel0, vel1, hist_new, d3


RADII = (5, 5, 5, 5, 4, 2, 3)
OFFSETS = tuple(sum(RADII[:k]) for k in range(len(RADII)))
STRIP = 32
LANE_W = 5


def on_device(displacement, velocity, damage, history, toughness):
    rows, cols = damage.shape
    nx = lax.axis_size("gx")
    ny = lax.axis_size("gy")
    ix = lax.axis_index("gx")
    iy = lax.axis_index("gy")
    assert ny == 2 and rows % 8 == 0 and cols % (2 * BW) == 0
    total_rows, total_cols = rows * nx, cols * ny
    nf = len(RADII)
    pos = jnp.stack([ix, iy]).astype(jnp.int32)
    nblocks = cols // BW
    per = BW // HC
    last_col_block = cols // HC - 1
    last_row_block = rows // 8 - 1
    f32 = damage.dtype
    rl = jnp_shift if INTERPRET else roll_shift

    def roll(x, s, axis):
        return rl(x, -s, axis)

    def split(refs):
        du, dv, dd, dh, dt = refs
        return [du[0], du[1], dv[0], dv[1], dd[...], dh[...], dt[...]]

    pw = cols
    half = cols // 2
    off = half // HC

    def pack_kernel(pos_ref, tu, tv, td, th, tt, bu, bv, bd, bh, bt,
                    lu, lv, ld, lh, lt, ru, rv, rd, rh, rt, top0_o, top1_o, bot0_o, bot1_o, col_o):
        j = pl.program_id(0)
        tops = split((tu, tv, td, th, tt))
        bots = split((bu, bv, bd, bh, bt))
        ridx = lax.broadcasted_iota(jnp.int32, (STRIP, pw), 0)
        top = jnp.zeros((STRIP, pw), f32)
        bot = jnp.zeros((STRIP, pw), f32)
        pad = jnp.zeros((STRIP - 8, pw), f32)
        for k in range(nf):
            r, o = RADII[k], OFFSETS[k]
            inside = (ridx >= o) & (ridx < o + r)
            x = roll(jnp.concatenate([tops[k], pad], axis=0), o, 0)
            top = jnp.where(inside, x, top)
            y = roll(jnp.concatenate([bots[k], pad], axis=0), o - (8 - r), 0)
            bot = jnp.where(inside, y, bot)
        top0_o[...] = top[:, :half + HC]
        top1_o[...] = top[:, half:]
        bot0_o[...] = bot[:, :half + HC]
        bot1_o[...] = bot[:, half:]

        @pl.when(j == 0)
        def _():
            lefts = split((lu, lv, ld, lh, lt))
            rights = split((ru, rv, rd, rh, rt))
            lidx = lax.broadcasted_iota(jnp.int32, (rows, HC), 1)
            col = jnp.zeros((rows, HC), f32)
            to_right = pos_ref[1] == 0
            for k in range(nf):
                inside = (lidx >= LANE_W * k) & (lidx < LANE_W * (k + 1))
                a = roll(rights[k], LANE_W * k - (HC - LANE_W), 1)
                b = roll(lefts[k], LANE_W * k, 1)
                col = jnp.where(inside, jnp.where(to_right, a, b), col)
            col_o[...] = col

    t2 = pl.BlockSpec((2, 8, pw), lambda j: (0, 0, j))
    t1 = pl.BlockSpec((8, pw), lambda j: (0, j))
    b2 = pl.BlockSpec((2, 8, pw), lambda j: (0, last_row_block, j))
    b1 = pl.BlockSpec((8, pw), lambda j: (last_row_block, j))
    l2 = pl.BlockSpec((2, rows, HC), lambda j: (0, 0, 0))
    l1 = pl.BlockSpec((rows, HC), lambda j: (0, 0))
    r2 = pl.BlockSpec((2, rows, HC), lambda j: (0, 0, last_col_block))
    r1 = pl.BlockSpec((rows, HC), lambda j: (0, last_col_block))
    smem = pl.BlockSpec(memory_space=pltpu.SMEM)
    ins = (displacement, velocity, damage, history, toughness)
    top0, top1, bot0, bot1, col_s = pl.pallas_call(
        pack_kernel,
        grid=(cols // pw,),
        in_specs=[smem, t2, t2, t1, t1, t1, b2, b2, b1, b1, b1, l2, l2, l1, l1, l1, r2, r2, r1, r1, r1],
        out_specs=[pl.BlockSpec((STRIP, half + HC), lambda j: (0, 0)), pl.BlockSpec((STRIP, half), lambda j: (0, 0)),
                   pl.BlockSpec((STRIP, half + HC), lambda j: (0, 0)), pl.BlockSpec((STRIP, half), lambda j: (0, 0)),
                   pl.BlockSpec((rows, HC), lambda j: (0, 0))],
        out_shape=[jax.ShapeDtypeStruct((STRIP, half + HC), f32), jax.ShapeDtypeStruct((STRIP, half), f32),
                   jax.ShapeDtypeStruct((STRIP, half + HC), f32), jax.ShapeDtypeStruct((STRIP, half), f32),
                   jax.ShapeDtypeStruct((rows, HC), f32)],
        interpret=INTERPRET,
    )(pos, *ins, *ins, *ins, *ins)

    down = [(i, i + 1) for i in range(nx - 1)]
    up = [(i + 1, i) for i in range(nx - 1)]
    above0 = lax.ppermute(bot0, "gx", down)
    below0 = lax.ppermute(top0, "gx", up)
    side = lax.ppermute(col_s, "gy", [(0, 1), (1, 0)])
    both = ("gx", "gy")
    corner_above = lax.ppermute(col_s[rows - 8:], both,
                                [(i * 2 + g, (i + 1) * 2 + 1 - g) for i in range(nx - 1) for g in range(2)])
    corner_below = lax.ppermute(col_s[:8], both,
                                [((i + 1) * 2 + g, i * 2 + 1 - g) for i in range(nx - 1) for g in range(2)])
    above0, below0, side, corner_above, corner_below, bot1, top1 = lax.optimization_barrier(
        (above0, below0, side, corner_above, corner_below, bot1, top1))
    above1 = lax.ppermute(bot1, "gx", down)
    below1 = lax.ppermute(top1, "gx", up)

    def kernel(jbase, pos_ref, um, ul, ur, vm, vl, vr, dm, dl, dr, hm, hl, hr, tm, tl, tr,
               am, al, ar, ap, bm, bl, br, bp, side_ref, ca_ref, cb_ref, *rest):
        uo, vo, ho, do = rest[-4:]
        j = pl.program_id(0) + jbase
        first = j == 0
        last = j == nblocks - 1
        has_left = pos_ref[1] == 1
        has_right = pos_ref[1] == 0
        mains = split((um, vm, dm, hm, tm))
        lefts = split((ul, vl, dl, hl, tl))
        rights = split((ur, vr, dr, hr, tr))
        side_v = side_ref[...]
        ca = ca_ref[...]
        cb = cb_ref[...]

        def lane_left(x, k):
            lidx = lax.broadcasted_iota(jnp.int32, x.shape, 1)
            y = roll(x, HC - LANE_W - LANE_W * k, 1)
            return jnp.where((lidx >= HC - LANE_W) & has_left, y, 0.0)

        def lane_right(x, k):
            lidx = lax.broadcasted_iota(jnp.int32, x.shape, 1)
            y = roll(x, -LANE_W * k, 1)
            return jnp.where((lidx < LANE_W) & has_right, y, 0.0)

        def above_tile(x, k):
            r, o = RADII[k], OFFSETS[k]
            y = roll(x, 8 - r - o, 0)[:8]
            ridx = lax.broadcasted_iota(jnp.int32, y.shape, 0)
            return jnp.where(ridx >= 8 - r, y, 0.0)

        def below_tile(x, k):
            r, o = RADII[k], OFFSETS[k]
            y = roll(x, -o, 0)[:8]
            ridx = lax.broadcasted_iota(jnp.int32, y.shape, 0)
            return jnp.where(ridx < r, y, 0.0)

        a_m, a_l, a_r = am[...], al[...], ar[...]
        b_m, b_l, b_r = bm[...], bl[...], br[...]
        if jbase:
            a_l = jnp.where(j == jbase, ap[...], a_l)
            b_l = jnp.where(j == jbase, bp[...], b_l)

        def window(k):
            lft = jnp.where(first, lane_left(side_v, k), lefts[k])
            rgt = jnp.where(last, lane_right(side_v, k), rights[k])
            core = jnp.concatenate([lft, mains[k], rgt], axis=-1)
            top = jnp.concatenate([jnp.where(first, lane_left(ca, k), above_tile(a_l, k)),
                                   above_tile(a_m, k),
                                   jnp.where(last, lane_right(ca, k), above_tile(a_r, k))], axis=-1)
            bot = jnp.concatenate([jnp.where(first, lane_left(cb, k), below_tile(b_l, k)),
                                   below_tile(b_m, k),
                                   jnp.where(last, lane_right(cb, k), below_tile(b_r, k))], axis=-1)
            return jnp.concatenate([top, core, bot], axis=0)

        u0, u1, v0, v1, d, h, t = [window(k) for k in range(nf)]
        shape = d.shape
        grow = lax.broadcasted_iota(jnp.int32, shape, 0) + (pos_ref[0] * rows - HR)
        gcol = lax.broadcasted_iota(jnp.int32, shape, 1) + (pos_ref[1] * cols + j * BW - HC)
        valid = (grow >= 0) & (grow < total_rows) & (gcol >= 0) & (gcol < total_cols)
        n0, n1, w0, w1, hn, d3 = step_fields(u0, u1, v0, v1, d, h, t, valid, rl)

        def core(x):
            return x[HR:HR + rows, HC:HC + BW]

        uo[0] = core(n0)
        uo[1] = core(n1)
        vo[0] = core(w0)
        vo[1] = core(w1)
        ho[...] = core(hn)
        do[...] = core(d3)

    def lcol(j):
        return jnp.maximum(j * per - 1, 0)

    def rcol(j):
        return jnp.minimum((j + 1) * per, last_col_block)

    nhalf = nblocks // 2

    def run_half(h, above_h, below_h, prior):
        jb = h * nhalf
        shift = off if h else 0

        def at(f):
            return lambda i: f(i + jb)

        main2 = pl.BlockSpec((2, rows, BW), at(lambda j: (0, 0, j)))
        left2 = pl.BlockSpec((2, rows, HC), at(lambda j: (0, 0, lcol(j))))
        right2 = pl.BlockSpec((2, rows, HC), at(lambda j: (0, 0, rcol(j))))
        main1 = pl.BlockSpec((rows, BW), at(lambda j: (0, j)))
        left1 = pl.BlockSpec((rows, HC), at(lambda j: (0, lcol(j))))
        right1 = pl.BlockSpec((rows, HC), at(lambda j: (0, rcol(j))))
        sm = pl.BlockSpec((STRIP, BW), lambda i: (0, i))
        sl = pl.BlockSpec((STRIP, HC), at(lambda j: (0, jnp.maximum(lcol(j) - shift, 0))))
        sr = pl.BlockSpec((STRIP, HC), at(lambda j: (0, rcol(j) - shift)))
        sp = pl.BlockSpec((STRIP, HC), lambda i: (0, off - 1))
        sidespec = pl.BlockSpec((rows, HC), lambda i: (0, 0))
        cornerspec = pl.BlockSpec((8, HC), lambda i: (0, 0))
        out2 = pl.BlockSpec((2, rows, BW), at(lambda j: (0, 0, j)))
        out1 = pl.BlockSpec((rows, BW), at(lambda j: (0, j)))
        in_specs = [smem, main2, left2, right2, main2, left2, right2,
                    main1, left1, right1, main1, left1, right1, main1, left1, right1,
                    sm, sl, sr, sp, sm, sl, sr, sp, sidespec, cornerspec, cornerspec]
        args = [pos, displacement, displacement, displacement, velocity, velocity, velocity,
                damage, damage, damage, history, history, history, toughness, toughness, toughness,
                above_h, above_h, above_h, above0, below_h, below_h, below_h, below0,
                side, corner_above, corner_below]
        aliases = {}
        if prior is not None:
            aliases = {len(args) + k: k for k in range(4)}
            in_specs = in_specs + [pl.BlockSpec(memory_space=pl.ANY)] * 4
            args = args + list(prior)
        return pl.pallas_call(
            functools.partial(kernel, jb),
            grid=(nhalf,),
            in_specs=in_specs,
            out_specs=[out2, out2, out1, out1],
            out_shape=[jax.ShapeDtypeStruct((2, rows, cols), f32), jax.ShapeDtypeStruct((2, rows, cols), f32),
                       jax.ShapeDtypeStruct((rows, cols), f32), jax.ShapeDtypeStruct((rows, cols), f32)],
            input_output_aliases=aliases,
            interpret=INTERPRET,
        )(*args)

    outs = run_half(0, above0, below0, None)
    outs = run_half(1, above1, below1, outs)
    return tuple(outs)


def solution(mesh):
    placed = (P(None, "gx", "gy"), P(None, "gx", "gy"), P("gx", "gy"), P("gx", "gy"), P("gx", "gy"))
    return jax.shard_map(
        on_device,
        mesh=mesh,
        in_specs=placed,
        out_specs=(P(None, "gx", "gy"), P(None, "gx", "gy"), P("gx", "gy"), P("gx", "gy")),
        check_vma=False,
    )
```

```python
import jax
import jax.numpy as jnp
from jax import lax
from jax.experimental import pallas as pl
from jax.experimental.pallas import tpu as pltpu
from jax.sharding import PartitionSpec as P

CHEB = 0.94
WEIGHT_TWO = 1.0 / (1.0 - CHEB * CHEB / 2.0)
WEIGHT_THREE = 1.0 / (1.0 - CHEB * CHEB * WEIGHT_TWO / 4.0)

HR = 8
HC = 128
BW = 2048
INTERPRET = False


def roll_shift(x, d, axis):
    return pltpu.roll(x, (-d) % x.shape[axis], axis)


def jnp_shift(x, d, axis):
    return jnp.roll(x, -d, axis)


def step_fields(u0, u1, v0, v1, dmg, hist, tough, valid, sh):
    zero = jnp.zeros_like(dmg)

    def strain(first, second):
        exx = (sh(first, 1, 0) - sh(first, -1, 0)) * 0.5
        eyy = (sh(second, 1, 1) - sh(second, -1, 1)) * 0.5
        exy = ((sh(first, 1, 1) - sh(first, -1, 1)) + (sh(second, 1, 0) - sh(second, -1, 0))) * 0.25
        return exx, eyy, exy

    degrade = (1.0 - dmg) ** 2 + 0.001

    def accel(exx, eyy, exy):
        trace = exx + eyy
        sxx = jnp.where(valid, degrade * (trace + 2.0 * exx), zero)
        syy = jnp.where(valid, degrade * (trace + 2.0 * eyy), zero)
        sxy = jnp.where(valid, degrade * 2.0 * exy, zero)
        a0 = ((sh(sxx, 1, 0) - sh(sxx, -1, 0)) + (sh(sxy, 1, 1) - sh(sxy, -1, 1))) * 0.5
        a1 = ((sh(sxy, 1, 0) - sh(sxy, -1, 0)) + (sh(syy, 1, 1) - sh(syy, -1, 1))) * 0.5
        return a0, a1

    a0, a1 = accel(*strain(u0 + 0.5 * v0, u1 + 0.5 * v1))
    h0 = jnp.where(valid, v0 + 0.1 * a0, zero)
    h1 = jnp.where(valid, v1 + 0.1 * a1, zero)
    n0 = jnp.where(valid, u0 + 0.2 * h0, zero)
    n1 = jnp.where(valid, u1 + 0.2 * h1, zero)
    e = strain(n0, n1)
    eh = strain(h0, h1)
    b0, b1 = accel(e[0] + 0.5 * eh[0], e[1] + 0.5 * eh[1], e[2] + 0.5 * eh[2])
    vel0 = h0 + 0.1 * b0
    vel1 = h1 + 0.1 * b1
    tr = jnp.maximum(e[0] + e[1], 0.0)
    hist_new = jnp.maximum(hist, 0.5 * tr * tr + e[0] * e[0] + e[1] * e[1] + 2.0 * e[2] * e[2])

    k_down = tough + sh(tough, 1, 0)
    k_up = tough + sh(tough, -1, 0)
    k_right = tough + sh(tough, 1, 1)
    k_left = tough + sh(tough, -1, 1)
    two_h = 2.0 * hist_new
    inv_denom = 1.0 / (tough * 0.5 + two_h + k_down + k_up + k_right + k_left)

    def jacobi(f):
        numer = two_h + k_down * sh(f, 1, 0) + k_up * sh(f, -1, 0)
        numer = numer + k_right * sh(f, 1, 1) + k_left * sh(f, -1, 1)
        return numer * inv_denom

    d1 = jnp.where(valid, jacobi(dmg), zero)
    d2 = jnp.where(valid, dmg + WEIGHT_TWO * (jacobi(d1) - dmg), zero)
    d3 = d1 + WEIGHT_THREE * (jacobi(d2) - d1)
    return n0, n1, vel0, vel1, hist_new, d3


RADII = (5, 5, 5, 5, 4, 2, 3)
OFFSETS = tuple(sum(RADII[:k]) for k in range(len(RADII)))
STRIP = 32
LANE_W = 5


def on_device(displacement, velocity, damage, history, toughness):
    rows, cols = damage.shape
    nx = lax.axis_size("gx")
    ny = lax.axis_size("gy")
    ix = lax.axis_index("gx")
    iy = lax.axis_index("gy")
    assert ny == 2 and rows % 8 == 0 and cols % BW == 0
    total_rows, total_cols = rows * nx, cols * ny
    nf = len(RADII)
    pos = jnp.stack([ix, iy]).astype(jnp.int32)
    nblocks = cols // BW
    per = BW // HC
    last_col_block = cols // HC - 1
    last_row_block = rows // 8 - 1
    f32 = damage.dtype
    rl = jnp_shift if INTERPRET else roll_shift

    def roll(x, s, axis):
        return rl(x, -s, axis)

    def split(refs):
        du, dv, dd, dh, dt = refs
        return [du[0], du[1], dv[0], dv[1], dd[...], dh[...], dt[...]]

    pw = cols // 4

    def pack_kernel(pos_ref, tu, tv, td, th, tt, bu, bv, bd, bh, bt,
                    lu, lv, ld, lh, lt, ru, rv, rd, rh, rt, top_o, bot_o, col_o):
        j = pl.program_id(0)
        tops = split((tu, tv, td, th, tt))
        bots = split((bu, bv, bd, bh, bt))
        ridx = lax.broadcasted_iota(jnp.int32, (STRIP, pw), 0)
        top = jnp.zeros((STRIP, pw), f32)
        bot = jnp.zeros((STRIP, pw), f32)
        pad = jnp.zeros((STRIP - 8, pw), f32)
        for k in range(nf):
            r, o = RADII[k], OFFSETS[k]
            inside = (ridx >= o) & (ridx < o + r)
            x = roll(jnp.concatenate([tops[k], pad], axis=0), o, 0)
            top = jnp.where(inside, x, top)
            y = roll(jnp.concatenate([bots[k], pad], axis=0), o - (8 - r), 0)
            bot = jnp.where(inside, y, bot)
        top_o[...] = top
        bot_o[...] = bot

        @pl.when(j == 0)
        def _():
            lefts = split((lu, lv, ld, lh, lt))
            rights = split((ru, rv, rd, rh, rt))
            lidx = lax.broadcasted_iota(jnp.int32, (rows, HC), 1)
            col = jnp.zeros((rows, HC), f32)
            to_right = pos_ref[1] == 0
            for k in range(nf):
                inside = (lidx >= LANE_W * k) & (lidx < LANE_W * (k + 1))
                a = roll(rights[k], LANE_W * k - (HC - LANE_W), 1)
                b = roll(lefts[k], LANE_W * k, 1)
                col = jnp.where(inside, jnp.where(to_right, a, b), col)
            col_o[...] = col

    t2 = pl.BlockSpec((2, 8, pw), lambda j: (0, 0, j))
    t1 = pl.BlockSpec((8, pw), lambda j: (0, j))
    b2 = pl.BlockSpec((2, 8, pw), lambda j: (0, last_row_block, j))
    b1 = pl.BlockSpec((8, pw), lambda j: (last_row_block, j))
    l2 = pl.BlockSpec((2, rows, HC), lambda j: (0, 0, 0))
    l1 = pl.BlockSpec((rows, HC), lambda j: (0, 0))
    r2 = pl.BlockSpec((2, rows, HC), lambda j: (0, 0, last_col_block))
    r1 = pl.BlockSpec((rows, HC), lambda j: (0, last_col_block))
    smem = pl.BlockSpec(memory_space=pltpu.SMEM)
    ins = (displacement, velocity, damage, history, toughness)
    top_s, bot_s, col_s = pl.pallas_call(
        pack_kernel,
        grid=(cols // pw,),
        in_specs=[smem, t2, t2, t1, t1, t1, b2, b2, b1, b1, b1, l2, l2, l1, l1, l1, r2, r2, r1, r1, r1],
        out_specs=[pl.BlockSpec((STRIP, pw), lambda j: (0, j)), pl.BlockSpec((STRIP, pw), lambda j: (0, j)),
                   pl.BlockSpec((rows, HC), lambda j: (0, 0))],
        out_shape=[jax.ShapeDtypeStruct((STRIP, cols), f32), jax.ShapeDtypeStruct((STRIP, cols), f32),
                   jax.ShapeDtypeStruct((rows, HC), f32)],
        interpret=INTERPRET,
    )(pos, *ins, *ins, *ins, *ins)

    above = lax.ppermute(bot_s, "gx", [(i, i + 1) for i in range(nx - 1)])
    below = lax.ppermute(top_s, "gx", [(i + 1, i) for i in range(nx - 1)])
    side = lax.ppermute(col_s, "gy", [(0, 1), (1, 0)])
    both = ("gx", "gy")
    corner_above = lax.ppermute(col_s[rows - 8:], both,
                                [(i * 2 + g, (i + 1) * 2 + 1 - g) for i in range(nx - 1) for g in range(2)])
    corner_below = lax.ppermute(col_s[:8], both,
                                [((i + 1) * 2 + g, i * 2 + 1 - g) for i in range(nx - 1) for g in range(2)])

    def kernel(pos_ref, um, ul, ur, vm, vl, vr, dm, dl, dr, hm, hl, hr, tm, tl, tr,
               am, al, ar, bm, bl, br, side_ref, ca_ref, cb_ref, uo, vo, ho, do):
        j = pl.program_id(0)
        first = j == 0
        last = j == nblocks - 1
        has_left = pos_ref[1] == 1
        has_right = pos_ref[1] == 0
        mains = split((um, vm, dm, hm, tm))
        lefts = split((ul, vl, dl, hl, tl))
        rights = split((ur, vr, dr, hr, tr))
        side_v = side_ref[...]
        ca = ca_ref[...]
        cb = cb_ref[...]

        def lane_left(x, k):
            lidx = lax.broadcasted_iota(jnp.int32, x.shape, 1)
            y = roll(x, HC - LANE_W - LANE_W * k, 1)
            return jnp.where((lidx >= HC - LANE_W) & has_left, y, 0.0)

        def lane_right(x, k):
            lidx = lax.broadcasted_iota(jnp.int32, x.shape, 1)
            y = roll(x, -LANE_W * k, 1)
            return jnp.where((lidx < LANE_W) & has_right, y, 0.0)

        def above_tile(x, k):
            r, o = RADII[k], OFFSETS[k]
            y = roll(x, 8 - r - o, 0)[:8]
            ridx = lax.broadcasted_iota(jnp.int32, y.shape, 0)
            return jnp.where(ridx >= 8 - r, y, 0.0)

        def below_tile(x, k):
            r, o = RADII[k], OFFSETS[k]
            y = roll(x, -o, 0)[:8]
            ridx = lax.broadcasted_iota(jnp.int32, y.shape, 0)
            return jnp.where(ridx < r, y, 0.0)

        a_m, a_l, a_r = am[...], al[...], ar[...]
        b_m, b_l, b_r = bm[...], bl[...], br[...]

        def window(k):
            lft = jnp.where(first, lane_left(side_v, k), lefts[k])
            rgt = jnp.where(last, lane_right(side_v, k), rights[k])
            core = jnp.concatenate([lft, mains[k], rgt], axis=-1)
            top = jnp.concatenate([jnp.where(first, lane_left(ca, k), above_tile(a_l, k)),
                                   above_tile(a_m, k),
                                   jnp.where(last, lane_right(ca, k), above_tile(a_r, k))], axis=-1)
            bot = jnp.concatenate([jnp.where(first, lane_left(cb, k), below_tile(b_l, k)),
                                   below_tile(b_m, k),
                                   jnp.where(last, lane_right(cb, k), below_tile(b_r, k))], axis=-1)
            return jnp.concatenate([top, core, bot], axis=0)

        u0, u1, v0, v1, d, h, t = [window(k) for k in range(nf)]
        shape = d.shape
        grow = lax.broadcasted_iota(jnp.int32, shape, 0) + (pos_ref[0] * rows - HR)
        gcol = lax.broadcasted_iota(jnp.int32, shape, 1) + (pos_ref[1] * cols + j * BW - HC)
        valid = (grow >= 0) & (grow < total_rows) & (gcol >= 0) & (gcol < total_cols)
        n0, n1, w0, w1, hn, d3 = step_fields(u0, u1, v0, v1, d, h, t, valid, rl)

        def core(x):
            return x[HR:HR + rows, HC:HC + BW]

        uo[0] = core(n0)
        uo[1] = core(n1)
        vo[0] = core(w0)
        vo[1] = core(w1)
        ho[...] = core(hn)
        do[...] = core(d3)

    def lcol(j):
        return jnp.maximum(j * per - 1, 0)

    def rcol(j):
        return jnp.minimum((j + 1) * per, last_col_block)

    main2 = pl.BlockSpec((2, rows, BW), lambda j: (0, 0, j))
    left2 = pl.BlockSpec((2, rows, HC), lambda j: (0, 0, lcol(j)))
    right2 = pl.BlockSpec((2, rows, HC), lambda j: (0, 0, rcol(j)))
    main1 = pl.BlockSpec((rows, BW), lambda j: (0, j))
    left1 = pl.BlockSpec((rows, HC), lambda j: (0, lcol(j)))
    right1 = pl.BlockSpec((rows, HC), lambda j: (0, rcol(j)))
    sm = pl.BlockSpec((STRIP, BW), lambda j: (0, j))
    sl = pl.BlockSpec((STRIP, HC), lambda j: (0, lcol(j)))
    sr = pl.BlockSpec((STRIP, HC), lambda j: (0, rcol(j)))
    sidespec = pl.BlockSpec((rows, HC), lambda j: (0, 0))
    cornerspec = pl.BlockSpec((8, HC), lambda j: (0, 0))
    out2 = pl.BlockSpec((2, rows, BW), lambda j: (0, 0, j))
    out1 = pl.BlockSpec((rows, BW), lambda j: (0, j))
    outs = pl.pallas_call(
        kernel,
        grid=(nblocks,),
        in_specs=[smem, main2, left2, right2, main2, left2, right2,
                  main1, left1, right1, main1, left1, right1, main1, left1, right1,
                  sm, sl, sr, sm, sl, sr, sidespec, cornerspec, cornerspec],
        out_specs=[out2, out2, out1, out1],
        out_shape=[jax.ShapeDtypeStruct((2, rows, cols), f32), jax.ShapeDtypeStruct((2, rows, cols), f32),
                   jax.ShapeDtypeStruct((rows, cols), f32), jax.ShapeDtypeStruct((rows, cols), f32)],
        interpret=INTERPRET,
    )(pos, displacement, displacement, displacement, velocity, velocity, velocity,
      damage, damage, damage, history, history, history, toughness, toughness, toughness,
      above, above, above, below, below, below, side, corner_above, corner_below)
    return tuple(outs)


def solution(mesh):
    placed = (P(None, "gx", "gy"), P(None, "gx", "gy"), P("gx", "gy"), P("gx", "gy"), P("gx", "gy"))
    return jax.shard_map(
        on_device,
        mesh=mesh,
        in_specs=placed,
        out_specs=(P(None, "gx", "gy"), P(None, "gx", "gy"), P("gx", "gy"), P("gx", "gy")),
        check_vma=False,
    )
```

```python
import functools

import jax
import jax.numpy as jnp
from jax import lax
from jax.experimental import pallas as pl
from jax.experimental.pallas import tpu as pltpu
from jax.sharding import PartitionSpec as P

CHEB = 0.94
WEIGHT_TWO = 1.0 / (1.0 - CHEB * CHEB / 2.0)
WEIGHT_THREE = 1.0 / (1.0 - CHEB * CHEB * WEIGHT_TWO / 4.0)

HR = 8
HC = 128
BW = 2048
INTERPRET = False


def roll_shift(x, d, axis):
    return pltpu.roll(x, (-d) % x.shape[axis], axis)


def jnp_shift(x, d, axis):
    return jnp.roll(x, -d, axis)


def step_fields(u0, u1, v0, v1, dmg, hist, tough, valid, sh):
    zero = jnp.zeros_like(dmg)

    def strain(first, second):
        exx = (sh(first, 1, 0) - sh(first, -1, 0)) * 0.5
        eyy = (sh(second, 1, 1) - sh(second, -1, 1)) * 0.5
        exy = ((sh(first, 1, 1) - sh(first, -1, 1)) + (sh(second, 1, 0) - sh(second, -1, 0))) * 0.25
        return exx, eyy, exy

    degrade = (1.0 - dmg) ** 2 + 0.001

    def accel(exx, eyy, exy):
        trace = exx + eyy
        sxx = jnp.where(valid, degrade * (trace + 2.0 * exx), zero)
        syy = jnp.where(valid, degrade * (trace + 2.0 * eyy), zero)
        sxy = jnp.where(valid, degrade * 2.0 * exy, zero)
        a0 = ((sh(sxx, 1, 0) - sh(sxx, -1, 0)) + (sh(sxy, 1, 1) - sh(sxy, -1, 1))) * 0.5
        a1 = ((sh(sxy, 1, 0) - sh(sxy, -1, 0)) + (sh(syy, 1, 1) - sh(syy, -1, 1))) * 0.5
        return a0, a1

    a0, a1 = accel(*strain(u0 + 0.5 * v0, u1 + 0.5 * v1))
    h0 = jnp.where(valid, v0 + 0.1 * a0, zero)
    h1 = jnp.where(valid, v1 + 0.1 * a1, zero)
    n0 = jnp.where(valid, u0 + 0.2 * h0, zero)
    n1 = jnp.where(valid, u1 + 0.2 * h1, zero)
    e = strain(n0, n1)
    eh = strain(h0, h1)
    b0, b1 = accel(e[0] + 0.5 * eh[0], e[1] + 0.5 * eh[1], e[2] + 0.5 * eh[2])
    vel0 = h0 + 0.1 * b0
    vel1 = h1 + 0.1 * b1
    tr = jnp.maximum(e[0] + e[1], 0.0)
    hist_new = jnp.maximum(hist, 0.5 * tr * tr + e[0] * e[0] + e[1] * e[1] + 2.0 * e[2] * e[2])

    k_down = tough + sh(tough, 1, 0)
    k_up = tough + sh(tough, -1, 0)
    k_right = tough + sh(tough, 1, 1)
    k_left = tough + sh(tough, -1, 1)
    two_h = 2.0 * hist_new
    inv_denom = 1.0 / (tough * 0.5 + two_h + k_down + k_up + k_right + k_left)

    def jacobi(f):
        numer = two_h + k_down * sh(f, 1, 0) + k_up * sh(f, -1, 0)
        numer = numer + k_right * sh(f, 1, 1) + k_left * sh(f, -1, 1)
        return numer * inv_denom

    d1 = jnp.where(valid, jacobi(dmg), zero)
    d2 = jnp.where(valid, dmg + WEIGHT_TWO * (jacobi(d1) - dmg), zero)
    d3 = d1 + WEIGHT_THREE * (jacobi(d2) - d1)
    return n0, n1, vel0, vel1, hist_new, d3


RADII = (5, 5, 5, 5, 4, 2, 3)
OFFSETS = tuple(sum(RADII[:k]) for k in range(len(RADII)))
STRIP = 32
LANE_W = 5


def on_device(displacement, velocity, damage, history, toughness):
    rows, cols = damage.shape
    nx = lax.axis_size("gx")
    ny = lax.axis_size("gy")
    ix = lax.axis_index("gx")
    iy = lax.axis_index("gy")
    assert ny == 2 and rows % 8 == 0 and cols % (2 * BW) == 0
    total_rows, total_cols = rows * nx, cols * ny
    nf = len(RADII)
    pos = jnp.stack([ix, iy]).astype(jnp.int32)
    nblocks = cols // BW
    per = BW // HC
    last_col_block = cols // HC - 1
    last_row_block = rows // 8 - 1
    f32 = damage.dtype
    rl = jnp_shift if INTERPRET else roll_shift

    def roll(x, s, axis):
        return rl(x, -s, axis)

    def split(refs):
        du, dv, dd, dh, dt = refs
        return [du[0], du[1], dv[0], dv[1], dd[...], dh[...], dt[...]]

    pw = cols
    half = cols // 2
    off = half // HC

    def pack_kernel(pos_ref, tu, tv, td, th, tt, bu, bv, bd, bh, bt,
                    lu, lv, ld, lh, lt, ru, rv, rd, rh, rt, top0_o, top1_o, bot0_o, bot1_o, col_o):
        j = pl.program_id(0)
        tops = split((tu, tv, td, th, tt))
        bots = split((bu, bv, bd, bh, bt))
        ridx = lax.broadcasted_iota(jnp.int32, (STRIP, pw), 0)
        top = jnp.zeros((STRIP, pw), f32)
        bot = jnp.zeros((STRIP, pw), f32)
        pad = jnp.zeros((STRIP - 8, pw), f32)
        for k in range(nf):
            r, o = RADII[k], OFFSETS[k]
            inside = (ridx >= o) & (ridx < o + r)
            x = roll(jnp.concatenate([tops[k], pad], axis=0), o, 0)
            top = jnp.where(inside, x, top)
            y = roll(jnp.concatenate([bots[k], pad], axis=0), o - (8 - r), 0)
            bot = jnp.where(inside, y, bot)
        top0_o[...] = top[:, :half + HC]
        top1_o[...] = top[:, half:]
        bot0_o[...] = bot[:, :half + HC]
        bot1_o[...] = bot[:, half:]

        @pl.when(j == 0)
        def _():
            lefts = split((lu, lv, ld, lh, lt))
            rights = split((ru, rv, rd, rh, rt))
            lidx = lax.broadcasted_iota(jnp.int32, (rows, HC), 1)
            col = jnp.zeros((rows, HC), f32)
            to_right = pos_ref[1] == 0
            for k in range(nf):
                inside = (lidx >= LANE_W * k) & (lidx < LANE_W * (k + 1))
                a = roll(rights[k], LANE_W * k - (HC - LANE_W), 1)
                b = roll(lefts[k], LANE_W * k, 1)
                col = jnp.where(inside, jnp.where(to_right, a, b), col)
            col_o[...] = col

    t2 = pl.BlockSpec((2, 8, pw), lambda j: (0, 0, j))
    t1 = pl.BlockSpec((8, pw), lambda j: (0, j))
    b2 = pl.BlockSpec((2, 8, pw), lambda j: (0, last_row_block, j))
    b1 = pl.BlockSpec((8, pw), lambda j: (last_row_block, j))
    l2 = pl.BlockSpec((2, rows, HC), lambda j: (0, 0, 0))
    l1 = pl.BlockSpec((rows, HC), lambda j: (0, 0))
    r2 = pl.BlockSpec((2, rows, HC), lambda j: (0, 0, last_col_block))
    r1 = pl.BlockSpec((rows, HC), lambda j: (0, last_col_block))
    smem = pl.BlockSpec(memory_space=pltpu.SMEM)
    ins = (displacement, velocity, damage, history, toughness)
    top0, top1, bot0, bot1, col_s = pl.pallas_call(
        pack_kernel,
        grid=(cols // pw,),
        in_specs=[smem, t2, t2, t1, t1, t1, b2, b2, b1, b1, b1, l2, l2, l1, l1, l1, r2, r2, r1, r1, r1],
        out_specs=[pl.BlockSpec((STRIP, half + HC), lambda j: (0, 0)), pl.BlockSpec((STRIP, half), lambda j: (0, 0)),
                   pl.BlockSpec((STRIP, half + HC), lambda j: (0, 0)), pl.BlockSpec((STRIP, half), lambda j: (0, 0)),
                   pl.BlockSpec((rows, HC), lambda j: (0, 0))],
        out_shape=[jax.ShapeDtypeStruct((STRIP, half + HC), f32), jax.ShapeDtypeStruct((STRIP, half), f32),
                   jax.ShapeDtypeStruct((STRIP, half + HC), f32), jax.ShapeDtypeStruct((STRIP, half), f32),
                   jax.ShapeDtypeStruct((rows, HC), f32)],
        interpret=INTERPRET,
    )(pos, *ins, *ins, *ins, *ins)

    down = [(i, i + 1) for i in range(nx - 1)]
    up = [(i + 1, i) for i in range(nx - 1)]
    above0 = lax.ppermute(bot0, "gx", down)
    below0 = lax.ppermute(top0, "gx", up)
    side = lax.ppermute(col_s, "gy", [(0, 1), (1, 0)])
    both = ("gx", "gy")
    corner_above = lax.ppermute(col_s[rows - 8:], both,
                                [(i * 2 + g, (i + 1) * 2 + 1 - g) for i in range(nx - 1) for g in range(2)])
    corner_below = lax.ppermute(col_s[:8], both,
                                [((i + 1) * 2 + g, i * 2 + 1 - g) for i in range(nx - 1) for g in range(2)])
    side, corner_above, corner_below, bot1, top1 = lax.optimization_barrier(
        (side, corner_above, corner_below, bot1, top1))
    above1 = lax.ppermute(bot1, "gx", down)
    below1 = lax.ppermute(top1, "gx", up)

    def kernel(jbase, pos_ref, um, ul, ur, vm, vl, vr, dm, dl, dr, hm, hl, hr, tm, tl, tr,
               am, al, ar, ap, bm, bl, br, bp, side_ref, ca_ref, cb_ref, *rest):
        uo, vo, ho, do = rest[-4:]
        j = pl.program_id(0) + jbase
        first = j == 0
        last = j == nblocks - 1
        has_left = pos_ref[1] == 1
        has_right = pos_ref[1] == 0
        mains = split((um, vm, dm, hm, tm))
        lefts = split((ul, vl, dl, hl, tl))
        rights = split((ur, vr, dr, hr, tr))
        side_v = side_ref[...]
        ca = ca_ref[...]
        cb = cb_ref[...]

        def lane_left(x, k):
            lidx = lax.broadcasted_iota(jnp.int32, x.shape, 1)
            y = roll(x, HC - LANE_W - LANE_W * k, 1)
            return jnp.where((lidx >= HC - LANE_W) & has_left, y, 0.0)

        def lane_right(x, k):
            lidx = lax.broadcasted_iota(jnp.int32, x.shape, 1)
            y = roll(x, -LANE_W * k, 1)
            return jnp.where((lidx < LANE_W) & has_right, y, 0.0)

        def above_tile(x, k):
            r, o = RADII[k], OFFSETS[k]
            y = roll(x, 8 - r - o, 0)[:8]
            ridx = lax.broadcasted_iota(jnp.int32, y.shape, 0)
            return jnp.where(ridx >= 8 - r, y, 0.0)

        def below_tile(x, k):
            r, o = RADII[k], OFFSETS[k]
            y = roll(x, -o, 0)[:8]
            ridx = lax.broadcasted_iota(jnp.int32, y.shape, 0)
            return jnp.where(ridx < r, y, 0.0)

        a_m, a_l, a_r = am[...], al[...], ar[...]
        b_m, b_l, b_r = bm[...], bl[...], br[...]
        if jbase:
            a_l = jnp.where(j == jbase, ap[...], a_l)
            b_l = jnp.where(j == jbase, bp[...], b_l)

        def window(k):
            lft = jnp.where(first, lane_left(side_v, k), lefts[k])
            rgt = jnp.where(last, lane_right(side_v, k), rights[k])
            core = jnp.concatenate([lft, mains[k], rgt], axis=-1)
            top = jnp.concatenate([jnp.where(first, lane_left(ca, k), above_tile(a_l, k)),
                                   above_tile(a_m, k),
                                   jnp.where(last, lane_right(ca, k), above_tile(a_r, k))], axis=-1)
            bot = jnp.concatenate([jnp.where(first, lane_left(cb, k), below_tile(b_l, k)),
                                   below_tile(b_m, k),
                                   jnp.where(last, lane_right(cb, k), below_tile(b_r, k))], axis=-1)
            return jnp.concatenate([top, core, bot], axis=0)

        u0, u1, v0, v1, d, h, t = [window(k) for k in range(nf)]
        shape = d.shape
        grow = lax.broadcasted_iota(jnp.int32, shape, 0) + (pos_ref[0] * rows - HR)
        gcol = lax.broadcasted_iota(jnp.int32, shape, 1) + (pos_ref[1] * cols + j * BW - HC)
        valid = (grow >= 0) & (grow < total_rows) & (gcol >= 0) & (gcol < total_cols)
        n0, n1, w0, w1, hn, d3 = step_fields(u0, u1, v0, v1, d, h, t, valid, rl)

        def core(x):
            return x[HR:HR + rows, HC:HC + BW]

        uo[0] = core(n0)
        uo[1] = core(n1)
        vo[0] = core(w0)
        vo[1] = core(w1)
        ho[...] = core(hn)
        do[...] = core(d3)

    def lcol(j):
        return jnp.maximum(j * per - 1, 0)

    def rcol(j):
        return jnp.minimum((j + 1) * per, last_col_block)

    nhalf = nblocks // 2

    def run_half(h, above_h, below_h, prior):
        jb = h * nhalf
        shift = off if h else 0

        def at(f):
            return lambda i: f(i + jb)

        main2 = pl.BlockSpec((2, rows, BW), at(lambda j: (0, 0, j)))
        left2 = pl.BlockSpec((2, rows, HC), at(lambda j: (0, 0, lcol(j))))
        right2 = pl.BlockSpec((2, rows, HC), at(lambda j: (0, 0, rcol(j))))
        main1 = pl.BlockSpec((rows, BW), at(lambda j: (0, j)))
        left1 = pl.BlockSpec((rows, HC), at(lambda j: (0, lcol(j))))
        right1 = pl.BlockSpec((rows, HC), at(lambda j: (0, rcol(j))))
        sm = pl.BlockSpec((STRIP, BW), lambda i: (0, i))
        sl = pl.BlockSpec((STRIP, HC), at(lambda j: (0, jnp.maximum(lcol(j) - shift, 0))))
        sr = pl.BlockSpec((STRIP, HC), at(lambda j: (0, rcol(j) - shift)))
        sp = pl.BlockSpec((STRIP, HC), lambda i: (0, off - 1))
        sidespec = pl.BlockSpec((rows, HC), lambda i: (0, 0))
        cornerspec = pl.BlockSpec((8, HC), lambda i: (0, 0))
        out2 = pl.BlockSpec((2, rows, BW), at(lambda j: (0, 0, j)))
        out1 = pl.BlockSpec((rows, BW), at(lambda j: (0, j)))
        in_specs = [smem, main2, left2, right2, main2, left2, right2,
                    main1, left1, right1, main1, left1, right1, main1, left1, right1,
                    sm, sl, sr, sp, sm, sl, sr, sp, sidespec, cornerspec, cornerspec]
        args = [pos, displacement, displacement, displacement, velocity, velocity, velocity,
                damage, damage, damage, history, history, history, toughness, toughness, toughness,
                above_h, above_h, above_h, above0, below_h, below_h, below_h, below0,
                side, corner_above, corner_below]
        aliases = {}
        if prior is not None:
            aliases = {len(args) + k: k for k in range(4)}
            in_specs = in_specs + [pl.BlockSpec(memory_space=pl.ANY)] * 4
            args = args + list(prior)
        return pl.pallas_call(
            functools.partial(kernel, jb),
            grid=(nhalf,),
            in_specs=in_specs,
            out_specs=[out2, out2, out1, out1],
            out_shape=[jax.ShapeDtypeStruct((2, rows, cols), f32), jax.ShapeDtypeStruct((2, rows, cols), f32),
                       jax.ShapeDtypeStruct((rows, cols), f32), jax.ShapeDtypeStruct((rows, cols), f32)],
            input_output_aliases=aliases,
            interpret=INTERPRET,
        )(*args)

    outs = run_half(0, above0, below0, None)
    outs = run_half(1, above1, below1, outs)
    return tuple(outs)


def solution(mesh):
    placed = (P(None, "gx", "gy"), P(None, "gx", "gy"), P("gx", "gy"), P("gx", "gy"), P("gx", "gy"))
    return jax.shard_map(
        on_device,
        mesh=mesh,
        in_specs=placed,
        out_specs=(P(None, "gx", "gy"), P(None, "gx", "gy"), P("gx", "gy"), P("gx", "gy")),
        check_vma=False,
    )
```

```python
import jax
import jax.numpy as jnp
from jax import lax
from jax.experimental import pallas as pl
from jax.experimental.pallas import tpu as pltpu
from jax.sharding import PartitionSpec as P

CHEB = 0.94
WEIGHT_TWO = 1.0 / (1.0 - CHEB * CHEB / 2.0)
WEIGHT_THREE = 1.0 / (1.0 - CHEB * CHEB * WEIGHT_TWO / 4.0)

HR = 8
HC = 128
BW = 2048
INTERPRET = False


def roll_shift(x, d, axis):
    return pltpu.roll(x, (-d) % x.shape[axis], axis)


def jnp_shift(x, d, axis):
    return jnp.roll(x, -d, axis)


def step_fields(u0, u1, v0, v1, dmg, hist, tough, valid, sh):
    zero = jnp.zeros_like(dmg)

    def strain(first, second):
        exx = (sh(first, 1, 0) - sh(first, -1, 0)) * 0.5
        eyy = (sh(second, 1, 1) - sh(second, -1, 1)) * 0.5
        exy = ((sh(first, 1, 1) - sh(first, -1, 1)) + (sh(second, 1, 0) - sh(second, -1, 0))) * 0.25
        return exx, eyy, exy

    degrade = (1.0 - dmg) ** 2 + 0.001
    degrade2 = degrade * 2.0

    def accel(exx, eyy, exy):
        trace = exx + eyy
        sxx = jnp.where(valid, degrade * (trace + 2.0 * exx), zero)
        syy = jnp.where(valid, degrade * (trace + 2.0 * eyy), zero)
        sxy = jnp.where(valid, degrade2 * exy, zero)
        a0 = ((sh(sxx, 1, 0) - sh(sxx, -1, 0)) + (sh(sxy, 1, 1) - sh(sxy, -1, 1))) * 0.5
        a1 = ((sh(sxy, 1, 0) - sh(sxy, -1, 0)) + (sh(syy, 1, 1) - sh(syy, -1, 1))) * 0.5
        return a0, a1

    a0, a1 = accel(*strain(u0 + 0.5 * v0, u1 + 0.5 * v1))
    h0 = jnp.where(valid, v0 + 0.1 * a0, zero)
    h1 = jnp.where(valid, v1 + 0.1 * a1, zero)
    n0 = jnp.where(valid, u0 + 0.2 * h0, zero)
    n1 = jnp.where(valid, u1 + 0.2 * h1, zero)
    e = strain(n0, n1)
    eh = strain(h0, h1)
    b0, b1 = accel(e[0] + 0.5 * eh[0], e[1] + 0.5 * eh[1], e[2] + 0.5 * eh[2])
    vel0 = h0 + 0.1 * b0
    vel1 = h1 + 0.1 * b1
    tr = jnp.maximum(e[0] + e[1], 0.0)
    hist_new = jnp.maximum(hist, 0.5 * tr * tr + e[0] * e[0] + e[1] * e[1] + 2.0 * e[2] * e[2])

    k_down = tough + sh(tough, 1, 0)
    k_up = tough + sh(tough, -1, 0)
    k_right = tough + sh(tough, 1, 1)
    k_left = tough + sh(tough, -1, 1)
    two_h = 2.0 * hist_new
    inv_denom = 1.0 / (tough * 0.5 + two_h + k_down + k_up + k_right + k_left)

    def jacobi(f):
        numer = two_h + k_down * sh(f, 1, 0) + k_up * sh(f, -1, 0)
        numer = numer + k_right * sh(f, 1, 1) + k_left * sh(f, -1, 1)
        return numer * inv_denom

    d1 = jnp.where(valid, jacobi(dmg), zero)
    d2 = jnp.where(valid, dmg + WEIGHT_TWO * (jacobi(d1) - dmg), zero)
    d3 = d1 + WEIGHT_THREE * (jacobi(d2) - d1)
    return n0, n1, vel0, vel1, hist_new, d3


RADII = (5, 5, 5, 5, 4, 2, 3)
OFFSETS = tuple(sum(RADII[:k]) for k in range(len(RADII)))
STRIP = 32
LANE_W = 5


def on_device(displacement, velocity, damage, history, toughness):
    rows, cols = damage.shape
    nx = lax.axis_size("gx")
    ny = lax.axis_size("gy")
    ix = lax.axis_index("gx")
    iy = lax.axis_index("gy")
    assert ny == 2 and rows % 8 == 0 and cols % BW == 0
    total_rows, total_cols = rows * nx, cols * ny
    nf = len(RADII)
    pos = jnp.stack([ix, iy]).astype(jnp.int32)
    nblocks = cols // BW
    per = BW // HC
    last_col_block = cols // HC - 1
    last_row_block = rows // 8 - 1
    f32 = damage.dtype
    rl = jnp_shift if INTERPRET else roll_shift

    def roll(x, s, axis):
        return rl(x, -s, axis)

    def split(refs):
        du, dv, dd, dh, dt = refs
        return [du[0], du[1], dv[0], dv[1], dd[...], dh[...], dt[...]]

    pw = cols

    def pack_kernel(pos_ref, tu, tv, td, th, tt, bu, bv, bd, bh, bt,
                    lu, lv, ld, lh, lt, ru, rv, rd, rh, rt, top_o, bot_o, col_o):
        j = pl.program_id(0)
        tops = split((tu, tv, td, th, tt))
        bots = split((bu, bv, bd, bh, bt))
        ridx = lax.broadcasted_iota(jnp.int32, (STRIP, pw), 0)
        top = jnp.zeros((STRIP, pw), f32)
        bot = jnp.zeros((STRIP, pw), f32)
        pad = jnp.zeros((STRIP - 8, pw), f32)
        for k in range(nf):
            r, o = RADII[k], OFFSETS[k]
            inside = (ridx >= o) & (ridx < o + r)
            x = roll(jnp.concatenate([tops[k], pad], axis=0), o, 0)
            top = jnp.where(inside, x, top)
            y = roll(jnp.concatenate([bots[k], pad], axis=0), o - (8 - r), 0)
            bot = jnp.where(inside, y, bot)
        top_o[...] = top
        bot_o[...] = bot

        @pl.when(j == 0)
        def _():
            lefts = split((lu, lv, ld, lh, lt))
            rights = split((ru, rv, rd, rh, rt))
            lidx = lax.broadcasted_iota(jnp.int32, (rows, HC), 1)
            col = jnp.zeros((rows, HC), f32)
            to_right = pos_ref[1] == 0
            for k in range(nf):
                inside = (lidx >= LANE_W * k) & (lidx < LANE_W * (k + 1))
                a = roll(rights[k], LANE_W * k - (HC - LANE_W), 1)
                b = roll(lefts[k], LANE_W * k, 1)
                col = jnp.where(inside, jnp.where(to_right, a, b), col)
            col_o[...] = col

    t2 = pl.BlockSpec((2, 8, pw), lambda j: (0, 0, j))
    t1 = pl.BlockSpec((8, pw), lambda j: (0, j))
    b2 = pl.BlockSpec((2, 8, pw), lambda j: (0, last_row_block, j))
    b1 = pl.BlockSpec((8, pw), lambda j: (last_row_block, j))
    l2 = pl.BlockSpec((2, rows, HC), lambda j: (0, 0, 0))
    l1 = pl.BlockSpec((rows, HC), lambda j: (0, 0))
    r2 = pl.BlockSpec((2, rows, HC), lambda j: (0, 0, last_col_block))
    r1 = pl.BlockSpec((rows, HC), lambda j: (0, last_col_block))
    smem = pl.BlockSpec(memory_space=pltpu.SMEM)
    ins = (displacement, velocity, damage, history, toughness)
    top_s, bot_s, col_s = pl.pallas_call(
        pack_kernel,
        grid=(cols // pw,),
        in_specs=[smem, t2, t2, t1, t1, t1, b2, b2, b1, b1, b1, l2, l2, l1, l1, l1, r2, r2, r1, r1, r1],
        out_specs=[pl.BlockSpec((STRIP, pw), lambda j: (0, j)), pl.BlockSpec((STRIP, pw), lambda j: (0, j)),
                   pl.BlockSpec((rows, HC), lambda j: (0, 0))],
        out_shape=[jax.ShapeDtypeStruct((STRIP, cols), f32), jax.ShapeDtypeStruct((STRIP, cols), f32),
                   jax.ShapeDtypeStruct((rows, HC), f32)],
        interpret=INTERPRET,
    )(pos, *ins, *ins, *ins, *ins)

    above = lax.ppermute(bot_s, "gx", [(i, i + 1) for i in range(nx - 1)])
    below = lax.ppermute(top_s, "gx", [(i + 1, i) for i in range(nx - 1)])
    side = lax.ppermute(col_s, "gy", [(0, 1), (1, 0)])
    both = ("gx", "gy")
    corner_above = lax.ppermute(col_s[rows - 8:], both,
                                [(i * 2 + g, (i + 1) * 2 + 1 - g) for i in range(nx - 1) for g in range(2)])
    corner_below = lax.ppermute(col_s[:8], both,
                                [((i + 1) * 2 + g, i * 2 + 1 - g) for i in range(nx - 1) for g in range(2)])

    def kernel(pos_ref, um, ul, ur, vm, vl, vr, dm, dl, dr, hm, hl, hr, tm, tl, tr,
               am, al, ar, bm, bl, br, side_ref, ca_ref, cb_ref, uo, vo, ho, do):
        j = pl.program_id(0)
        first = j == 0
        last = j == nblocks - 1
        has_left = pos_ref[1] == 1
        has_right = pos_ref[1] == 0
        mains = split((um, vm, dm, hm, tm))
        lefts = split((ul, vl, dl, hl, tl))
        rights = split((ur, vr, dr, hr, tr))
        side_v = side_ref[...]
        ca = ca_ref[...]
        cb = cb_ref[...]

        def lane_left(x, k):
            lidx = lax.broadcasted_iota(jnp.int32, x.shape, 1)
            y = roll(x, HC - LANE_W - LANE_W * k, 1)
            return jnp.where((lidx >= HC - LANE_W) & has_left, y, 0.0)

        def lane_right(x, k):
            lidx = lax.broadcasted_iota(jnp.int32, x.shape, 1)
            y = roll(x, -LANE_W * k, 1)
            return jnp.where((lidx < LANE_W) & has_right, y, 0.0)

        def above_tile(x, k):
            r, o = RADII[k], OFFSETS[k]
            y = roll(x, 8 - r - o, 0)[:8]
            ridx = lax.broadcasted_iota(jnp.int32, y.shape, 0)
            return jnp.where(ridx >= 8 - r, y, 0.0)

        def below_tile(x, k):
            r, o = RADII[k], OFFSETS[k]
            y = roll(x, -o, 0)[:8]
            ridx = lax.broadcasted_iota(jnp.int32, y.shape, 0)
            return jnp.where(ridx < r, y, 0.0)

        a_m, a_l, a_r = am[...], al[...], ar[...]
        b_m, b_l, b_r = bm[...], bl[...], br[...]

        def window(k):
            lft = jnp.where(first, lane_left(side_v, k), lefts[k])
            rgt = jnp.where(last, lane_right(side_v, k), rights[k])
            core = jnp.concatenate([lft, mains[k], rgt], axis=-1)
            top = jnp.concatenate([jnp.where(first, lane_left(ca, k), above_tile(a_l, k)),
                                   above_tile(a_m, k),
                                   jnp.where(last, lane_right(ca, k), above_tile(a_r, k))], axis=-1)
            bot = jnp.concatenate([jnp.where(first, lane_left(cb, k), below_tile(b_l, k)),
                                   below_tile(b_m, k),
                                   jnp.where(last, lane_right(cb, k), below_tile(b_r, k))], axis=-1)
            return jnp.concatenate([top, core, bot], axis=0)

        u0, u1, v0, v1, d, h, t = [window(k) for k in range(nf)]
        shape = d.shape
        grow = lax.broadcasted_iota(jnp.int32, (shape[0], 1), 0) + (pos_ref[0] * rows - HR)
        gcol = lax.broadcasted_iota(jnp.int32, (1, shape[1]), 1) + (pos_ref[1] * cols + j * BW - HC)
        valid = ((grow >= 0) & (grow < total_rows)) & ((gcol >= 0) & (gcol < total_cols))
        n0, n1, w0, w1, hn, d3 = step_fields(u0, u1, v0, v1, d, h, t, valid, rl)

        def core(x):
            return x[HR:HR + rows, HC:HC + BW]

        uo[0] = core(n0)
        uo[1] = core(n1)
        vo[0] = core(w0)
        vo[1] = core(w1)
        ho[...] = core(hn)
        do[...] = core(d3)

    def lcol(j):
        return jnp.maximum(j * per - 1, 0)

    def rcol(j):
        return jnp.minimum((j + 1) * per, last_col_block)

    main2 = pl.BlockSpec((2, rows, BW), lambda j: (0, 0, j))
    left2 = pl.BlockSpec((2, rows, HC), lambda j: (0, 0, lcol(j)))
    right2 = pl.BlockSpec((2, rows, HC), lambda j: (0, 0, rcol(j)))
    main1 = pl.BlockSpec((rows, BW), lambda j: (0, j))
    left1 = pl.BlockSpec((rows, HC), lambda j: (0, lcol(j)))
    right1 = pl.BlockSpec((rows, HC), lambda j: (0, rcol(j)))
    sm = pl.BlockSpec((STRIP, BW), lambda j: (0, j))
    sl = pl.BlockSpec((STRIP, HC), lambda j: (0, lcol(j)))
    sr = pl.BlockSpec((STRIP, HC), lambda j: (0, rcol(j)))
    sidespec = pl.BlockSpec((rows, HC), lambda j: (0, 0))
    cornerspec = pl.BlockSpec((8, HC), lambda j: (0, 0))
    out2 = pl.BlockSpec((2, rows, BW), lambda j: (0, 0, j))
    out1 = pl.BlockSpec((rows, BW), lambda j: (0, j))
    outs = pl.pallas_call(
        kernel,
        grid=(nblocks,),
        in_specs=[smem, main2, left2, right2, main2, left2, right2,
                  main1, left1, right1, main1, left1, right1, main1, left1, right1,
                  sm, sl, sr, sm, sl, sr, sidespec, cornerspec, cornerspec],
        out_specs=[out2, out2, out1, out1],
        out_shape=[jax.ShapeDtypeStruct((2, rows, cols), f32), jax.ShapeDtypeStruct((2, rows, cols), f32),
                   jax.ShapeDtypeStruct((rows, cols), f32), jax.ShapeDtypeStruct((rows, cols), f32)],
        interpret=INTERPRET,
    )(pos, displacement, displacement, displacement, velocity, velocity, velocity,
      damage, damage, damage, history, history, history, toughness, toughness, toughness,
      above, above, above, below, below, below, side, corner_above, corner_below)
    return tuple(outs)


def solution(mesh):
    placed = (P(None, "gx", "gy"), P(None, "gx", "gy"), P("gx", "gy"), P("gx", "gy"), P("gx", "gy"))
    return jax.shard_map(
        on_device,
        mesh=mesh,
        in_specs=placed,
        out_specs=(P(None, "gx", "gy"), P(None, "gx", "gy"), P("gx", "gy"), P("gx", "gy")),
        check_vma=False,
    )
```

```python
import jax
import jax.numpy as jnp
from jax import lax
from jax.experimental import pallas as pl
from jax.experimental.pallas import tpu as pltpu
from jax.sharding import PartitionSpec as P

CHEB = 0.94
WEIGHT_TWO = 1.0 / (1.0 - CHEB * CHEB / 2.0)
WEIGHT_THREE = 1.0 / (1.0 - CHEB * CHEB * WEIGHT_TWO / 4.0)

HR = 8
HC = 128
BW = 2048
INTERPRET = False


def roll_shift(x, d, axis):
    return pltpu.roll(x, (-d) % x.shape[axis], axis)


def jnp_shift(x, d, axis):
    return jnp.roll(x, -d, axis)


def step_fields(u0, u1, v0, v1, dmg, hist, tough, valid, sh):
    zero = jnp.zeros_like(dmg)

    def strain(first, second):
        exx = (sh(first, 1, 0) - sh(first, -1, 0)) * 0.5
        eyy = (sh(second, 1, 1) - sh(second, -1, 1)) * 0.5
        exy = ((sh(first, 1, 1) - sh(first, -1, 1)) + (sh(second, 1, 0) - sh(second, -1, 0))) * 0.25
        return exx, eyy, exy

    degrade = (1.0 - dmg) ** 2 + 0.001
    degrade2 = degrade * 2.0

    def accel(exx, eyy, exy):
        trace = exx + eyy
        sxx = jnp.where(valid, degrade * (trace + 2.0 * exx), zero)
        syy = jnp.where(valid, degrade * (trace + 2.0 * eyy), zero)
        sxy = jnp.where(valid, degrade2 * exy, zero)
        a0 = ((sh(sxx, 1, 0) - sh(sxx, -1, 0)) + (sh(sxy, 1, 1) - sh(sxy, -1, 1))) * 0.5
        a1 = ((sh(sxy, 1, 0) - sh(sxy, -1, 0)) + (sh(syy, 1, 1) - sh(syy, -1, 1))) * 0.5
        return a0, a1

    a0, a1 = accel(*strain(u0 + 0.5 * v0, u1 + 0.5 * v1))
    h0 = jnp.where(valid, v0 + 0.1 * a0, zero)
    h1 = jnp.where(valid, v1 + 0.1 * a1, zero)
    n0 = jnp.where(valid, u0 + 0.2 * h0, zero)
    n1 = jnp.where(valid, u1 + 0.2 * h1, zero)
    e = strain(n0, n1)
    eh = strain(h0, h1)
    b0, b1 = accel(e[0] + 0.5 * eh[0], e[1] + 0.5 * eh[1], e[2] + 0.5 * eh[2])
    vel0 = h0 + 0.1 * b0
    vel1 = h1 + 0.1 * b1
    tr = jnp.maximum(e[0] + e[1], 0.0)
    hist_new = jnp.maximum(hist, 0.5 * tr * tr + e[0] * e[0] + e[1] * e[1] + 2.0 * e[2] * e[2])

    k_down = tough + sh(tough, 1, 0)
    k_up = tough + sh(tough, -1, 0)
    k_right = tough + sh(tough, 1, 1)
    k_left = tough + sh(tough, -1, 1)
    two_h = 2.0 * hist_new
    inv_denom = 1.0 / (tough * 0.5 + two_h + k_down + k_up + k_right + k_left)

    def jacobi(f):
        numer = two_h + k_down * sh(f, 1, 0) + k_up * sh(f, -1, 0)
        numer = numer + k_right * sh(f, 1, 1) + k_left * sh(f, -1, 1)
        return numer * inv_denom

    d1 = jnp.where(valid, jacobi(dmg), zero)
    d2 = jnp.where(valid, dmg + WEIGHT_TWO * (jacobi(d1) - dmg), zero)
    d3 = d1 + WEIGHT_THREE * (jacobi(d2) - d1)
    return n0, n1, vel0, vel1, hist_new, d3


RADII = (5, 5, 5, 5, 4, 2, 3)
OFFSETS = tuple(sum(RADII[:k]) for k in range(len(RADII)))
STRIP = 32
SENT = sum(RADII)
LANE_W = 5


def on_device(displacement, velocity, damage, history, toughness):
    rows, cols = damage.shape
    nx = lax.axis_size("gx")
    ny = lax.axis_size("gy")
    ix = lax.axis_index("gx")
    iy = lax.axis_index("gy")
    assert ny == 2 and rows % 8 == 0 and cols % BW == 0
    total_rows, total_cols = rows * nx, cols * ny
    nf = len(RADII)
    pos = jnp.stack([ix, iy]).astype(jnp.int32)
    nblocks = cols // BW
    per = BW // HC
    last_col_block = cols // HC - 1
    last_row_block = rows // 8 - 1
    f32 = damage.dtype
    rl = jnp_shift if INTERPRET else roll_shift

    def roll(x, s, axis):
        return rl(x, -s, axis)

    def split(refs):
        du, dv, dd, dh, dt = refs
        return [du[0], du[1], dv[0], dv[1], dd[...], dh[...], dt[...]]

    pw = cols

    def pack_kernel(pos_ref, tu, tv, td, th, tt, bu, bv, bd, bh, bt,
                    lu, lv, ld, lh, lt, ru, rv, rd, rh, rt, top_o, bot_o, col_o):
        j = pl.program_id(0)
        tops = split((tu, tv, td, th, tt))
        bots = split((bu, bv, bd, bh, bt))
        ridx = lax.broadcasted_iota(jnp.int32, (STRIP, pw), 0)
        top = jnp.zeros((STRIP, pw), f32)
        bot = jnp.zeros((STRIP, pw), f32)
        pad = jnp.zeros((STRIP - 8, pw), f32)
        for k in range(nf):
            r, o = RADII[k], OFFSETS[k]
            inside = (ridx >= o) & (ridx < o + r)
            x = roll(jnp.concatenate([tops[k], pad], axis=0), o, 0)
            top = jnp.where(inside, x, top)
            y = roll(jnp.concatenate([bots[k], pad], axis=0), o - (8 - r), 0)
            bot = jnp.where(inside, y, bot)
        top_o[...] = top[:SENT]
        bot_o[...] = bot[:SENT]

        @pl.when(j == 0)
        def _():
            lefts = split((lu, lv, ld, lh, lt))
            rights = split((ru, rv, rd, rh, rt))
            lidx = lax.broadcasted_iota(jnp.int32, (rows, HC), 1)
            col = jnp.zeros((rows, HC), f32)
            to_right = pos_ref[1] == 0
            for k in range(nf):
                inside = (lidx >= LANE_W * k) & (lidx < LANE_W * (k + 1))
                a = roll(rights[k], LANE_W * k - (HC - LANE_W), 1)
                b = roll(lefts[k], LANE_W * k, 1)
                col = jnp.where(inside, jnp.where(to_right, a, b), col)
            col_o[...] = col

    t2 = pl.BlockSpec((2, 8, pw), lambda j: (0, 0, j))
    t1 = pl.BlockSpec((8, pw), lambda j: (0, j))
    b2 = pl.BlockSpec((2, 8, pw), lambda j: (0, last_row_block, j))
    b1 = pl.BlockSpec((8, pw), lambda j: (last_row_block, j))
    l2 = pl.BlockSpec((2, rows, HC), lambda j: (0, 0, 0))
    l1 = pl.BlockSpec((rows, HC), lambda j: (0, 0))
    r2 = pl.BlockSpec((2, rows, HC), lambda j: (0, 0, last_col_block))
    r1 = pl.BlockSpec((rows, HC), lambda j: (0, last_col_block))
    smem = pl.BlockSpec(memory_space=pltpu.SMEM)
    ins = (displacement, velocity, damage, history, toughness)
    top_s, bot_s, col_s = pl.pallas_call(
        pack_kernel,
        grid=(cols // pw,),
        in_specs=[smem, t2, t2, t1, t1, t1, b2, b2, b1, b1, b1, l2, l2, l1, l1, l1, r2, r2, r1, r1, r1],
        out_specs=[pl.BlockSpec((SENT, pw), lambda j: (0, j)), pl.BlockSpec((SENT, pw), lambda j: (0, j)),
                   pl.BlockSpec((rows, HC), lambda j: (0, 0))],
        out_shape=[jax.ShapeDtypeStruct((SENT, cols), f32), jax.ShapeDtypeStruct((SENT, cols), f32),
                   jax.ShapeDtypeStruct((rows, HC), f32)],
        interpret=INTERPRET,
    )(pos, *ins, *ins, *ins, *ins)

    above = lax.ppermute(bot_s, "gx", [(i, i + 1) for i in range(nx - 1)])
    below = lax.ppermute(top_s, "gx", [(i + 1, i) for i in range(nx - 1)])
    side = lax.ppermute(col_s, "gy", [(0, 1), (1, 0)])
    both = ("gx", "gy")
    corner_above = lax.ppermute(col_s[rows - 8:], both,
                                [(i * 2 + g, (i + 1) * 2 + 1 - g) for i in range(nx - 1) for g in range(2)])
    corner_below = lax.ppermute(col_s[:8], both,
                                [((i + 1) * 2 + g, i * 2 + 1 - g) for i in range(nx - 1) for g in range(2)])

    def kernel(pos_ref, um, ul, ur, vm, vl, vr, dm, dl, dr, hm, hl, hr, tm, tl, tr,
               am, al, ar, bm, bl, br, side_ref, ca_ref, cb_ref, uo, vo, ho, do):
        j = pl.program_id(0)
        first = j == 0
        last = j == nblocks - 1
        has_left = pos_ref[1] == 1
        has_right = pos_ref[1] == 0
        mains = split((um, vm, dm, hm, tm))
        lefts = split((ul, vl, dl, hl, tl))
        rights = split((ur, vr, dr, hr, tr))
        side_v = side_ref[...]
        ca = ca_ref[...]
        cb = cb_ref[...]

        def lane_left(x, k):
            lidx = lax.broadcasted_iota(jnp.int32, x.shape, 1)
            y = roll(x, HC - LANE_W - LANE_W * k, 1)
            return jnp.where((lidx >= HC - LANE_W) & has_left, y, 0.0)

        def lane_right(x, k):
            lidx = lax.broadcasted_iota(jnp.int32, x.shape, 1)
            y = roll(x, -LANE_W * k, 1)
            return jnp.where((lidx < LANE_W) & has_right, y, 0.0)

        def tile_of(ref, k, first_row):
            r, o = RADII[k], OFFSETS[k]
            s = min(max(o + first_row + r - 8 if first_row else o, 0), SENT - 8)
            y = ref[s:s + 8, :]
            shift = (first_row - (o - s)) % 8
            if shift:
                y = roll(y, shift, 0)
            ridx = lax.broadcasted_iota(jnp.int32, y.shape, 0)
            return jnp.where((ridx >= first_row) & (ridx < first_row + r), y, 0.0)

        def above_tile(ref, k):
            return tile_of(ref, k, 8 - RADII[k])

        def below_tile(ref, k):
            return tile_of(ref, k, 0)

        a_m, a_l, a_r = am, al, ar
        b_m, b_l, b_r = bm, bl, br

        def window(k):
            lft = jnp.where(first, lane_left(side_v, k), lefts[k])
            rgt = jnp.where(last, lane_right(side_v, k), rights[k])
            core = jnp.concatenate([lft, mains[k], rgt], axis=-1)
            top = jnp.concatenate([jnp.where(first, lane_left(ca, k), above_tile(a_l, k)),
                                   above_tile(a_m, k),
                                   jnp.where(last, lane_right(ca, k), above_tile(a_r, k))], axis=-1)
            bot = jnp.concatenate([jnp.where(first, lane_left(cb, k), below_tile(b_l, k)),
                                   below_tile(b_m, k),
                                   jnp.where(last, lane_right(cb, k), below_tile(b_r, k))], axis=-1)
            return jnp.concatenate([top, core, bot], axis=0)

        u0, u1, v0, v1, d, h, t = [window(k) for k in range(nf)]
        shape = d.shape
        grow = lax.broadcasted_iota(jnp.int32, (shape[0], 1), 0) + (pos_ref[0] * rows - HR)
        gcol = lax.broadcasted_iota(jnp.int32, (1, shape[1]), 1) + (pos_ref[1] * cols + j * BW - HC)
        valid = ((grow >= 0) & (grow < total_rows)) & ((gcol >= 0) & (gcol < total_cols))
        n0, n1, w0, w1, hn, d3 = step_fields(u0, u1, v0, v1, d, h, t, valid, rl)

        def core(x):
            return x[HR:HR + rows, HC:HC + BW]

        uo[0] = core(n0)
        uo[1] = core(n1)
        vo[0] = core(w0)
        vo[1] = core(w1)
        ho[...] = core(hn)
        do[...] = core(d3)

    def lcol(j):
        return jnp.maximum(j * per - 1, 0)

    def rcol(j):
        return jnp.minimum((j + 1) * per, last_col_block)

    main2 = pl.BlockSpec((2, rows, BW), lambda j: (0, 0, j))
    left2 = pl.BlockSpec((2, rows, HC), lambda j: (0, 0, lcol(j)))
    right2 = pl.BlockSpec((2, rows, HC), lambda j: (0, 0, rcol(j)))
    main1 = pl.BlockSpec((rows, BW), lambda j: (0, j))
    left1 = pl.BlockSpec((rows, HC), lambda j: (0, lcol(j)))
    right1 = pl.BlockSpec((rows, HC), lambda j: (0, rcol(j)))
    sm = pl.BlockSpec((SENT, BW), lambda j: (0, j))
    sl = pl.BlockSpec((SENT, HC), lambda j: (0, lcol(j)))
    sr = pl.BlockSpec((SENT, HC), lambda j: (0, rcol(j)))
    sidespec = pl.BlockSpec((rows, HC), lambda j: (0, 0))
    cornerspec = pl.BlockSpec((8, HC), lambda j: (0, 0))
    out2 = pl.BlockSpec((2, rows, BW), lambda j: (0, 0, j))
    out1 = pl.BlockSpec((rows, BW), lambda j: (0, j))
    outs = pl.pallas_call(
        kernel,
        grid=(nblocks,),
        in_specs=[smem, main2, left2, right2, main2, left2, right2,
                  main1, left1, right1, main1, left1, right1, main1, left1, right1,
                  sm, sl, sr, sm, sl, sr, sidespec, cornerspec, cornerspec],
        out_specs=[out2, out2, out1, out1],
        out_shape=[jax.ShapeDtypeStruct((2, rows, cols), f32), jax.ShapeDtypeStruct((2, rows, cols), f32),
                   jax.ShapeDtypeStruct((rows, cols), f32), jax.ShapeDtypeStruct((rows, cols), f32)],
        interpret=INTERPRET,
    )(pos, displacement, displacement, displacement, velocity, velocity, velocity,
      damage, damage, damage, history, history, history, toughness, toughness, toughness,
      above, above, above, below, below, below, side, corner_above, corner_below)
    return tuple(outs)


def solution(mesh):
    placed = (P(None, "gx", "gy"), P(None, "gx", "gy"), P("gx", "gy"), P("gx", "gy"), P("gx", "gy"))
    return jax.shard_map(
        on_device,
        mesh=mesh,
        in_specs=placed,
        out_specs=(P(None, "gx", "gy"), P(None, "gx", "gy"), P("gx", "gy"), P("gx", "gy")),
        check_vma=False,
    )
```

```python
import jax
import jax.numpy as jnp
from jax import lax
from jax.experimental import pallas as pl
from jax.experimental.pallas import tpu as pltpu
from jax.sharding import PartitionSpec as P

CHEB = 0.94
WEIGHT_TWO = 1.0 / (1.0 - CHEB * CHEB / 2.0)
WEIGHT_THREE = 1.0 / (1.0 - CHEB * CHEB * WEIGHT_TWO / 4.0)

HR = 8
HC = 128
BW = 2048
INTERPRET = False


def roll_shift(x, d, axis):
    return pltpu.roll(x, (-d) % x.shape[axis], axis)


def jnp_shift(x, d, axis):
    return jnp.roll(x, -d, axis)


def step_fields(u0, u1, v0, v1, dmg, hist, tough, valid, sh):
    zero = jnp.zeros_like(dmg)

    def strain(first, second):
        exx = (sh(first, 1, 0) - sh(first, -1, 0)) * 0.5
        eyy = (sh(second, 1, 1) - sh(second, -1, 1)) * 0.5
        exy = ((sh(first, 1, 1) - sh(first, -1, 1)) + (sh(second, 1, 0) - sh(second, -1, 0))) * 0.25
        return exx, eyy, exy

    degrade = (1.0 - dmg) ** 2 + 0.001
    degrade2 = degrade * 2.0

    def accel(exx, eyy, exy):
        trace = exx + eyy
        sxx = jnp.where(valid, degrade * (trace + 2.0 * exx), zero)
        syy = jnp.where(valid, degrade * (trace + 2.0 * eyy), zero)
        sxy = jnp.where(valid, degrade2 * exy, zero)
        a0 = ((sh(sxx, 1, 0) - sh(sxx, -1, 0)) + (sh(sxy, 1, 1) - sh(sxy, -1, 1))) * 0.5
        a1 = ((sh(sxy, 1, 0) - sh(sxy, -1, 0)) + (sh(syy, 1, 1) - sh(syy, -1, 1))) * 0.5
        return a0, a1

    a0, a1 = accel(*strain(u0 + 0.5 * v0, u1 + 0.5 * v1))
    h0 = jnp.where(valid, v0 + 0.1 * a0, zero)
    h1 = jnp.where(valid, v1 + 0.1 * a1, zero)
    n0 = jnp.where(valid, u0 + 0.2 * h0, zero)
    n1 = jnp.where(valid, u1 + 0.2 * h1, zero)
    e = strain(n0, n1)
    eh = strain(h0, h1)
    b0, b1 = accel(e[0] + 0.5 * eh[0], e[1] + 0.5 * eh[1], e[2] + 0.5 * eh[2])
    vel0 = h0 + 0.1 * b0
    vel1 = h1 + 0.1 * b1
    tr = jnp.maximum(e[0] + e[1], 0.0)
    hist_new = jnp.maximum(hist, 0.5 * tr * tr + e[0] * e[0] + e[1] * e[1] + 2.0 * e[2] * e[2])

    k_down = tough + sh(tough, 1, 0)
    k_up = tough + sh(tough, -1, 0)
    k_right = tough + sh(tough, 1, 1)
    k_left = tough + sh(tough, -1, 1)
    two_h = 2.0 * hist_new
    inv_denom = 1.0 / (tough * 0.5 + two_h + k_down + k_up + k_right + k_left)

    def jacobi(f):
        numer = two_h + k_down * sh(f, 1, 0) + k_up * sh(f, -1, 0)
        numer = numer + k_right * sh(f, 1, 1) + k_left * sh(f, -1, 1)
        return numer * inv_denom

    d1 = jnp.where(valid, jacobi(dmg), zero)
    d2 = jnp.where(valid, dmg + WEIGHT_TWO * (jacobi(d1) - dmg), zero)
    d3 = d1 + WEIGHT_THREE * (jacobi(d2) - d1)
    return n0, n1, vel0, vel1, hist_new, d3


RADII = (5, 5, 5, 5, 4, 2, 3)
OFFSETS = tuple(sum(RADII[:k]) for k in range(len(RADII)))
STRIP = 32
SENT = sum(RADII)
LANE_W = 5


def on_device(displacement, velocity, damage, history, toughness):
    rows, cols = damage.shape
    nx = lax.axis_size("gx")
    ny = lax.axis_size("gy")
    ix = lax.axis_index("gx")
    iy = lax.axis_index("gy")
    assert ny == 2 and rows % 8 == 0 and cols % BW == 0
    total_rows, total_cols = rows * nx, cols * ny
    nf = len(RADII)
    pos = jnp.stack([ix, iy]).astype(jnp.int32)
    nblocks = cols // BW
    per = BW // HC
    last_col_block = cols // HC - 1
    last_row_block = rows // 8 - 1
    f32 = damage.dtype
    rl = jnp_shift if INTERPRET else roll_shift

    def roll(x, s, axis):
        return rl(x, -s, axis)

    def split(refs):
        du, dv, dd, dh, dt = refs
        return [du[0], du[1], dv[0], dv[1], dd[...], dh[...], dt[...]]

    pw = cols

    def pack_kernel(tu, tv, td, th, tt, bu, bv, bd, bh, bt, after, top_o, bot_o):
        tops = split((tu, tv, td, th, tt))
        bots = split((bu, bv, bd, bh, bt))
        ridx = lax.broadcasted_iota(jnp.int32, (STRIP, pw), 0)
        top = jnp.zeros((STRIP, pw), f32)
        bot = jnp.zeros((STRIP, pw), f32)
        pad = jnp.zeros((STRIP - 8, pw), f32)
        for k in range(nf):
            r, o = RADII[k], OFFSETS[k]
            inside = (ridx >= o) & (ridx < o + r)
            x = roll(jnp.concatenate([tops[k], pad], axis=0), o, 0)
            top = jnp.where(inside, x, top)
            y = roll(jnp.concatenate([bots[k], pad], axis=0), o - (8 - r), 0)
            bot = jnp.where(inside, y, bot)
        top_o[...] = top[:SENT]
        bot_o[...] = bot[:SENT]


    def col_kernel(pos_ref, lu, lv, ld, lh, lt, ru, rv, rd, rh, rt, col_o):
        lefts = split((lu, lv, ld, lh, lt))
        rights = split((ru, rv, rd, rh, rt))
        lidx = lax.broadcasted_iota(jnp.int32, (rows, HC), 1)
        col = jnp.zeros((rows, HC), f32)
        to_right = pos_ref[1] == 0
        for k in range(nf):
            inside = (lidx >= LANE_W * k) & (lidx < LANE_W * (k + 1))
            a = roll(rights[k], LANE_W * k - (HC - LANE_W), 1)
            b = roll(lefts[k], LANE_W * k, 1)
            col = jnp.where(inside, jnp.where(to_right, a, b), col)
        col_o[...] = col

    t2 = pl.BlockSpec((2, 8, pw), lambda j: (0, 0, j))
    t1 = pl.BlockSpec((8, pw), lambda j: (0, j))
    b2 = pl.BlockSpec((2, 8, pw), lambda j: (0, last_row_block, j))
    b1 = pl.BlockSpec((8, pw), lambda j: (last_row_block, j))
    l2 = pl.BlockSpec((2, rows, HC), lambda j: (0, 0, 0))
    l1 = pl.BlockSpec((rows, HC), lambda j: (0, 0))
    r2 = pl.BlockSpec((2, rows, HC), lambda j: (0, 0, last_col_block))
    r1 = pl.BlockSpec((rows, HC), lambda j: (0, last_col_block))
    smem = pl.BlockSpec(memory_space=pltpu.SMEM)
    ins = (displacement, velocity, damage, history, toughness)
    col_s = pl.pallas_call(
        col_kernel,
        grid=(1,),
        in_specs=[smem, l2, l2, l1, l1, l1, r2, r2, r1, r1, r1],
        out_specs=pl.BlockSpec((rows, HC), lambda j: (0, 0)),
        out_shape=jax.ShapeDtypeStruct((rows, HC), f32),
        interpret=INTERPRET,
    )(pos, *ins, *ins)
    top_s, bot_s = pl.pallas_call(
        pack_kernel,
        grid=(cols // pw,),
        in_specs=[t2, t2, t1, t1, t1, b2, b2, b1, b1, b1, pl.BlockSpec((8, HC), lambda j: (0, 0))],
        out_specs=[pl.BlockSpec((SENT, pw), lambda j: (0, j)), pl.BlockSpec((SENT, pw), lambda j: (0, j))],
        out_shape=[jax.ShapeDtypeStruct((SENT, cols), f32), jax.ShapeDtypeStruct((SENT, cols), f32)],
        interpret=INTERPRET,
    )(*ins, *ins, col_s)

    side = lax.ppermute(col_s, "gy", [(0, 1), (1, 0)])
    both = ("gx", "gy")
    corner_above = lax.ppermute(col_s[rows - 8:], both,
                                [(i * 2 + g, (i + 1) * 2 + 1 - g) for i in range(nx - 1) for g in range(2)])
    corner_below = lax.ppermute(col_s[:8], both,
                                [((i + 1) * 2 + g, i * 2 + 1 - g) for i in range(nx - 1) for g in range(2)])
    side, corner_above, corner_below, top_s, bot_s = lax.optimization_barrier(
        (side, corner_above, corner_below, top_s, bot_s))
    above = lax.ppermute(bot_s, "gx", [(i, i + 1) for i in range(nx - 1)])
    below = lax.ppermute(top_s, "gx", [(i + 1, i) for i in range(nx - 1)])

    def kernel(pos_ref, um, ul, ur, vm, vl, vr, dm, dl, dr, hm, hl, hr, tm, tl, tr,
               am, al, ar, bm, bl, br, side_ref, ca_ref, cb_ref, uo, vo, ho, do):
        j = pl.program_id(0)
        first = j == 0
        last = j == nblocks - 1
        has_left = pos_ref[1] == 1
        has_right = pos_ref[1] == 0
        mains = split((um, vm, dm, hm, tm))
        lefts = split((ul, vl, dl, hl, tl))
        rights = split((ur, vr, dr, hr, tr))
        side_v = side_ref[...]
        ca = ca_ref[...]
        cb = cb_ref[...]

        def lane_left(x, k):
            lidx = lax.broadcasted_iota(jnp.int32, x.shape, 1)
            y = roll(x, HC - LANE_W - LANE_W * k, 1)
            return jnp.where((lidx >= HC - LANE_W) & has_left, y, 0.0)

        def lane_right(x, k):
            lidx = lax.broadcasted_iota(jnp.int32, x.shape, 1)
            y = roll(x, -LANE_W * k, 1)
            return jnp.where((lidx < LANE_W) & has_right, y, 0.0)

        def tile_of(ref, k, first_row):
            r, o = RADII[k], OFFSETS[k]
            s = min(max(o + first_row + r - 8 if first_row else o, 0), SENT - 8)
            y = ref[s:s + 8, :]
            shift = (first_row - (o - s)) % 8
            if shift:
                y = roll(y, shift, 0)
            ridx = lax.broadcasted_iota(jnp.int32, y.shape, 0)
            return jnp.where((ridx >= first_row) & (ridx < first_row + r), y, 0.0)

        def above_tile(ref, k):
            return tile_of(ref, k, 8 - RADII[k])

        def below_tile(ref, k):
            return tile_of(ref, k, 0)

        a_m, a_l, a_r = am, al, ar
        b_m, b_l, b_r = bm, bl, br

        def window(k):
            lft = jnp.where(first, lane_left(side_v, k), lefts[k])
            rgt = jnp.where(last, lane_right(side_v, k), rights[k])
            core = jnp.concatenate([lft, mains[k], rgt], axis=-1)
            top = jnp.concatenate([jnp.where(first, lane_left(ca, k), above_tile(a_l, k)),
                                   above_tile(a_m, k),
                                   jnp.where(last, lane_right(ca, k), above_tile(a_r, k))], axis=-1)
            bot = jnp.concatenate([jnp.where(first, lane_left(cb, k), below_tile(b_l, k)),
                                   below_tile(b_m, k),
                                   jnp.where(last, lane_right(cb, k), below_tile(b_r, k))], axis=-1)
            return jnp.concatenate([top, core, bot], axis=0)

        u0, u1, v0, v1, d, h, t = [window(k) for k in range(nf)]
        shape = d.shape
        grow = lax.broadcasted_iota(jnp.int32, (shape[0], 1), 0) + (pos_ref[0] * rows - HR)
        gcol = lax.broadcasted_iota(jnp.int32, (1, shape[1]), 1) + (pos_ref[1] * cols + j * BW - HC)
        valid = ((grow >= 0) & (grow < total_rows)) & ((gcol >= 0) & (gcol < total_cols))
        n0, n1, w0, w1, hn, d3 = step_fields(u0, u1, v0, v1, d, h, t, valid, rl)

        def core(x):
            return x[HR:HR + rows, HC:HC + BW]

        uo[0] = core(n0)
        uo[1] = core(n1)
        vo[0] = core(w0)
        vo[1] = core(w1)
        ho[...] = core(hn)
        do[...] = core(d3)

    def lcol(j):
        return jnp.maximum(j * per - 1, 0)

    def rcol(j):
        return jnp.minimum((j + 1) * per, last_col_block)

    main2 = pl.BlockSpec((2, rows, BW), lambda j: (0, 0, j))
    left2 = pl.BlockSpec((2, rows, HC), lambda j: (0, 0, lcol(j)))
    right2 = pl.BlockSpec((2, rows, HC), lambda j: (0, 0, rcol(j)))
    main1 = pl.BlockSpec((rows, BW), lambda j: (0, j))
    left1 = pl.BlockSpec((rows, HC), lambda j: (0, lcol(j)))
    right1 = pl.BlockSpec((rows, HC), lambda j: (0, rcol(j)))
    sm = pl.BlockSpec((SENT, BW), lambda j: (0, j))
    sl = pl.BlockSpec((SENT, HC), lambda j: (0, lcol(j)))
    sr = pl.BlockSpec((SENT, HC), lambda j: (0, rcol(j)))
    sidespec = pl.BlockSpec((rows, HC), lambda j: (0, 0))
    cornerspec = pl.BlockSpec((8, HC), lambda j: (0, 0))
    out2 = pl.BlockSpec((2, rows, BW), lambda j: (0, 0, j))
    out1 = pl.BlockSpec((rows, BW), lambda j: (0, j))
    outs = pl.pallas_call(
        kernel,
        grid=(nblocks,),
        in_specs=[smem, main2, left2, right2, main2, left2, right2,
                  main1, left1, right1, main1, left1, right1, main1, left1, right1,
                  sm, sl, sr, sm, sl, sr, sidespec, cornerspec, cornerspec],
        out_specs=[out2, out2, out1, out1],
        out_shape=[jax.ShapeDtypeStruct((2, rows, cols), f32), jax.ShapeDtypeStruct((2, rows, cols), f32),
                   jax.ShapeDtypeStruct((rows, cols), f32), jax.ShapeDtypeStruct((rows, cols), f32)],
        interpret=INTERPRET,
    )(pos, displacement, displacement, displacement, velocity, velocity, velocity,
      damage, damage, damage, history, history, history, toughness, toughness, toughness,
      above, above, above, below, below, below, side, corner_above, corner_below)
    return tuple(outs)


def solution(mesh):
    placed = (P(None, "gx", "gy"), P(None, "gx", "gy"), P("gx", "gy"), P("gx", "gy"), P("gx", "gy"))
    return jax.shard_map(
        on_device,
        mesh=mesh,
        in_specs=placed,
        out_specs=(P(None, "gx", "gy"), P(None, "gx", "gy"), P("gx", "gy"), P("gx", "gy")),
        check_vma=False,
    )
```

```python
import jax
import jax.numpy as jnp
from jax import lax
from jax.experimental import pallas as pl
from jax.experimental.pallas import tpu as pltpu
from jax.sharding import PartitionSpec as P

CHEB = 0.94
WEIGHT_TWO = 1.0 / (1.0 - CHEB * CHEB / 2.0)
WEIGHT_THREE = 1.0 / (1.0 - CHEB * CHEB * WEIGHT_TWO / 4.0)

HR = 8
HC = 128
BW = 2048
INTERPRET = False


def roll_shift(x, d, axis):
    return pltpu.roll(x, (-d) % x.shape[axis], axis)


def jnp_shift(x, d, axis):
    return jnp.roll(x, -d, axis)


def step_fields(u0, u1, v0, v1, dmg, hist, tough, valid, sh):
    zero = jnp.zeros_like(dmg)

    def strain(first, second):
        exx = (sh(first, 1, 0) - sh(first, -1, 0)) * 0.5
        eyy = (sh(second, 1, 1) - sh(second, -1, 1)) * 0.5
        exy = ((sh(first, 1, 1) - sh(first, -1, 1)) + (sh(second, 1, 0) - sh(second, -1, 0))) * 0.25
        return exx, eyy, exy

    degrade = (1.0 - dmg) ** 2 + 0.001
    degrade2 = degrade * 2.0

    def accel(exx, eyy, exy):
        trace = exx + eyy
        sxx = jnp.where(valid, degrade * (trace + 2.0 * exx), zero)
        syy = jnp.where(valid, degrade * (trace + 2.0 * eyy), zero)
        sxy = jnp.where(valid, degrade2 * exy, zero)
        a0 = ((sh(sxx, 1, 0) - sh(sxx, -1, 0)) + (sh(sxy, 1, 1) - sh(sxy, -1, 1))) * 0.5
        a1 = ((sh(sxy, 1, 0) - sh(sxy, -1, 0)) + (sh(syy, 1, 1) - sh(syy, -1, 1))) * 0.5
        return a0, a1

    a0, a1 = accel(*strain(u0 + 0.5 * v0, u1 + 0.5 * v1))
    h0 = jnp.where(valid, v0 + 0.1 * a0, zero)
    h1 = jnp.where(valid, v1 + 0.1 * a1, zero)
    n0 = jnp.where(valid, u0 + 0.2 * h0, zero)
    n1 = jnp.where(valid, u1 + 0.2 * h1, zero)
    e = strain(n0, n1)
    eh = strain(h0, h1)
    b0, b1 = accel(e[0] + 0.5 * eh[0], e[1] + 0.5 * eh[1], e[2] + 0.5 * eh[2])
    vel0 = h0 + 0.1 * b0
    vel1 = h1 + 0.1 * b1
    tr = jnp.maximum(e[0] + e[1], 0.0)
    hist_new = jnp.maximum(hist, 0.5 * tr * tr + e[0] * e[0] + e[1] * e[1] + 2.0 * e[2] * e[2])

    k_down = tough + sh(tough, 1, 0)
    k_up = tough + sh(tough, -1, 0)
    k_right = tough + sh(tough, 1, 1)
    k_left = tough + sh(tough, -1, 1)
    two_h = 2.0 * hist_new
    inv_denom = 1.0 / (tough * 0.5 + two_h + k_down + k_up + k_right + k_left)

    def jacobi(f):
        numer = two_h + k_down * sh(f, 1, 0) + k_up * sh(f, -1, 0)
        numer = numer + k_right * sh(f, 1, 1) + k_left * sh(f, -1, 1)
        return numer * inv_denom

    d1 = jnp.where(valid, jacobi(dmg), zero)
    d2 = jnp.where(valid, dmg + WEIGHT_TWO * (jacobi(d1) - dmg), zero)
    d3 = d1 + WEIGHT_THREE * (jacobi(d2) - d1)
    return n0, n1, vel0, vel1, hist_new, d3


RADII = (5, 5, 5, 5, 4, 2, 3)
OFFSETS = tuple(sum(RADII[:k]) for k in range(len(RADII)))
STRIP = 32
SENT = sum(RADII)
LANE_W = 5


def on_device(displacement, velocity, damage, history, toughness):
    rows, cols = damage.shape
    nx = lax.axis_size("gx")
    ny = lax.axis_size("gy")
    ix = lax.axis_index("gx")
    iy = lax.axis_index("gy")
    assert ny == 2 and rows % 8 == 0 and cols % BW == 0
    total_rows, total_cols = rows * nx, cols * ny
    nf = len(RADII)
    pos = jnp.stack([ix, iy]).astype(jnp.int32)
    nblocks = cols // BW
    per = BW // HC
    last_col_block = cols // HC - 1
    last_row_block = rows // 8 - 1
    f32 = damage.dtype
    rl = jnp_shift if INTERPRET else roll_shift

    def roll(x, s, axis):
        return rl(x, -s, axis)

    def split(refs):
        du, dv, dd, dh, dt = refs
        return [du[0], du[1], dv[0], dv[1], dd[...], dh[...], dt[...]]

    pw = cols

    def pack_kernel(tu, tv, td, th, tt, bu, bv, bd, bh, bt, top_o, bot_o):
        tops = split((tu, tv, td, th, tt))
        bots = split((bu, bv, bd, bh, bt))
        ridx = lax.broadcasted_iota(jnp.int32, (STRIP, pw), 0)
        top = jnp.zeros((STRIP, pw), f32)
        bot = jnp.zeros((STRIP, pw), f32)
        pad = jnp.zeros((STRIP - 8, pw), f32)
        for k in range(nf):
            r, o = RADII[k], OFFSETS[k]
            inside = (ridx >= o) & (ridx < o + r)
            x = roll(jnp.concatenate([tops[k], pad], axis=0), o, 0)
            top = jnp.where(inside, x, top)
            y = roll(jnp.concatenate([bots[k], pad], axis=0), o - (8 - r), 0)
            bot = jnp.where(inside, y, bot)
        top_o[...] = top[:SENT]
        bot_o[...] = bot[:SENT]


    def col_kernel(pos_ref, lu, lv, ld, lh, lt, ru, rv, rd, rh, rt, col_o):
        lefts = split((lu, lv, ld, lh, lt))
        rights = split((ru, rv, rd, rh, rt))
        lidx = lax.broadcasted_iota(jnp.int32, (rows, HC), 1)
        col = jnp.zeros((rows, HC), f32)
        to_right = pos_ref[1] == 0
        for k in range(nf):
            inside = (lidx >= LANE_W * k) & (lidx < LANE_W * (k + 1))
            a = roll(rights[k], LANE_W * k - (HC - LANE_W), 1)
            b = roll(lefts[k], LANE_W * k, 1)
            col = jnp.where(inside, jnp.where(to_right, a, b), col)
        col_o[...] = col

    t2 = pl.BlockSpec((2, 8, pw), lambda j: (0, 0, j))
    t1 = pl.BlockSpec((8, pw), lambda j: (0, j))
    b2 = pl.BlockSpec((2, 8, pw), lambda j: (0, last_row_block, j))
    b1 = pl.BlockSpec((8, pw), lambda j: (last_row_block, j))
    l2 = pl.BlockSpec((2, rows, HC), lambda j: (0, 0, 0))
    l1 = pl.BlockSpec((rows, HC), lambda j: (0, 0))
    r2 = pl.BlockSpec((2, rows, HC), lambda j: (0, 0, last_col_block))
    r1 = pl.BlockSpec((rows, HC), lambda j: (0, last_col_block))
    smem = pl.BlockSpec(memory_space=pltpu.SMEM)
    ins = (displacement, velocity, damage, history, toughness)
    top_s, bot_s = pl.pallas_call(
        pack_kernel,
        grid=(cols // pw,),
        in_specs=[t2, t2, t1, t1, t1, b2, b2, b1, b1, b1],
        out_specs=[pl.BlockSpec((SENT, pw), lambda j: (0, j)), pl.BlockSpec((SENT, pw), lambda j: (0, j))],
        out_shape=[jax.ShapeDtypeStruct((SENT, cols), f32), jax.ShapeDtypeStruct((SENT, cols), f32)],
        interpret=INTERPRET,
    )(*ins, *ins)
    col_s = pl.pallas_call(
        col_kernel,
        grid=(1,),
        in_specs=[smem, l2, l2, l1, l1, l1, r2, r2, r1, r1, r1],
        out_specs=pl.BlockSpec((rows, HC), lambda j: (0, 0)),
        out_shape=jax.ShapeDtypeStruct((rows, HC), f32),
        interpret=INTERPRET,
    )(pos, *ins, *ins)

    above = lax.ppermute(bot_s, "gx", [(i, i + 1) for i in range(nx - 1)])
    below = lax.ppermute(top_s, "gx", [(i + 1, i) for i in range(nx - 1)])
    side = lax.ppermute(col_s, "gy", [(0, 1), (1, 0)])
    both = ("gx", "gy")
    corner_above = lax.ppermute(col_s[rows - 8:], both,
                                [(i * 2 + g, (i + 1) * 2 + 1 - g) for i in range(nx - 1) for g in range(2)])
    corner_below = lax.ppermute(col_s[:8], both,
                                [((i + 1) * 2 + g, i * 2 + 1 - g) for i in range(nx - 1) for g in range(2)])

    def kernel(pos_ref, um, ul, ur, vm, vl, vr, dm, dl, dr, hm, hl, hr, tm, tl, tr,
               am, al, ar, bm, bl, br, side_ref, ca_ref, cb_ref, uo, vo, ho, do):
        j = pl.program_id(0)
        first = j == 0
        last = j == nblocks - 1
        has_left = pos_ref[1] == 1
        has_right = pos_ref[1] == 0
        mains = split((um, vm, dm, hm, tm))
        lefts = split((ul, vl, dl, hl, tl))
        rights = split((ur, vr, dr, hr, tr))
        side_v = side_ref[...]
        ca = ca_ref[...]
        cb = cb_ref[...]

        def lane_left(x, k):
            lidx = lax.broadcasted_iota(jnp.int32, x.shape, 1)
            y = roll(x, HC - LANE_W - LANE_W * k, 1)
            return jnp.where((lidx >= HC - LANE_W) & has_left, y, 0.0)

        def lane_right(x, k):
            lidx = lax.broadcasted_iota(jnp.int32, x.shape, 1)
            y = roll(x, -LANE_W * k, 1)
            return jnp.where((lidx < LANE_W) & has_right, y, 0.0)

        def tile_of(ref, k, first_row):
            r, o = RADII[k], OFFSETS[k]
            s = min(max(o + first_row + r - 8 if first_row else o, 0), SENT - 8)
            y = ref[s:s + 8, :]
            shift = (first_row - (o - s)) % 8
            if shift:
                y = roll(y, shift, 0)
            ridx = lax.broadcasted_iota(jnp.int32, y.shape, 0)
            return jnp.where((ridx >= first_row) & (ridx < first_row + r), y, 0.0)

        def above_tile(ref, k):
            return tile_of(ref, k, 8 - RADII[k])

        def below_tile(ref, k):
            return tile_of(ref, k, 0)

        a_m, a_l, a_r = am, al, ar
        b_m, b_l, b_r = bm, bl, br

        def window(k):
            lft = jnp.where(first, lane_left(side_v, k), lefts[k])
            rgt = jnp.where(last, lane_right(side_v, k), rights[k])
            core = jnp.concatenate([lft, mains[k], rgt], axis=-1)
            top = jnp.concatenate([jnp.where(first, lane_left(ca, k), above_tile(a_l, k)),
                                   above_tile(a_m, k),
                                   jnp.where(last, lane_right(ca, k), above_tile(a_r, k))], axis=-1)
            bot = jnp.concatenate([jnp.where(first, lane_left(cb, k), below_tile(b_l, k)),
                                   below_tile(b_m, k),
                                   jnp.where(last, lane_right(cb, k), below_tile(b_r, k))], axis=-1)
            return jnp.concatenate([top, core, bot], axis=0)

        u0, u1, v0, v1, d, h, t = [window(k) for k in range(nf)]
        shape = d.shape
        grow = lax.broadcasted_iota(jnp.int32, (shape[0], 1), 0) + (pos_ref[0] * rows - HR)
        gcol = lax.broadcasted_iota(jnp.int32, (1, shape[1]), 1) + (pos_ref[1] * cols + j * BW - HC)
        valid = ((grow >= 0) & (grow < total_rows)) & ((gcol >= 0) & (gcol < total_cols))
        n0, n1, w0, w1, hn, d3 = step_fields(u0, u1, v0, v1, d, h, t, valid, rl)

        def core(x):
            return x[HR:HR + rows, HC:HC + BW]

        uo[0] = core(n0)
        uo[1] = core(n1)
        vo[0] = core(w0)
        vo[1] = core(w1)
        ho[...] = core(hn)
        do[...] = core(d3)

    def lcol(j):
        return jnp.maximum(j * per - 1, 0)

    def rcol(j):
        return jnp.minimum((j + 1) * per, last_col_block)

    main2 = pl.BlockSpec((2, rows, BW), lambda j: (0, 0, j))
    left2 = pl.BlockSpec((2, rows, HC), lambda j: (0, 0, lcol(j)))
    right2 = pl.BlockSpec((2, rows, HC), lambda j: (0, 0, rcol(j)))
    main1 = pl.BlockSpec((rows, BW), lambda j: (0, j))
    left1 = pl.BlockSpec((rows, HC), lambda j: (0, lcol(j)))
    right1 = pl.BlockSpec((rows, HC), lambda j: (0, rcol(j)))
    sm = pl.BlockSpec((SENT, BW), lambda j: (0, j))
    sl = pl.BlockSpec((SENT, HC), lambda j: (0, lcol(j)))
    sr = pl.BlockSpec((SENT, HC), lambda j: (0, rcol(j)))
    sidespec = pl.BlockSpec((rows, HC), lambda j: (0, 0))
    cornerspec = pl.BlockSpec((8, HC), lambda j: (0, 0))
    out2 = pl.BlockSpec((2, rows, BW), lambda j: (0, 0, j))
    out1 = pl.BlockSpec((rows, BW), lambda j: (0, j))
    outs = pl.pallas_call(
        kernel,
        grid=(nblocks,),
        in_specs=[smem, main2, left2, right2, main2, left2, right2,
                  main1, left1, right1, main1, left1, right1, main1, left1, right1,
                  sm, sl, sr, sm, sl, sr, sidespec, cornerspec, cornerspec],
        out_specs=[out2, out2, out1, out1],
        out_shape=[jax.ShapeDtypeStruct((2, rows, cols), f32), jax.ShapeDtypeStruct((2, rows, cols), f32),
                   jax.ShapeDtypeStruct((rows, cols), f32), jax.ShapeDtypeStruct((rows, cols), f32)],
        interpret=INTERPRET,
    )(pos, displacement, displacement, displacement, velocity, velocity, velocity,
      damage, damage, damage, history, history, history, toughness, toughness, toughness,
      above, above, above, below, below, below, side, corner_above, corner_below)
    return tuple(outs)


def solution(mesh):
    placed = (P(None, "gx", "gy"), P(None, "gx", "gy"), P("gx", "gy"), P("gx", "gy"), P("gx", "gy"))
    return jax.shard_map(
        on_device,
        mesh=mesh,
        in_specs=placed,
        out_specs=(P(None, "gx", "gy"), P(None, "gx", "gy"), P("gx", "gy"), P("gx", "gy")),
        check_vma=False,
    )
```

```python
import functools

import jax
import jax.numpy as jnp
from jax import lax
from jax.experimental import pallas as pl
from jax.experimental.pallas import tpu as pltpu
from jax.sharding import PartitionSpec as P

CHEB = 0.94
WEIGHT_TWO = 1.0 / (1.0 - CHEB * CHEB / 2.0)
WEIGHT_THREE = 1.0 / (1.0 - CHEB * CHEB * WEIGHT_TWO / 4.0)

HR = 8
HC = 128
BW = 2048
INTERPRET = False


def roll_shift(x, d, axis):
    return pltpu.roll(x, (-d) % x.shape[axis], axis)


def jnp_shift(x, d, axis):
    return jnp.roll(x, -d, axis)


def step_fields(u0, u1, v0, v1, dmg, hist, tough, valid, sh):
    zero = jnp.zeros_like(dmg)

    def strain(first, second):
        exx = (sh(first, 1, 0) - sh(first, -1, 0)) * 0.5
        eyy = (sh(second, 1, 1) - sh(second, -1, 1)) * 0.5
        exy = ((sh(first, 1, 1) - sh(first, -1, 1)) + (sh(second, 1, 0) - sh(second, -1, 0))) * 0.25
        return exx, eyy, exy

    degrade = (1.0 - dmg) ** 2 + 0.001
    degrade2 = degrade * 2.0

    def accel(exx, eyy, exy):
        trace = exx + eyy
        sxx = jnp.where(valid, degrade * (trace + 2.0 * exx), zero)
        syy = jnp.where(valid, degrade * (trace + 2.0 * eyy), zero)
        sxy = jnp.where(valid, degrade2 * exy, zero)
        a0 = ((sh(sxx, 1, 0) - sh(sxx, -1, 0)) + (sh(sxy, 1, 1) - sh(sxy, -1, 1))) * 0.5
        a1 = ((sh(sxy, 1, 0) - sh(sxy, -1, 0)) + (sh(syy, 1, 1) - sh(syy, -1, 1))) * 0.5
        return a0, a1

    a0, a1 = accel(*strain(u0 + 0.5 * v0, u1 + 0.5 * v1))
    h0 = jnp.where(valid, v0 + 0.1 * a0, zero)
    h1 = jnp.where(valid, v1 + 0.1 * a1, zero)
    n0 = jnp.where(valid, u0 + 0.2 * h0, zero)
    n1 = jnp.where(valid, u1 + 0.2 * h1, zero)
    e = strain(n0, n1)
    eh = strain(h0, h1)
    b0, b1 = accel(e[0] + 0.5 * eh[0], e[1] + 0.5 * eh[1], e[2] + 0.5 * eh[2])
    vel0 = h0 + 0.1 * b0
    vel1 = h1 + 0.1 * b1
    tr = jnp.maximum(e[0] + e[1], 0.0)
    hist_new = jnp.maximum(hist, 0.5 * tr * tr + e[0] * e[0] + e[1] * e[1] + 2.0 * e[2] * e[2])

    k_down = tough + sh(tough, 1, 0)
    k_up = tough + sh(tough, -1, 0)
    k_right = tough + sh(tough, 1, 1)
    k_left = tough + sh(tough, -1, 1)
    two_h = 2.0 * hist_new
    inv_denom = 1.0 / (tough * 0.5 + two_h + k_down + k_up + k_right + k_left)

    def jacobi(f):
        numer = two_h + k_down * sh(f, 1, 0) + k_up * sh(f, -1, 0)
        numer = numer + k_right * sh(f, 1, 1) + k_left * sh(f, -1, 1)
        return numer * inv_denom

    d1 = jnp.where(valid, jacobi(dmg), zero)
    d2 = jnp.where(valid, dmg + WEIGHT_TWO * (jacobi(d1) - dmg), zero)
    d3 = d1 + WEIGHT_THREE * (jacobi(d2) - d1)
    return n0, n1, vel0, vel1, hist_new, d3


RADII = (5, 5, 5, 5, 4, 2, 3)
OFFSETS = tuple(sum(RADII[:k]) for k in range(len(RADII)))
STRIP = 32
SENT = sum(RADII)
LANE_W = 5


def on_device(displacement, velocity, damage, history, toughness):
    rows, cols = damage.shape
    nx = lax.axis_size("gx")
    ny = lax.axis_size("gy")
    ix = lax.axis_index("gx")
    iy = lax.axis_index("gy")
    assert ny == 2 and rows % 8 == 0 and cols % BW == 0
    total_rows, total_cols = rows * nx, cols * ny
    nf = len(RADII)
    pos = jnp.stack([ix, iy]).astype(jnp.int32)
    nblocks = cols // BW
    per = BW // HC
    last_col_block = cols // HC - 1
    last_row_block = rows // 8 - 1
    f32 = damage.dtype
    rl = jnp_shift if INTERPRET else roll_shift

    def roll(x, s, axis):
        return rl(x, -s, axis)

    def split(refs):
        du, dv, dd, dh, dt = refs
        return [du[0], du[1], dv[0], dv[1], dd[...], dh[...], dt[...]]

    pw = cols

    def strip_kernel(first_row_of, u_ref, v_ref, d_ref, h_ref, t_ref, out_o):
        tiles = split((u_ref, v_ref, d_ref, h_ref, t_ref))
        ridx = lax.broadcasted_iota(jnp.int32, (STRIP, pw), 0)
        acc = jnp.zeros((STRIP, pw), f32)
        pad = jnp.zeros((STRIP - 8, pw), f32)
        for k in range(nf):
            r, o = RADII[k], OFFSETS[k]
            inside = (ridx >= o) & (ridx < o + r)
            x = roll(jnp.concatenate([tiles[k], pad], axis=0), o - first_row_of(r), 0)
            acc = jnp.where(inside, x, acc)
        out_o[...] = acc[:SENT]


    def col_kernel(pos_ref, lu, lv, ld, lh, lt, ru, rv, rd, rh, rt, col_o):
        lefts = split((lu, lv, ld, lh, lt))
        rights = split((ru, rv, rd, rh, rt))
        lidx = lax.broadcasted_iota(jnp.int32, (rows, HC), 1)
        col = jnp.zeros((rows, HC), f32)
        to_right = pos_ref[1] == 0
        for k in range(nf):
            inside = (lidx >= LANE_W * k) & (lidx < LANE_W * (k + 1))
            a = roll(rights[k], LANE_W * k - (HC - LANE_W), 1)
            b = roll(lefts[k], LANE_W * k, 1)
            col = jnp.where(inside, jnp.where(to_right, a, b), col)
        col_o[...] = col

    t2 = pl.BlockSpec((2, 8, pw), lambda j: (0, 0, j))
    t1 = pl.BlockSpec((8, pw), lambda j: (0, j))
    b2 = pl.BlockSpec((2, 8, pw), lambda j: (0, last_row_block, j))
    b1 = pl.BlockSpec((8, pw), lambda j: (last_row_block, j))
    l2 = pl.BlockSpec((2, rows, HC), lambda j: (0, 0, 0))
    l1 = pl.BlockSpec((rows, HC), lambda j: (0, 0))
    r2 = pl.BlockSpec((2, rows, HC), lambda j: (0, 0, last_col_block))
    r1 = pl.BlockSpec((rows, HC), lambda j: (0, last_col_block))
    smem = pl.BlockSpec(memory_space=pltpu.SMEM)
    ins = (displacement, velocity, damage, history, toughness)
    def strip(first_row_of, s2, s1):
        return pl.pallas_call(
            functools.partial(strip_kernel, first_row_of),
            grid=(cols // pw,),
            in_specs=[s2, s2, s1, s1, s1],
            out_specs=pl.BlockSpec((SENT, pw), lambda j: (0, j)),
            out_shape=jax.ShapeDtypeStruct((SENT, cols), f32),
            interpret=INTERPRET,
        )(*ins)

    bot_s = strip(lambda r: 8 - r, b2, b1)
    top_s = strip(lambda r: 0, t2, t1)
    col_s = pl.pallas_call(
        col_kernel,
        grid=(1,),
        in_specs=[smem, l2, l2, l1, l1, l1, r2, r2, r1, r1, r1],
        out_specs=pl.BlockSpec((rows, HC), lambda j: (0, 0)),
        out_shape=jax.ShapeDtypeStruct((rows, HC), f32),
        interpret=INTERPRET,
    )(pos, *ins, *ins)

    above = lax.ppermute(bot_s, "gx", [(i, i + 1) for i in range(nx - 1)])
    below = lax.ppermute(top_s, "gx", [(i + 1, i) for i in range(nx - 1)])
    side = lax.ppermute(col_s, "gy", [(0, 1), (1, 0)])
    both = ("gx", "gy")
    corner_above = lax.ppermute(col_s[rows - 8:], both,
                                [(i * 2 + g, (i + 1) * 2 + 1 - g) for i in range(nx - 1) for g in range(2)])
    corner_below = lax.ppermute(col_s[:8], both,
                                [((i + 1) * 2 + g, i * 2 + 1 - g) for i in range(nx - 1) for g in range(2)])

    def kernel(pos_ref, um, ul, ur, vm, vl, vr, dm, dl, dr, hm, hl, hr, tm, tl, tr,
               am, al, ar, bm, bl, br, side_ref, ca_ref, cb_ref, uo, vo, ho, do):
        j = pl.program_id(0)
        first = j == 0
        last = j == nblocks - 1
        has_left = pos_ref[1] == 1
        has_right = pos_ref[1] == 0
        mains = split((um, vm, dm, hm, tm))
        lefts = split((ul, vl, dl, hl, tl))
        rights = split((ur, vr, dr, hr, tr))
        side_v = side_ref[...]
        ca = ca_ref[...]
        cb = cb_ref[...]

        def lane_left(x, k):
            lidx = lax.broadcasted_iota(jnp.int32, x.shape, 1)
            y = roll(x, HC - LANE_W - LANE_W * k, 1)
            return jnp.where((lidx >= HC - LANE_W) & has_left, y, 0.0)

        def lane_right(x, k):
            lidx = lax.broadcasted_iota(jnp.int32, x.shape, 1)
            y = roll(x, -LANE_W * k, 1)
            return jnp.where((lidx < LANE_W) & has_right, y, 0.0)

        def tile_of(ref, k, first_row):
            r, o = RADII[k], OFFSETS[k]
            s = min(max(o + first_row + r - 8 if first_row else o, 0), SENT - 8)
            y = ref[s:s + 8, :]
            shift = (first_row - (o - s)) % 8
            if shift:
                y = roll(y, shift, 0)
            ridx = lax.broadcasted_iota(jnp.int32, y.shape, 0)
            return jnp.where((ridx >= first_row) & (ridx < first_row + r), y, 0.0)

        def above_tile(ref, k):
            return tile_of(ref, k, 8 - RADII[k])

        def below_tile(ref, k):
            return tile_of(ref, k, 0)

        a_m, a_l, a_r = am, al, ar
        b_m, b_l, b_r = bm, bl, br

        def window(k):
            lft = jnp.where(first, lane_left(side_v, k), lefts[k])
            rgt = jnp.where(last, lane_right(side_v, k), rights[k])
            core = jnp.concatenate([lft, mains[k], rgt], axis=-1)
            top = jnp.concatenate([jnp.where(first, lane_left(ca, k), above_tile(a_l, k)),
                                   above_tile(a_m, k),
                                   jnp.where(last, lane_right(ca, k), above_tile(a_r, k))], axis=-1)
            bot = jnp.concatenate([jnp.where(first, lane_left(cb, k), below_tile(b_l, k)),
                                   below_tile(b_m, k),
                                   jnp.where(last, lane_right(cb, k), below_tile(b_r, k))], axis=-1)
            return jnp.concatenate([top, core, bot], axis=0)

        u0, u1, v0, v1, d, h, t = [window(k) for k in range(nf)]
        shape = d.shape
        grow = lax.broadcasted_iota(jnp.int32, (shape[0], 1), 0) + (pos_ref[0] * rows - HR)
        gcol = lax.broadcasted_iota(jnp.int32, (1, shape[1]), 1) + (pos_ref[1] * cols + j * BW - HC)
        valid = ((grow >= 0) & (grow < total_rows)) & ((gcol >= 0) & (gcol < total_cols))
        n0, n1, w0, w1, hn, d3 = step_fields(u0, u1, v0, v1, d, h, t, valid, rl)

        def core(x):
            return x[HR:HR + rows, HC:HC + BW]

        uo[0] = core(n0)
        uo[1] = core(n1)
        vo[0] = core(w0)
        vo[1] = core(w1)
        ho[...] = core(hn)
        do[...] = core(d3)

    def lcol(j):
        return jnp.maximum(j * per - 1, 0)

    def rcol(j):
        return jnp.minimum((j + 1) * per, last_col_block)

    main2 = pl.BlockSpec((2, rows, BW), lambda j: (0, 0, j))
    left2 = pl.BlockSpec((2, rows, HC), lambda j: (0, 0, lcol(j)))
    right2 = pl.BlockSpec((2, rows, HC), lambda j: (0, 0, rcol(j)))
    main1 = pl.BlockSpec((rows, BW), lambda j: (0, j))
    left1 = pl.BlockSpec((rows, HC), lambda j: (0, lcol(j)))
    right1 = pl.BlockSpec((rows, HC), lambda j: (0, rcol(j)))
    sm = pl.BlockSpec((SENT, BW), lambda j: (0, j))
    sl = pl.BlockSpec((SENT, HC), lambda j: (0, lcol(j)))
    sr = pl.BlockSpec((SENT, HC), lambda j: (0, rcol(j)))
    sidespec = pl.BlockSpec((rows, HC), lambda j: (0, 0))
    cornerspec = pl.BlockSpec((8, HC), lambda j: (0, 0))
    out2 = pl.BlockSpec((2, rows, BW), lambda j: (0, 0, j))
    out1 = pl.BlockSpec((rows, BW), lambda j: (0, j))
    outs = pl.pallas_call(
        kernel,
        grid=(nblocks,),
        in_specs=[smem, main2, left2, right2, main2, left2, right2,
                  main1, left1, right1, main1, left1, right1, main1, left1, right1,
                  sm, sl, sr, sm, sl, sr, sidespec, cornerspec, cornerspec],
        out_specs=[out2, out2, out1, out1],
        out_shape=[jax.ShapeDtypeStruct((2, rows, cols), f32), jax.ShapeDtypeStruct((2, rows, cols), f32),
                   jax.ShapeDtypeStruct((rows, cols), f32), jax.ShapeDtypeStruct((rows, cols), f32)],
        interpret=INTERPRET,
    )(pos, displacement, displacement, displacement, velocity, velocity, velocity,
      damage, damage, damage, history, history, history, toughness, toughness, toughness,
      above, above, above, below, below, below, side, corner_above, corner_below)
    return tuple(outs)


def solution(mesh):
    placed = (P(None, "gx", "gy"), P(None, "gx", "gy"), P("gx", "gy"), P("gx", "gy"), P("gx", "gy"))
    return jax.shard_map(
        on_device,
        mesh=mesh,
        in_specs=placed,
        out_specs=(P(None, "gx", "gy"), P(None, "gx", "gy"), P("gx", "gy"), P("gx", "gy")),
        check_vma=False,
    )
```

```python
import functools

import jax
import jax.numpy as jnp
from jax import lax
from jax.experimental import pallas as pl
from jax.experimental.pallas import tpu as pltpu
from jax.sharding import PartitionSpec as P

CHEB = 0.94
WEIGHT_TWO = 1.0 / (1.0 - CHEB * CHEB / 2.0)
WEIGHT_THREE = 1.0 / (1.0 - CHEB * CHEB * WEIGHT_TWO / 4.0)

HR = 8
HC = 128
BW = 2048
INTERPRET = False


def roll_shift(x, d, axis):
    return pltpu.roll(x, (-d) % x.shape[axis], axis)


def jnp_shift(x, d, axis):
    return jnp.roll(x, -d, axis)


def step_fields(u0, u1, v0, v1, dmg, hist, tough, valid, sh):
    zero = jnp.zeros_like(dmg)

    def strain(first, second):
        exx = (sh(first, 1, 0) - sh(first, -1, 0)) * 0.5
        eyy = (sh(second, 1, 1) - sh(second, -1, 1)) * 0.5
        exy = ((sh(first, 1, 1) - sh(first, -1, 1)) + (sh(second, 1, 0) - sh(second, -1, 0))) * 0.25
        return exx, eyy, exy

    degrade = (1.0 - dmg) ** 2 + 0.001
    degrade2 = degrade * 2.0

    def accel(exx, eyy, exy):
        trace = exx + eyy
        sxx = jnp.where(valid, degrade * (trace + 2.0 * exx), zero)
        syy = jnp.where(valid, degrade * (trace + 2.0 * eyy), zero)
        sxy = jnp.where(valid, degrade2 * exy, zero)
        a0 = ((sh(sxx, 1, 0) - sh(sxx, -1, 0)) + (sh(sxy, 1, 1) - sh(sxy, -1, 1))) * 0.5
        a1 = ((sh(sxy, 1, 0) - sh(sxy, -1, 0)) + (sh(syy, 1, 1) - sh(syy, -1, 1))) * 0.5
        return a0, a1

    a0, a1 = accel(*strain(u0 + 0.5 * v0, u1 + 0.5 * v1))
    h0 = jnp.where(valid, v0 + 0.1 * a0, zero)
    h1 = jnp.where(valid, v1 + 0.1 * a1, zero)
    n0 = jnp.where(valid, u0 + 0.2 * h0, zero)
    n1 = jnp.where(valid, u1 + 0.2 * h1, zero)
    e = strain(n0, n1)
    eh = strain(h0, h1)
    b0, b1 = accel(e[0] + 0.5 * eh[0], e[1] + 0.5 * eh[1], e[2] + 0.5 * eh[2])
    vel0 = h0 + 0.1 * b0
    vel1 = h1 + 0.1 * b1
    tr = jnp.maximum(e[0] + e[1], 0.0)
    hist_new = jnp.maximum(hist, 0.5 * tr * tr + e[0] * e[0] + e[1] * e[1] + 2.0 * e[2] * e[2])

    k_down = tough + sh(tough, 1, 0)
    k_up = tough + sh(tough, -1, 0)
    k_right = tough + sh(tough, 1, 1)
    k_left = tough + sh(tough, -1, 1)
    two_h = 2.0 * hist_new
    inv_denom = 1.0 / (tough * 0.5 + two_h + k_down + k_up + k_right + k_left)

    def jacobi(f):
        numer = two_h + k_down * sh(f, 1, 0) + k_up * sh(f, -1, 0)
        numer = numer + k_right * sh(f, 1, 1) + k_left * sh(f, -1, 1)
        return numer * inv_denom

    d1 = jnp.where(valid, jacobi(dmg), zero)
    d2 = jnp.where(valid, dmg + WEIGHT_TWO * (jacobi(d1) - dmg), zero)
    d3 = d1 + WEIGHT_THREE * (jacobi(d2) - d1)
    return n0, n1, vel0, vel1, hist_new, d3


RADII = (5, 5, 5, 5, 4, 2, 3)
OFFSETS = tuple(sum(RADII[:k]) for k in range(len(RADII)))
STRIP = 32
SENT = sum(RADII)
LANE_W = 5


def on_device(displacement, velocity, damage, history, toughness):
    rows, cols = damage.shape
    nx = lax.axis_size("gx")
    ny = lax.axis_size("gy")
    ix = lax.axis_index("gx")
    iy = lax.axis_index("gy")
    assert ny == 2 and rows % 8 == 0 and cols % BW == 0
    total_rows, total_cols = rows * nx, cols * ny
    nf = len(RADII)
    pos = jnp.stack([ix, iy]).astype(jnp.int32)
    nblocks = cols // BW
    per = BW // HC
    last_col_block = cols // HC - 1
    last_row_block = rows // 8 - 1
    f32 = damage.dtype
    rl = jnp_shift if INTERPRET else roll_shift

    def roll(x, s, axis):
        return rl(x, -s, axis)

    def split(refs):
        du, dv, dd, dh, dt = refs
        return [du[0], du[1], dv[0], dv[1], dd[...], dh[...], dt[...]]

    pw = cols // 2

    def strip_kernel(first_row_of, u_ref, v_ref, d_ref, h_ref, t_ref, out_o):
        tiles = split((u_ref, v_ref, d_ref, h_ref, t_ref))
        ridx = lax.broadcasted_iota(jnp.int32, (STRIP, pw), 0)
        acc = jnp.zeros((STRIP, pw), f32)
        pad = jnp.zeros((STRIP - 8, pw), f32)
        for k in range(nf):
            r, o = RADII[k], OFFSETS[k]
            inside = (ridx >= o) & (ridx < o + r)
            x = roll(jnp.concatenate([tiles[k], pad], axis=0), o - first_row_of(r), 0)
            acc = jnp.where(inside, x, acc)
        out_o[...] = acc[:SENT]


    def col_kernel(pos_ref, lu, lv, ld, lh, lt, ru, rv, rd, rh, rt, col_o):
        lefts = split((lu, lv, ld, lh, lt))
        rights = split((ru, rv, rd, rh, rt))
        lidx = lax.broadcasted_iota(jnp.int32, (rows, HC), 1)
        col = jnp.zeros((rows, HC), f32)
        to_right = pos_ref[1] == 0
        for k in range(nf):
            inside = (lidx >= LANE_W * k) & (lidx < LANE_W * (k + 1))
            a = roll(rights[k], LANE_W * k - (HC - LANE_W), 1)
            b = roll(lefts[k], LANE_W * k, 1)
            col = jnp.where(inside, jnp.where(to_right, a, b), col)
        col_o[...] = col

    t2 = pl.BlockSpec((2, 8, pw), lambda j: (0, 0, j))
    t1 = pl.BlockSpec((8, pw), lambda j: (0, j))
    b2 = pl.BlockSpec((2, 8, pw), lambda j: (0, last_row_block, j))
    b1 = pl.BlockSpec((8, pw), lambda j: (last_row_block, j))
    l2 = pl.BlockSpec((2, rows, HC), lambda j: (0, 0, 0))
    l1 = pl.BlockSpec((rows, HC), lambda j: (0, 0))
    r2 = pl.BlockSpec((2, rows, HC), lambda j: (0, 0, last_col_block))
    r1 = pl.BlockSpec((rows, HC), lambda j: (0, last_col_block))
    smem = pl.BlockSpec(memory_space=pltpu.SMEM)
    ins = (displacement, velocity, damage, history, toughness)
    def strip(first_row_of, s2, s1):
        return pl.pallas_call(
            functools.partial(strip_kernel, first_row_of),
            grid=(cols // pw,),
            in_specs=[s2, s2, s1, s1, s1],
            out_specs=pl.BlockSpec((SENT, pw), lambda j: (0, j)),
            out_shape=jax.ShapeDtypeStruct((SENT, cols), f32),
            interpret=INTERPRET,
        )(*ins)

    bot_s = strip(lambda r: 8 - r, b2, b1)
    top_s = strip(lambda r: 0, t2, t1)
    col_s = pl.pallas_call(
        col_kernel,
        grid=(1,),
        in_specs=[smem, l2, l2, l1, l1, l1, r2, r2, r1, r1, r1],
        out_specs=pl.BlockSpec((rows, HC), lambda j: (0, 0)),
        out_shape=jax.ShapeDtypeStruct((rows, HC), f32),
        interpret=INTERPRET,
    )(pos, *ins, *ins)

    above = lax.ppermute(bot_s, "gx", [(i, i + 1) for i in range(nx - 1)])
    below = lax.ppermute(top_s, "gx", [(i + 1, i) for i in range(nx - 1)])
    side = lax.ppermute(col_s, "gy", [(0, 1), (1, 0)])
    both = ("gx", "gy")
    corner_above = lax.ppermute(col_s[rows - 8:], both,
                                [(i * 2 + g, (i + 1) * 2 + 1 - g) for i in range(nx - 1) for g in range(2)])
    corner_below = lax.ppermute(col_s[:8], both,
                                [((i + 1) * 2 + g, i * 2 + 1 - g) for i in range(nx - 1) for g in range(2)])

    def kernel(pos_ref, um, ul, ur, vm, vl, vr, dm, dl, dr, hm, hl, hr, tm, tl, tr,
               am, al, ar, bm, bl, br, side_ref, ca_ref, cb_ref, uo, vo, ho, do):
        j = pl.program_id(0)
        first = j == 0
        last = j == nblocks - 1
        has_left = pos_ref[1] == 1
        has_right = pos_ref[1] == 0
        mains = split((um, vm, dm, hm, tm))
        lefts = split((ul, vl, dl, hl, tl))
        rights = split((ur, vr, dr, hr, tr))
        side_v = side_ref[...]
        ca = ca_ref[...]
        cb = cb_ref[...]

        def lane_left(x, k):
            lidx = lax.broadcasted_iota(jnp.int32, x.shape, 1)
            y = roll(x, HC - LANE_W - LANE_W * k, 1)
            return jnp.where((lidx >= HC - LANE_W) & has_left, y, 0.0)

        def lane_right(x, k):
            lidx = lax.broadcasted_iota(jnp.int32, x.shape, 1)
            y = roll(x, -LANE_W * k, 1)
            return jnp.where((lidx < LANE_W) & has_right, y, 0.0)

        def tile_of(ref, k, first_row):
            r, o = RADII[k], OFFSETS[k]
            s = min(max(o + first_row + r - 8 if first_row else o, 0), SENT - 8)
            y = ref[s:s + 8, :]
            shift = (first_row - (o - s)) % 8
            if shift:
                y = roll(y, shift, 0)
            ridx = lax.broadcasted_iota(jnp.int32, y.shape, 0)
            return jnp.where((ridx >= first_row) & (ridx < first_row + r), y, 0.0)

        def above_tile(ref, k):
            return tile_of(ref, k, 8 - RADII[k])

        def below_tile(ref, k):
            return tile_of(ref, k, 0)

        a_m, a_l, a_r = am, al, ar
        b_m, b_l, b_r = bm, bl, br

        def window(k):
            lft = jnp.where(first, lane_left(side_v, k), lefts[k])
            rgt = jnp.where(last, lane_right(side_v, k), rights[k])
            core = jnp.concatenate([lft, mains[k], rgt], axis=-1)
            top = jnp.concatenate([jnp.where(first, lane_left(ca, k), above_tile(a_l, k)),
                                   above_tile(a_m, k),
                                   jnp.where(last, lane_right(ca, k), above_tile(a_r, k))], axis=-1)
            bot = jnp.concatenate([jnp.where(first, lane_left(cb, k), below_tile(b_l, k)),
                                   below_tile(b_m, k),
                                   jnp.where(last, lane_right(cb, k), below_tile(b_r, k))], axis=-1)
            return jnp.concatenate([top, core, bot], axis=0)

        u0, u1, v0, v1, d, h, t = [window(k) for k in range(nf)]
        shape = d.shape
        grow = lax.broadcasted_iota(jnp.int32, (shape[0], 1), 0) + (pos_ref[0] * rows - HR)
        gcol = lax.broadcasted_iota(jnp.int32, (1, shape[1]), 1) + (pos_ref[1] * cols + j * BW - HC)
        valid = ((grow >= 0) & (grow < total_rows)) & ((gcol >= 0) & (gcol < total_cols))
        n0, n1, w0, w1, hn, d3 = step_fields(u0, u1, v0, v1, d, h, t, valid, rl)

        def core(x):
            return x[HR:HR + rows, HC:HC + BW]

        uo[0] = core(n0)
        uo[1] = core(n1)
        vo[0] = core(w0)
        vo[1] = core(w1)
        ho[...] = core(hn)
        do[...] = core(d3)

    def lcol(j):
        return jnp.maximum(j * per - 1, 0)

    def rcol(j):
        return jnp.minimum((j + 1) * per, last_col_block)

    main2 = pl.BlockSpec((2, rows, BW), lambda j: (0, 0, j))
    left2 = pl.BlockSpec((2, rows, HC), lambda j: (0, 0, lcol(j)))
    right2 = pl.BlockSpec((2, rows, HC), lambda j: (0, 0, rcol(j)))
    main1 = pl.BlockSpec((rows, BW), lambda j: (0, j))
    left1 = pl.BlockSpec((rows, HC), lambda j: (0, lcol(j)))
    right1 = pl.BlockSpec((rows, HC), lambda j: (0, rcol(j)))
    sm = pl.BlockSpec((SENT, BW), lambda j: (0, j))
    sl = pl.BlockSpec((SENT, HC), lambda j: (0, lcol(j)))
    sr = pl.BlockSpec((SENT, HC), lambda j: (0, rcol(j)))
    sidespec = pl.BlockSpec((rows, HC), lambda j: (0, 0))
    cornerspec = pl.BlockSpec((8, HC), lambda j: (0, 0))
    out2 = pl.BlockSpec((2, rows, BW), lambda j: (0, 0, j))
    out1 = pl.BlockSpec((rows, BW), lambda j: (0, j))
    outs = pl.pallas_call(
        kernel,
        grid=(nblocks,),
        in_specs=[smem, main2, left2, right2, main2, left2, right2,
                  main1, left1, right1, main1, left1, right1, main1, left1, right1,
                  sm, sl, sr, sm, sl, sr, sidespec, cornerspec, cornerspec],
        out_specs=[out2, out2, out1, out1],
        out_shape=[jax.ShapeDtypeStruct((2, rows, cols), f32), jax.ShapeDtypeStruct((2, rows, cols), f32),
                   jax.ShapeDtypeStruct((rows, cols), f32), jax.ShapeDtypeStruct((rows, cols), f32)],
        interpret=INTERPRET,
    )(pos, displacement, displacement, displacement, velocity, velocity, velocity,
      damage, damage, damage, history, history, history, toughness, toughness, toughness,
      above, above, above, below, below, below, side, corner_above, corner_below)
    return tuple(outs)


def solution(mesh):
    placed = (P(None, "gx", "gy"), P(None, "gx", "gy"), P("gx", "gy"), P("gx", "gy"), P("gx", "gy"))
    return jax.shard_map(
        on_device,
        mesh=mesh,
        in_specs=placed,
        out_specs=(P(None, "gx", "gy"), P(None, "gx", "gy"), P("gx", "gy"), P("gx", "gy")),
        check_vma=False,
    )
```

```python
import functools

import jax
import jax.numpy as jnp
from jax import lax
from jax.experimental import pallas as pl
from jax.experimental.pallas import tpu as pltpu
from jax.sharding import PartitionSpec as P

CHEB = 0.94
WEIGHT_TWO = 1.0 / (1.0 - CHEB * CHEB / 2.0)
WEIGHT_THREE = 1.0 / (1.0 - CHEB * CHEB * WEIGHT_TWO / 4.0)

HR = 8
HC = 128
BW = 2048
INTERPRET = False


def roll_shift(x, d, axis):
    return pltpu.roll(x, (-d) % x.shape[axis], axis)


def jnp_shift(x, d, axis):
    return jnp.roll(x, -d, axis)


def step_fields(u0, u1, v0, v1, dmg, hist, tough, valid, sh):
    zero = jnp.zeros_like(dmg)

    def strain(first, second):
        exx = (sh(first, 1, 0) - sh(first, -1, 0)) * 0.5
        eyy = (sh(second, 1, 1) - sh(second, -1, 1)) * 0.5
        exy = ((sh(first, 1, 1) - sh(first, -1, 1)) + (sh(second, 1, 0) - sh(second, -1, 0))) * 0.25
        return exx, eyy, exy

    degrade = (1.0 - dmg) ** 2 + 0.001
    degrade2 = degrade * 2.0

    def accel(exx, eyy, exy):
        trace = exx + eyy
        sxx = jnp.where(valid, degrade * (trace + 2.0 * exx), zero)
        syy = jnp.where(valid, degrade * (trace + 2.0 * eyy), zero)
        sxy = jnp.where(valid, degrade2 * exy, zero)
        a0 = ((sh(sxx, 1, 0) - sh(sxx, -1, 0)) + (sh(sxy, 1, 1) - sh(sxy, -1, 1))) * 0.5
        a1 = ((sh(sxy, 1, 0) - sh(sxy, -1, 0)) + (sh(syy, 1, 1) - sh(syy, -1, 1))) * 0.5
        return a0, a1

    a0, a1 = accel(*strain(u0 + 0.5 * v0, u1 + 0.5 * v1))
    h0 = jnp.where(valid, v0 + 0.1 * a0, zero)
    h1 = jnp.where(valid, v1 + 0.1 * a1, zero)
    n0 = jnp.where(valid, u0 + 0.2 * h0, zero)
    n1 = jnp.where(valid, u1 + 0.2 * h1, zero)
    e = strain(n0, n1)
    eh = strain(h0, h1)
    b0, b1 = accel(e[0] + 0.5 * eh[0], e[1] + 0.5 * eh[1], e[2] + 0.5 * eh[2])
    vel0 = h0 + 0.1 * b0
    vel1 = h1 + 0.1 * b1
    tr = jnp.maximum(e[0] + e[1], 0.0)
    hist_new = jnp.maximum(hist, 0.5 * tr * tr + e[0] * e[0] + e[1] * e[1] + 2.0 * e[2] * e[2])

    k_down = tough + sh(tough, 1, 0)
    k_up = tough + sh(tough, -1, 0)
    k_right = tough + sh(tough, 1, 1)
    k_left = tough + sh(tough, -1, 1)
    two_h = 2.0 * hist_new
    inv_denom = 1.0 / (tough * 0.5 + two_h + k_down + k_up + k_right + k_left)

    def jacobi(f):
        numer = two_h + k_down * sh(f, 1, 0) + k_up * sh(f, -1, 0)
        numer = numer + k_right * sh(f, 1, 1) + k_left * sh(f, -1, 1)
        return numer * inv_denom

    d1 = jnp.where(valid, jacobi(dmg), zero)
    d2 = jnp.where(valid, dmg + WEIGHT_TWO * (jacobi(d1) - dmg), zero)
    d3 = d1 + WEIGHT_THREE * (jacobi(d2) - d1)
    return n0, n1, vel0, vel1, hist_new, d3


RADII = (5, 5, 5, 5, 4, 2, 3)
OFFSETS = tuple(sum(RADII[:k]) for k in range(len(RADII)))
STRIP = 32
SENT = sum(RADII)
LANE_W = 5


def on_device(displacement, velocity, damage, history, toughness):
    rows, cols = damage.shape
    nx = lax.axis_size("gx")
    ny = lax.axis_size("gy")
    ix = lax.axis_index("gx")
    iy = lax.axis_index("gy")
    assert ny == 2 and rows % 8 == 0 and cols % BW == 0
    total_rows, total_cols = rows * nx, cols * ny
    nf = len(RADII)
    pos = jnp.stack([ix, iy]).astype(jnp.int32)
    nblocks = cols // BW
    per = BW // HC
    last_col_block = cols // HC - 1
    last_row_block = rows // 8 - 1
    f32 = damage.dtype
    rl = jnp_shift if INTERPRET else roll_shift

    def roll(x, s, axis):
        return rl(x, -s, axis)

    def split(refs):
        du, dv, dd, dh, dt = refs
        return [du[0], du[1], dv[0], dv[1], dd[...], dh[...], dt[...]]

    pw = cols // 4

    def strip_kernel(first_row_of, u_ref, v_ref, d_ref, h_ref, t_ref, out_o):
        tiles = split((u_ref, v_ref, d_ref, h_ref, t_ref))
        ridx = lax.broadcasted_iota(jnp.int32, (STRIP, pw), 0)
        acc = jnp.zeros((STRIP, pw), f32)
        pad = jnp.zeros((STRIP - 8, pw), f32)
        for k in range(nf):
            r, o = RADII[k], OFFSETS[k]
            inside = (ridx >= o) & (ridx < o + r)
            x = roll(jnp.concatenate([tiles[k], pad], axis=0), o - first_row_of(r), 0)
            acc = jnp.where(inside, x, acc)
        out_o[...] = acc[:SENT]


    def col_kernel(pos_ref, lu, lv, ld, lh, lt, ru, rv, rd, rh, rt, col_o):
        lefts = split((lu, lv, ld, lh, lt))
        rights = split((ru, rv, rd, rh, rt))
        lidx = lax.broadcasted_iota(jnp.int32, (rows, HC), 1)
        col = jnp.zeros((rows, HC), f32)
        to_right = pos_ref[1] == 0
        for k in range(nf):
            inside = (lidx >= LANE_W * k) & (lidx < LANE_W * (k + 1))
            a = roll(rights[k], LANE_W * k - (HC - LANE_W), 1)
            b = roll(lefts[k], LANE_W * k, 1)
            col = jnp.where(inside, jnp.where(to_right, a, b), col)
        col_o[...] = col

    t2 = pl.BlockSpec((2, 8, pw), lambda j: (0, 0, j))
    t1 = pl.BlockSpec((8, pw), lambda j: (0, j))
    b2 = pl.BlockSpec((2, 8, pw), lambda j: (0, last_row_block, j))
    b1 = pl.BlockSpec((8, pw), lambda j: (last_row_block, j))
    l2 = pl.BlockSpec((2, rows, HC), lambda j: (0, 0, 0))
    l1 = pl.BlockSpec((rows, HC), lambda j: (0, 0))
    r2 = pl.BlockSpec((2, rows, HC), lambda j: (0, 0, last_col_block))
    r1 = pl.BlockSpec((rows, HC), lambda j: (0, last_col_block))
    smem = pl.BlockSpec(memory_space=pltpu.SMEM)
    ins = (displacement, velocity, damage, history, toughness)
    def strip(first_row_of, s2, s1):
        return pl.pallas_call(
            functools.partial(strip_kernel, first_row_of),
            grid=(cols // pw,),
            in_specs=[s2, s2, s1, s1, s1],
            out_specs=pl.BlockSpec((SENT, pw), lambda j: (0, j)),
            out_shape=jax.ShapeDtypeStruct((SENT, cols), f32),
            interpret=INTERPRET,
        )(*ins)

    bot_s = strip(lambda r: 8 - r, b2, b1)
    top_s = strip(lambda r: 0, t2, t1)
    col_s = pl.pallas_call(
        col_kernel,
        grid=(1,),
        in_specs=[smem, l2, l2, l1, l1, l1, r2, r2, r1, r1, r1],
        out_specs=pl.BlockSpec((rows, HC), lambda j: (0, 0)),
        out_shape=jax.ShapeDtypeStruct((rows, HC), f32),
        interpret=INTERPRET,
    )(pos, *ins, *ins)

    above = lax.ppermute(bot_s, "gx", [(i, i + 1) for i in range(nx - 1)])
    below = lax.ppermute(top_s, "gx", [(i + 1, i) for i in range(nx - 1)])
    side = lax.ppermute(col_s, "gy", [(0, 1), (1, 0)])
    both = ("gx", "gy")
    corner_above = lax.ppermute(col_s[rows - 8:], both,
                                [(i * 2 + g, (i + 1) * 2 + 1 - g) for i in range(nx - 1) for g in range(2)])
    corner_below = lax.ppermute(col_s[:8], both,
                                [((i + 1) * 2 + g, i * 2 + 1 - g) for i in range(nx - 1) for g in range(2)])

    def kernel(pos_ref, um, ul, ur, vm, vl, vr, dm, dl, dr, hm, hl, hr, tm, tl, tr,
               am, al, ar, bm, bl, br, side_ref, ca_ref, cb_ref, uo, vo, ho, do):
        j = pl.program_id(0)
        first = j == 0
        last = j == nblocks - 1
        has_left = pos_ref[1] == 1
        has_right = pos_ref[1] == 0
        mains = split((um, vm, dm, hm, tm))
        lefts = split((ul, vl, dl, hl, tl))
        rights = split((ur, vr, dr, hr, tr))
        side_v = side_ref[...]
        ca = ca_ref[...]
        cb = cb_ref[...]

        def lane_left(x, k):
            lidx = lax.broadcasted_iota(jnp.int32, x.shape, 1)
            y = roll(x, HC - LANE_W - LANE_W * k, 1)
            return jnp.where((lidx >= HC - LANE_W) & has_left, y, 0.0)

        def lane_right(x, k):
            lidx = lax.broadcasted_iota(jnp.int32, x.shape, 1)
            y = roll(x, -LANE_W * k, 1)
            return jnp.where((lidx < LANE_W) & has_right, y, 0.0)

        def tile_of(ref, k, first_row):
            r, o = RADII[k], OFFSETS[k]
            s = min(max(o + first_row + r - 8 if first_row else o, 0), SENT - 8)
            y = ref[s:s + 8, :]
            shift = (first_row - (o - s)) % 8
            if shift:
                y = roll(y, shift, 0)
            ridx = lax.broadcasted_iota(jnp.int32, y.shape, 0)
            return jnp.where((ridx >= first_row) & (ridx < first_row + r), y, 0.0)

        def above_tile(ref, k):
            return tile_of(ref, k, 8 - RADII[k])

        def below_tile(ref, k):
            return tile_of(ref, k, 0)

        a_m, a_l, a_r = am, al, ar
        b_m, b_l, b_r = bm, bl, br

        def window(k):
            lft = jnp.where(first, lane_left(side_v, k), lefts[k])
            rgt = jnp.where(last, lane_right(side_v, k), rights[k])
            core = jnp.concatenate([lft, mains[k], rgt], axis=-1)
            top = jnp.concatenate([jnp.where(first, lane_left(ca, k), above_tile(a_l, k)),
                                   above_tile(a_m, k),
                                   jnp.where(last, lane_right(ca, k), above_tile(a_r, k))], axis=-1)
            bot = jnp.concatenate([jnp.where(first, lane_left(cb, k), below_tile(b_l, k)),
                                   below_tile(b_m, k),
                                   jnp.where(last, lane_right(cb, k), below_tile(b_r, k))], axis=-1)
            return jnp.concatenate([top, core, bot], axis=0)

        u0, u1, v0, v1, d, h, t = [window(k) for k in range(nf)]
        shape = d.shape
        grow = lax.broadcasted_iota(jnp.int32, (shape[0], 1), 0) + (pos_ref[0] * rows - HR)
        gcol = lax.broadcasted_iota(jnp.int32, (1, shape[1]), 1) + (pos_ref[1] * cols + j * BW - HC)
        valid = ((grow >= 0) & (grow < total_rows)) & ((gcol >= 0) & (gcol < total_cols))
        n0, n1, w0, w1, hn, d3 = step_fields(u0, u1, v0, v1, d, h, t, valid, rl)

        def core(x):
            return x[HR:HR + rows, HC:HC + BW]

        uo[0] = core(n0)
        uo[1] = core(n1)
        vo[0] = core(w0)
        vo[1] = core(w1)
        ho[...] = core(hn)
        do[...] = core(d3)

    def lcol(j):
        return jnp.maximum(j * per - 1, 0)

    def rcol(j):
        return jnp.minimum((j + 1) * per, last_col_block)

    main2 = pl.BlockSpec((2, rows, BW), lambda j: (0, 0, j))
    left2 = pl.BlockSpec((2, rows, HC), lambda j: (0, 0, lcol(j)))
    right2 = pl.BlockSpec((2, rows, HC), lambda j: (0, 0, rcol(j)))
    main1 = pl.BlockSpec((rows, BW), lambda j: (0, j))
    left1 = pl.BlockSpec((rows, HC), lambda j: (0, lcol(j)))
    right1 = pl.BlockSpec((rows, HC), lambda j: (0, rcol(j)))
    sm = pl.BlockSpec((SENT, BW), lambda j: (0, j))
    sl = pl.BlockSpec((SENT, HC), lambda j: (0, lcol(j)))
    sr = pl.BlockSpec((SENT, HC), lambda j: (0, rcol(j)))
    sidespec = pl.BlockSpec((rows, HC), lambda j: (0, 0))
    cornerspec = pl.BlockSpec((8, HC), lambda j: (0, 0))
    out2 = pl.BlockSpec((2, rows, BW), lambda j: (0, 0, j))
    out1 = pl.BlockSpec((rows, BW), lambda j: (0, j))
    outs = pl.pallas_call(
        kernel,
        grid=(nblocks,),
        in_specs=[smem, main2, left2, right2, main2, left2, right2,
                  main1, left1, right1, main1, left1, right1, main1, left1, right1,
                  sm, sl, sr, sm, sl, sr, sidespec, cornerspec, cornerspec],
        out_specs=[out2, out2, out1, out1],
        out_shape=[jax.ShapeDtypeStruct((2, rows, cols), f32), jax.ShapeDtypeStruct((2, rows, cols), f32),
                   jax.ShapeDtypeStruct((rows, cols), f32), jax.ShapeDtypeStruct((rows, cols), f32)],
        interpret=INTERPRET,
    )(pos, displacement, displacement, displacement, velocity, velocity, velocity,
      damage, damage, damage, history, history, history, toughness, toughness, toughness,
      above, above, above, below, below, below, side, corner_above, corner_below)
    return tuple(outs)


def solution(mesh):
    placed = (P(None, "gx", "gy"), P(None, "gx", "gy"), P("gx", "gy"), P("gx", "gy"), P("gx", "gy"))
    return jax.shard_map(
        on_device,
        mesh=mesh,
        in_specs=placed,
        out_specs=(P(None, "gx", "gy"), P(None, "gx", "gy"), P("gx", "gy"), P("gx", "gy")),
        check_vma=False,
    )
```
